32 devices in a mesh: ctx: 8 (over z, y), tp: 4 (over x, core).
Axes of the slice: x: 2, y: 2, z: 4, core: 2. Of those that a mesh axis runs over, the one named last changes fastest.
Arguments:
- features: bfloat16 [2048, 8192], P('ctx', 'tp'), may hold values from -6 to 6
- input_map: bfloat16 [2048, 512], P('ctx', 'tp'), may hold values from -1.5 to 1.5
- output_map: bfloat16 [2048, 512], P('ctx', 'tp'), may hold values from -1.5 to 1.5
- gate_in: bfloat16 [2048, 8192], P('ctx', 'tp'), may hold values from -6 to 6
- conv_feat: float32 [4, 8192], P(None, 'tp'), may hold values from -3 to 3
- conv_input: float32 [4, 512], P(None, 'tp'), may hold values from -3 to 3
- conv_output: float32 [4, 512], P(None, 'tp'), may hold values from -3 to 3
- step_size: float32 [2048, 128], P('ctx', 'tp'), may hold values from 0.1 to 1
- log_decay: float32 [2048, 128], P('ctx', 'tp'), may hold values from -1 to 0, as said below
- skip_gain: float32 [128], P('tp'), may hold values from 0.5 to 2
- norm_gain: float32 [8192], P('tp'), may hold values from 0.5 to 1.5
- out_weight: bfloat16 [8192, 4096], P('tp', 'ctx'), may hold values from -0.0625 to 0.0625
Outputs:
- layer_out: bfloat16 [2048, 4096], P('ctx', 'tp')
The draws below stay inside these ranges and needn't reach their ends.
Inputs may be any that keep to these rules, and one draw needn't show every extreme that they name: log_decay is negative.
All inputs are finite; a program needn't handle non-finite values.
Results may differ from the reference program's by a relative error of at most 0.0066.
Values may be sent and summed in bfloat16 or wider, within the bound.
No kernel may reach another device: no remote copies, remote signals or barrier semaphores. Data moves between devices by JAX's collectives and lax.ppermute only.
A program may use at most 192 MiB of HBM per device.

```python
import math
import jax
import jax.numpy as jnp
from jax import lax

D = 4096
STATE_HEADS = 128
P_SIZE = 64
N = 128
GROUPS = 4
CONV = 4
BLOCK = 256
TOK_DEV = 256
HP = 8192
SEQUENCE_TOKENS = 2048


def draw_log_decay(key, part):
    random_subkey_list = jax.random.split(key, 6)
    fast_share = 0.5
    fast_heads = jax.random.uniform(random_subkey_list[0], (STATE_HEADS,)) < fast_share
    head_decay_rate = jnp.where(fast_heads, 1.0 / 40.0, 0.5 / SEQUENCE_TOKENS)
    head_decay_rate = head_decay_rate * jax.random.uniform(random_subkey_list[1], (STATE_HEADS,), minval=0.7, maxval=1.4)
    jaggedness_level = jax.random.uniform(random_subkey_list[2], (SEQUENCE_TOKENS, STATE_HEADS), minval=0.5, maxval=1.5)
    segment_scale = jnp.exp(jax.random.uniform(random_subkey_list[3], (SEQUENCE_TOKENS // TOK_DEV, STATE_HEADS), minval=math.log(0.6), maxval=math.log(1.7)))
    segment_scale = jnp.repeat(segment_scale, TOK_DEV, axis=0)
    spike_position = jax.random.randint(random_subkey_list[4], (3,), 0, SEQUENCE_TOKENS)
    spike_row_index = jnp.any(jnp.arange(SEQUENCE_TOKENS)[:, None] == spike_position[None, :], axis=1)
    spike_penalty = jax.random.uniform(random_subkey_list[5], (SEQUENCE_TOKENS, STATE_HEADS), minval=math.log(0.6), maxval=math.log(0.8))
    value_entries = -head_decay_rate[None, :] * jaggedness_level * segment_scale + jnp.where(spike_row_index[:, None], spike_penalty, 0.0)
    return value_entries.astype(jnp.float32)


def block_scale(key, dims, shards, smallest, top_value):
    def one(axis_at, shards_of):
        draws = jax.random.uniform(jax.random.fold_in(jax.random.fold_in(key, 6), axis_at), (shards_of,), jnp.float32, smallest / len(shards), top_value / len(shards))
        return jnp.repeat(jnp.exp(draws), dims[axis_at] // shards_of).reshape((-1,) + (1,) * (len(dims) - axis_at - 1))

    factor_of = one(*shards[0])
    for cut in shards[1:]:
        factor_of = factor_of * one(*cut)
    return factor_of


def noise(own_key, extent, spread, reach, pieces=(), dtype=jnp.bfloat16):
    level = block_scale(own_key, extent, pieces, -0.22, 0.18) if pieces else 1.0
    entries = jax.random.normal(own_key, extent, jnp.float32) * spread * level
    return jnp.minimum(jnp.maximum(entries, -reach), reach).astype(dtype)


def setup_inputs(seed: int = 0) -> dict:
    arg_keys = jax.random.split(jax.random.key(seed), 13)
    return {
        "features": noise(arg_keys[0], (SEQUENCE_TOKENS, HP), 1.0, 6.0, ((0, 8), (1, 4))),
        "input_map": noise(arg_keys[1], (SEQUENCE_TOKENS, GROUPS * N), 0.25, 1.5, ((0, 8), (1, 4))),
        "output_map": noise(arg_keys[2], (SEQUENCE_TOKENS, GROUPS * N), 0.25, 1.5, ((0, 8), (1, 4))),
        "gate_in": noise(arg_keys[3], (SEQUENCE_TOKENS, HP), 1.0, 6.0, ((0, 8), (1, 4))),
        "conv_feat": noise(arg_keys[4], (CONV, HP), CONV ** -0.5, 3.0, ((1, 4),), jnp.float32),
        "conv_input": noise(arg_keys[5], (CONV, GROUPS * N), CONV ** -0.5, 3.0, ((1, 4),), jnp.float32),
        "conv_output": noise(arg_keys[6], (CONV, GROUPS * N), CONV ** -0.5, 3.0, ((1, 4),), jnp.float32),
        "step_size": jnp.clip(jnp.exp(math.log(1.0) - 2.3025851 * jax.random.uniform(arg_keys[7], (SEQUENCE_TOKENS, STATE_HEADS), jnp.float32) ** block_scale(arg_keys[7], (SEQUENCE_TOKENS, STATE_HEADS), ((0, 8), (1, 4)), -0.2, 0.2)), 0.1, 1.0),
        "log_decay": draw_log_decay(jax.random.fold_in(arg_keys[12], 71), 0),
        "skip_gain": jnp.clip(jnp.exp(math.log(2.0) - 1.3862944 * jax.random.uniform(arg_keys[9], (STATE_HEADS,), jnp.float32) ** block_scale(arg_keys[9], (STATE_HEADS,), ((0, 4),), -0.2, 0.2)), 0.5, 2.0),
        "norm_gain": jnp.clip(1.0 + 0.1 * jax.random.normal(arg_keys[10], (HP,), jnp.float32), 0.5, 1.5),
        "out_weight": noise(arg_keys[11], (HP, D), HP ** -0.5, 0.0625, ((0, 4), (1, 8))),
    }


def to_bf16(value_entries):
    return lax.optimization_barrier(value_entries.astype(jnp.bfloat16))

def conv_block(tail_rows, block_rows, kernel):
    tap_count = kernel.shape[0]
    block_len = block_rows.shape[0]
    extended = jnp.concatenate([tail_rows, block_rows], axis=0).astype(jnp.float32)
    pre_act = jnp.zeros((block_len, kernel.shape[1]), jnp.float32)
    for tap_index in range(tap_count):
        pre_act = pre_act + kernel[tap_index] * extended[tap_index:tap_index + block_len]
    return jax.nn.silu(pre_act).astype(jnp.bfloat16)

def intra_block(scaled, b_rows, c_rows, cum_log):
    scores = jnp.einsum('tgn,sgn->gts', c_rows.astype(jnp.float32), b_rows.astype(jnp.float32))
    cum_cols = jnp.moveaxis(cum_log, 0, -1)
    log_gap = cum_cols[..., :, None] - cum_cols[..., None, :]
    block_len = cum_log.shape[0]
    causal = jnp.arange(block_len)[:, None] >= jnp.arange(block_len)[None, :]
    decays = jnp.exp(jnp.where(causal, log_gap, -jnp.inf))
    weights = to_bf16(scores[:, None] * decays)
    return jnp.einsum('gjts,sgjp->tgjp', weights.astype(jnp.float32), scaled.astype(jnp.float32))

def block_state(scaled, b_rows, cum_log):
    end_decay = jnp.exp(cum_log[-1][None] - cum_log)
    b_weighted = to_bf16(b_rows.astype(jnp.float32)[:, :, None, :] * end_decay[..., None])
    return jnp.einsum('sgjp,sgjn->gjpn', scaled.astype(jnp.float32), b_weighted.astype(jnp.float32))

def inter_block(c_rows, cum_log, state_carry):
    rounded = to_bf16(state_carry)
    inner = jnp.einsum('tgn,gjpn->tgjp', c_rows.astype(jnp.float32), rounded.astype(jnp.float32))
    return inner * jnp.exp(cum_log)[..., None]

def reference(features, input_map, output_map, gate_in, conv_feat, conv_input, conv_output, step_size, log_decay, skip_gain, norm_gain, out_weight):
    per_group = STATE_HEADS // GROUPS
    n_blocks = SEQUENCE_TOKENS // BLOCK
    tail_len = CONV - 1

    def blocked(value_entries):
        return value_entries.reshape((n_blocks, BLOCK) + value_entries.shape[1:])

    def advance(state_carry, block_in):
        state_now, tail_feat, tail_in, tail_out = state_carry
        feat_b, in_b, out_b, gate_b, step_b, decay_b = block_in
        x_conv = conv_block(tail_feat, feat_b, conv_feat)
        b_conv = conv_block(tail_in, in_b, conv_input)
        c_conv = conv_block(tail_out, out_b, conv_output)
        x_heads = x_conv.astype(jnp.float32).reshape(BLOCK, GROUPS, per_group, P_SIZE)
        scaled = to_bf16(x_heads * step_b.reshape(BLOCK, GROUPS, per_group)[..., None])
        b_rows = b_conv.reshape(BLOCK, GROUPS, N)
        c_rows = c_conv.reshape(BLOCK, GROUPS, N)
        cum_log = jnp.cumsum(decay_b.reshape(BLOCK, GROUPS, per_group), axis=0)
        mixed_y = intra_block(scaled, b_rows, c_rows, cum_log) + inter_block(c_rows, cum_log, state_now)
        mixed_y = mixed_y + skip_gain.reshape(GROUPS, per_group)[..., None] * x_heads
        gated_y = mixed_y.reshape(BLOCK, HP) * jax.nn.silu(gate_b.astype(jnp.float32))
        grouped = gated_y.reshape(BLOCK, GROUPS, HP // GROUPS)
        inv_root = lax.rsqrt(lax.optimization_barrier(jnp.mean(grouped * grouped, axis=-1, keepdims=True)) + 1e-05)
        hidden = ((grouped * inv_root).reshape(BLOCK, HP) * norm_gain).astype(jnp.bfloat16)
        next_state = jnp.exp(cum_log[-1])[..., None, None] * state_now + block_state(scaled, b_rows, cum_log)
        carry_out = (next_state, feat_b[BLOCK - tail_len:], in_b[BLOCK - tail_len:], out_b[BLOCK - tail_len:])
        return (carry_out, hidden)
    start_state = (jnp.zeros((GROUPS, per_group, P_SIZE, N), jnp.float32), jnp.zeros((tail_len, HP), jnp.bfloat16), jnp.zeros((tail_len, GROUPS * N), jnp.bfloat16), jnp.zeros((tail_len, GROUPS * N), jnp.bfloat16))
    block_inputs = (blocked(features), blocked(input_map), blocked(output_map), blocked(gate_in), blocked(step_size), blocked(log_decay))
    _, hidden = lax.scan(advance, start_state, block_inputs)
    hidden = hidden.reshape(SEQUENCE_TOKENS, HP)
    return jnp.dot(hidden, out_weight, preferred_element_type=jnp.float32).astype(jnp.bfloat16)
```

```python
import jax
import jax.numpy as jnp
from jax import lax
from jax.sharding import PartitionSpec as P

N = 128
BLOCK = 256


def shifted(value, axis, steps):
    count = lax.axis_size(axis)
    first, last = (max(0, -steps), min(count, count - steps))
    return lax.ppermute(value, axis, [(source, source + steps) for source in range(first, last)])


def local_conv(packed, kernel, tok_rows):
    tail_len = kernel.shape[0] - 1
    padded = jnp.pad(packed.astype(jnp.float32), ((tail_len, 0), (0, 0)))
    pre_act = jnp.zeros((tok_rows, kernel.shape[1]), jnp.float32)
    for tap_index in range(kernel.shape[0]):
        pre_act = pre_act + kernel[tap_index] * padded[tap_index : tap_index + tok_rows]
    return pre_act


def edge_partial(tail_rows, kernel):
    tail_len = kernel.shape[0] - 1
    tail_vals = tail_rows.astype(jnp.float32)
    outputs = []
    for row_index in range(tail_len):
        accum = jnp.zeros((kernel.shape[1],), jnp.float32)
        for tap_index in range(tail_len - row_index):
            accum = accum + kernel[tap_index] * tail_vals[row_index + tap_index]
        outputs.append(accum)
    return jnp.stack(outputs, axis=0)


def intra_block(scaled, b_rows, c_rows, cum_log):
    scores = jnp.einsum("tgn,sgn->gts", c_rows, b_rows, preferred_element_type=jnp.float32)
    cum_cols = jnp.moveaxis(cum_log, 0, -1)
    log_gap = cum_cols[..., :, None] - cum_cols[..., None, :]
    block_len = cum_log.shape[0]
    causal = jnp.arange(block_len)[:, None] >= jnp.arange(block_len)[None, :]
    decays = jnp.exp(jnp.where(causal, log_gap, -jnp.inf))
    weights = (scores[:, None] * decays).astype(jnp.bfloat16)
    return jnp.einsum("gjts,sgjp->tgjp", weights, scaled, preferred_element_type=jnp.float32)


def block_state(scaled, b_rows, cum_log):
    end_decay = jnp.exp(cum_log[-1][None] - cum_log)
    b_weighted = (b_rows.astype(jnp.float32)[:, :, None, :] * end_decay[..., None]).astype(
        jnp.bfloat16
    )
    return jnp.einsum("sgjp,sgjn->gjpn", scaled, b_weighted, preferred_element_type=jnp.float32)


def inter_block(c_rows, cum_log, state_carry):
    rounded = state_carry.astype(jnp.bfloat16)
    inner = jnp.einsum("tgn,gjpn->tgjp", c_rows, rounded, preferred_element_type=jnp.float32)
    return inner * jnp.exp(cum_log)[..., None]


def combine(first_part, second_part):
    decay_first, state_first = first_part
    decay_second, state_second = second_part
    return (decay_first * decay_second, decay_second[..., None, None] * state_first + state_second)


def prefix_states(dev_decay, dev_state):
    count = lax.axis_size("ctx")
    own = (dev_decay, dev_state)
    if count == 1:
        return jnp.zeros_like(dev_state)
    got = shifted(own, "ctx", 1)
    before = got
    upto = combine(got, own)
    step = 2
    while step < count:
        got = shifted(upto, "ctx", step)
        before = combine(got, before)
        if step * 2 < count:
            upto = combine(got, upto)
        step *= 2
    return before[1]


def on_device(
    features,
    input_map,
    output_map,
    gate_in,
    conv_feat,
    conv_input,
    conv_output,
    step_size,
    log_decay,
    skip_gain,
    norm_gain,
    out_weight,
):
    tok_rows, width_x = features.shape
    width_b = input_map.shape[1]
    head_count = step_size.shape[1]
    head_dim = width_x // head_count
    groups_here = width_b // N
    per_group = head_count // groups_here
    tail_len = conv_feat.shape[0] - 1
    n_blocks = tok_rows // BLOCK
    packed = jnp.concatenate([features, input_map, output_map], axis=1)
    kernel = jnp.concatenate([conv_feat, conv_input, conv_output], axis=1)
    pre_act = local_conv(packed, kernel, tok_rows)
    tail_rows = shifted(packed[tok_rows - tail_len :], "ctx", 1)
    edge_sums = edge_partial(tail_rows, kernel)
    pre_act = pre_act + jnp.pad(edge_sums, ((0, tok_rows - tail_len), (0, 0)))
    conv_out = jax.nn.silu(pre_act).astype(jnp.bfloat16)
    x_conv = conv_out[:, :width_x]
    b_conv = conv_out[:, width_x : width_x + width_b]
    c_conv = conv_out[:, width_x + width_b :]
    x_heads = x_conv.astype(jnp.float32).reshape(tok_rows, groups_here, per_group, head_dim)
    scaled = (x_heads * step_size.reshape(tok_rows, groups_here, per_group)[..., None]).astype(
        jnp.bfloat16
    )

    def blocked(value_entries):
        return value_entries.reshape((n_blocks, BLOCK) + value_entries.shape[1:])

    scaled_b = blocked(scaled)
    b_rows = blocked(b_conv.reshape(tok_rows, groups_here, N))
    c_rows = blocked(c_conv.reshape(tok_rows, groups_here, N))
    cum_log = jnp.cumsum(blocked(log_decay.reshape(tok_rows, groups_here, per_group)), axis=1)
    blk_states = jax.vmap(block_state)(scaled_b, b_rows, cum_log)
    blk_decay = jnp.exp(cum_log[:, -1])

    def fold_local(state_carry, block_in):
        decay_b, state_b = block_in
        return (decay_b[..., None, None] * state_carry + state_b, None)

    dev_state, _ = lax.scan(
        fold_local, jnp.zeros(blk_states.shape[1:], jnp.float32), (blk_decay, blk_states)
    )
    dev_decay = jnp.prod(blk_decay, axis=0)
    incoming = prefix_states(dev_decay, dev_state)

    def advance(state_carry, block_in):
        scaled_k, b_k, c_k, cum_k, decay_k, state_k = block_in
        block_y = intra_block(scaled_k, b_k, c_k, cum_k) + inter_block(c_k, cum_k, state_carry)
        return (decay_k[..., None, None] * state_carry + state_k, block_y)

    _, ssm_y = lax.scan(
        advance, incoming, (scaled_b, b_rows, c_rows, cum_log, blk_decay, blk_states)
    )
    mixed_y = ssm_y.reshape(tok_rows, groups_here, per_group, head_dim)
    mixed_y = mixed_y + skip_gain.reshape(groups_here, per_group)[..., None] * x_heads
    gated_y = mixed_y.reshape(tok_rows, width_x) * jax.nn.silu(gate_in.astype(jnp.float32))
    grouped = gated_y.reshape(tok_rows, groups_here, width_x // groups_here)
    inv_root = lax.rsqrt(jnp.mean(grouped * grouped, axis=-1, keepdims=True) + 1e-05)
    hidden = ((grouped * inv_root).reshape(tok_rows, width_x) * norm_gain).astype(jnp.bfloat16)
    partial_out = jnp.dot(
        hidden,
        lax.all_gather(out_weight, "ctx", axis=1, tiled=True),
        preferred_element_type=jnp.float32,
    )
    return lax.psum_scatter(partial_out, "tp", scatter_dimension=1, tiled=True).astype(jnp.bfloat16)


def solution(mesh):
    placed = (
        P("ctx", "tp"),
        P("ctx", "tp"),
        P("ctx", "tp"),
        P("ctx", "tp"),
        P(None, "tp"),
        P(None, "tp"),
        P(None, "tp"),
        P("ctx", "tp"),
        P("ctx", "tp"),
        P("tp"),
        P("tp"),
        P("tp", "ctx"),
    )
    return jax.shard_map(
        on_device, mesh=mesh, in_specs=placed, out_specs=P("ctx", "tp"), check_vma=False
    )
```

```python
import functools

import jax
import jax.numpy as jnp
from jax import lax
from jax.sharding import PartitionSpec as P

N = 128
BLOCK = 256


def shifted(value, axis, steps, count):
    first, last = (max(0, -steps), min(count, count - steps))
    return lax.ppermute(value, axis, [(source, source + steps) for source in range(first, last)])


def local_conv(packed, kernel, tok_rows):
    tail_len = kernel.shape[0] - 1
    padded = jnp.pad(packed.astype(jnp.float32), ((tail_len, 0), (0, 0)))
    pre_act = jnp.zeros((tok_rows, kernel.shape[1]), jnp.float32)
    for tap_index in range(kernel.shape[0]):
        pre_act = pre_act + kernel[tap_index] * padded[tap_index : tap_index + tok_rows]
    return pre_act


def edge_partial(tail_rows, kernel):
    tail_len = kernel.shape[0] - 1
    tail_vals = tail_rows.astype(jnp.float32)
    outputs = []
    for row_index in range(tail_len):
        accum = jnp.zeros((kernel.shape[1],), jnp.float32)
        for tap_index in range(tail_len - row_index):
            accum = accum + kernel[tap_index] * tail_vals[row_index + tap_index]
        outputs.append(accum)
    return jnp.stack(outputs, axis=0)


def intra_block(scaled, b_rows, c_rows, cum_log):
    scores = jnp.einsum("tgn,sgn->gts", c_rows, b_rows, preferred_element_type=jnp.float32)
    cum_cols = jnp.moveaxis(cum_log, 0, -1)
    log_gap = cum_cols[..., :, None] - cum_cols[..., None, :]
    block_len = cum_log.shape[0]
    causal = jnp.arange(block_len)[:, None] >= jnp.arange(block_len)[None, :]
    decays = jnp.exp(jnp.where(causal, log_gap, -jnp.inf))
    weights = (scores[:, None] * decays).astype(jnp.bfloat16)
    return jnp.einsum("gjts,sgjp->tgjp", weights, scaled, preferred_element_type=jnp.float32)


def block_state(scaled, b_rows, cum_log):
    end_decay = jnp.exp(cum_log[-1][None] - cum_log)
    b_weighted = (b_rows.astype(jnp.float32)[:, :, None, :] * end_decay[..., None]).astype(
        jnp.bfloat16
    )
    return jnp.einsum("sgjp,sgjn->gjpn", scaled, b_weighted, preferred_element_type=jnp.float32)


def inter_block(c_rows, cum_log, state_carry):
    rounded = state_carry.astype(jnp.bfloat16)
    inner = jnp.einsum("tgn,gjpn->tgjp", c_rows, rounded, preferred_element_type=jnp.float32)
    return inner * jnp.exp(cum_log)[..., None]


def combine(first_part, second_part):
    decay_first, state_first = first_part
    decay_second, state_second = second_part
    return (decay_first * decay_second, decay_second[..., None, None] * state_first + state_second)


def prefix_states(dev_decay, dev_state, axis, count):
    own = (dev_decay, dev_state)
    if count == 1:
        return jnp.zeros_like(dev_state)
    got = shifted(own, axis, 1, count)
    before = got
    upto = combine(got, own)
    step = 2
    while step < count:
        got = shifted(upto, axis, step, count)
        before = combine(got, before)
        if step * 2 < count:
            upto = combine(got, upto)
        step *= 2
    return before[1]


def on_device(
    layout,
    features,
    input_map,
    output_map,
    gate_in,
    conv_feat,
    conv_input,
    conv_output,
    step_size,
    log_decay,
    skip_gain,
    norm_gain,
    out_weight,
):
    tok_rows, width_x = features.shape
    width_b = input_map.shape[1]
    head_count = step_size.shape[1]
    head_dim = width_x // head_count
    groups_here = width_b // N
    per_group = head_count // groups_here
    tail_len = conv_feat.shape[0] - 1
    n_blocks = tok_rows // BLOCK
    packed = jnp.concatenate([features, input_map, output_map], axis=1)
    kernel = jnp.concatenate([conv_feat, conv_input, conv_output], axis=1)
    pre_act = local_conv(packed, kernel, tok_rows)
    ctx_axes, ctx_count, outer_axis, inner_axis, tp_count = layout
    tail_rows = shifted(packed[tok_rows - tail_len :], ctx_axes, 1, ctx_count)
    edge_sums = edge_partial(tail_rows, kernel)
    pre_act = pre_act + jnp.pad(edge_sums, ((0, tok_rows - tail_len), (0, 0)))
    conv_out = jax.nn.silu(pre_act).astype(jnp.bfloat16)
    x_conv = conv_out[:, :width_x]
    b_conv = conv_out[:, width_x : width_x + width_b]
    c_conv = conv_out[:, width_x + width_b :]
    x_heads = x_conv.astype(jnp.float32).reshape(tok_rows, groups_here, per_group, head_dim)
    scaled = (x_heads * step_size.reshape(tok_rows, groups_here, per_group)[..., None]).astype(
        jnp.bfloat16
    )

    def blocked(value_entries):
        return value_entries.reshape((n_blocks, BLOCK) + value_entries.shape[1:])

    scaled_b = blocked(scaled)
    b_rows = blocked(b_conv.reshape(tok_rows, groups_here, N))
    c_rows = blocked(c_conv.reshape(tok_rows, groups_here, N))
    cum_log = jnp.cumsum(blocked(log_decay.reshape(tok_rows, groups_here, per_group)), axis=1)
    blk_states = jax.vmap(block_state)(scaled_b, b_rows, cum_log)
    blk_decay = jnp.exp(cum_log[:, -1])

    def fold_local(state_carry, block_in):
        decay_b, state_b = block_in
        return (decay_b[..., None, None] * state_carry + state_b, None)

    dev_state, _ = lax.scan(
        fold_local, jnp.zeros(blk_states.shape[1:], jnp.float32), (blk_decay, blk_states)
    )
    dev_decay = jnp.prod(blk_decay, axis=0)
    incoming = prefix_states(dev_decay, dev_state, ctx_axes, ctx_count)

    def advance(state_carry, block_in):
        scaled_k, b_k, c_k, cum_k, decay_k, state_k = block_in
        block_y = intra_block(scaled_k, b_k, c_k, cum_k) + inter_block(c_k, cum_k, state_carry)
        return (decay_k[..., None, None] * state_carry + state_k, block_y)

    _, ssm_y = lax.scan(
        advance, incoming, (scaled_b, b_rows, c_rows, cum_log, blk_decay, blk_states)
    )
    mixed_y = ssm_y.reshape(tok_rows, groups_here, per_group, head_dim)
    mixed_y = mixed_y + skip_gain.reshape(groups_here, per_group)[..., None] * x_heads
    gated_y = mixed_y.reshape(tok_rows, width_x) * jax.nn.silu(gate_in.astype(jnp.float32))
    grouped = gated_y.reshape(tok_rows, groups_here, width_x // groups_here)
    inv_root = lax.rsqrt(jnp.mean(grouped * grouped, axis=-1, keepdims=True) + 1e-05)
    hidden = ((grouped * inv_root).reshape(tok_rows, width_x) * norm_gain).astype(jnp.bfloat16)
    if outer_axis is None:
        partial_out = jnp.dot(
            hidden,
            lax.all_gather(out_weight, ctx_axes, axis=1, tiled=True),
            preferred_element_type=jnp.float32,
        )
        return lax.psum_scatter(partial_out, "tp", scatter_dimension=1, tiled=True).astype(
            jnp.bfloat16
        )
    rows_all = lax.all_gather(hidden, outer_axis, axis=0, tiled=True)
    cols_all = lax.all_gather(out_weight, inner_axis, axis=1, tiled=True)
    partial_out = jnp.dot(rows_all, cols_all, preferred_element_type=jnp.float32)
    reduced = lax.psum_scatter(partial_out, "tp", scatter_dimension=0, tiled=True)
    swap = [(o * tp_count + t, t * tp_count + o) for o in range(tp_count) for t in range(tp_count)]
    return lax.ppermute(reduced.astype(jnp.bfloat16), (outer_axis, "tp"), swap)


def solution(mesh):
    ctx_count = mesh.shape["ctx"]
    tp_count = mesh.shape["tp"]
    if ctx_count % tp_count == 0:
        inner = ctx_count // tp_count
        grid = mesh.devices.reshape(tp_count, inner, tp_count)
        mesh = jax.sharding.Mesh(grid, ("outer", "inner", "tp"))
        ctx_axes = ("outer", "inner")
        layout = (ctx_axes, ctx_count, "outer", "inner", tp_count)
    else:
        ctx_axes = "ctx"
        layout = (ctx_axes, ctx_count, None, None, tp_count)
    placed = (
        P(ctx_axes, "tp"),
        P(ctx_axes, "tp"),
        P(ctx_axes, "tp"),
        P(ctx_axes, "tp"),
        P(None, "tp"),
        P(None, "tp"),
        P(None, "tp"),
        P(ctx_axes, "tp"),
        P(ctx_axes, "tp"),
        P("tp"),
        P("tp"),
        P("tp", ctx_axes),
    )
    return jax.shard_map(
        functools.partial(on_device, layout),
        mesh=mesh,
        in_specs=placed,
        out_specs=P(ctx_axes, "tp"),
        check_vma=False,
    )
```

```python
import functools

import jax
import jax.numpy as jnp
from jax import lax
from jax.sharding import PartitionSpec as P

N = 128
BLOCK = 256


def shifted(value, axis, steps, count):
    first, last = (max(0, -steps), min(count, count - steps))
    return lax.ppermute(value, axis, [(source, source + steps) for source in range(first, last)])


def local_conv(packed, kernel, tok_rows):
    tail_len = kernel.shape[0] - 1
    padded = jnp.pad(packed.astype(jnp.float32), ((tail_len, 0), (0, 0)))
    pre_act = jnp.zeros((tok_rows, kernel.shape[1]), jnp.float32)
    for tap_index in range(kernel.shape[0]):
        pre_act = pre_act + kernel[tap_index] * padded[tap_index : tap_index + tok_rows]
    return pre_act


def edge_partial(tail_rows, kernel):
    tail_len = kernel.shape[0] - 1
    tail_vals = tail_rows.astype(jnp.float32)
    outputs = []
    for row_index in range(tail_len):
        accum = jnp.zeros((kernel.shape[1],), jnp.float32)
        for tap_index in range(tail_len - row_index):
            accum = accum + kernel[tap_index] * tail_vals[row_index + tap_index]
        outputs.append(accum)
    return jnp.stack(outputs, axis=0)


def intra_block(scaled, b_rows, c_rows, cum_log):
    scores = jnp.einsum("tgn,sgn->gts", c_rows, b_rows, preferred_element_type=jnp.float32)
    cum_cols = jnp.moveaxis(cum_log, 0, -1)
    log_gap = cum_cols[..., :, None] - cum_cols[..., None, :]
    block_len = cum_log.shape[0]
    causal = jnp.arange(block_len)[:, None] >= jnp.arange(block_len)[None, :]
    decays = jnp.exp(jnp.where(causal, log_gap, -jnp.inf))
    weights = (scores[:, None] * decays).astype(jnp.bfloat16)
    return jnp.einsum("gjts,sgjp->tgjp", weights, scaled, preferred_element_type=jnp.float32)


def block_state(scaled, b_rows, cum_log):
    end_decay = jnp.exp(cum_log[-1][None] - cum_log)
    b_weighted = (b_rows.astype(jnp.float32)[:, :, None, :] * end_decay[..., None]).astype(
        jnp.bfloat16
    )
    return jnp.einsum("sgjp,sgjn->gjpn", scaled, b_weighted, preferred_element_type=jnp.float32)


def inter_block(c_rows, cum_log, state_carry):
    rounded = state_carry.astype(jnp.bfloat16)
    inner = jnp.einsum("tgn,gjpn->tgjp", c_rows, rounded, preferred_element_type=jnp.float32)
    return inner * jnp.exp(cum_log)[..., None]


def combine(first_part, second_part):
    decay_first, state_first = first_part
    decay_second, state_second = second_part
    return (decay_first * decay_second, decay_second[..., None, None] * state_first + state_second)


def prefix_states(dev_decay, dev_state, axis, count):
    own = (dev_decay, dev_state)
    if count == 1:
        return jnp.zeros_like(dev_state)
    got = shifted(own, axis, 1, count)
    before = got
    upto = combine(got, own)
    step = 2
    while step < count:
        got = shifted(upto, axis, step, count)
        before = combine(got, before)
        if step * 2 < count:
            upto = combine(got, upto)
        step *= 2
    return before[1]


def on_device(
    layout,
    features,
    input_map,
    output_map,
    gate_in,
    conv_feat,
    conv_input,
    conv_output,
    step_size,
    log_decay,
    skip_gain,
    norm_gain,
    out_weight,
):
    tok_rows, width_x = features.shape
    width_b = input_map.shape[1]
    head_count = step_size.shape[1]
    head_dim = width_x // head_count
    groups_here = width_b // N
    per_group = head_count // groups_here
    tail_len = conv_feat.shape[0] - 1
    n_blocks = tok_rows // BLOCK
    packed = jnp.concatenate([features, input_map, output_map], axis=1)
    kernel = jnp.concatenate([conv_feat, conv_input, conv_output], axis=1)
    pre_act = local_conv(packed, kernel, tok_rows)
    ctx_axes, ctx_count, outer_axis, inner_axis, tp_count = layout
    tail_rows = shifted(packed[tok_rows - tail_len :], ctx_axes, 1, ctx_count)
    edge_sums = edge_partial(tail_rows, kernel)
    pre_act = pre_act + jnp.pad(edge_sums, ((0, tok_rows - tail_len), (0, 0)))
    conv_out = jax.nn.silu(pre_act).astype(jnp.bfloat16)
    x_conv = conv_out[:, :width_x]
    b_conv = conv_out[:, width_x : width_x + width_b]
    c_conv = conv_out[:, width_x + width_b :]
    x_heads = x_conv.astype(jnp.float32).reshape(tok_rows, groups_here, per_group, head_dim)
    scaled = (x_heads * step_size.reshape(tok_rows, groups_here, per_group)[..., None]).astype(
        jnp.bfloat16
    )

    def blocked(value_entries):
        return value_entries.reshape((n_blocks, BLOCK) + value_entries.shape[1:])

    scaled_b = blocked(scaled)
    b_rows = blocked(b_conv.reshape(tok_rows, groups_here, N))
    c_rows = blocked(c_conv.reshape(tok_rows, groups_here, N))
    cum_log = jnp.cumsum(blocked(log_decay.reshape(tok_rows, groups_here, per_group)), axis=1)
    blk_states = jax.vmap(block_state)(scaled_b, b_rows, cum_log)
    blk_decay = jnp.exp(cum_log[:, -1])

    def fold_local(state_carry, block_in):
        decay_b, state_b = block_in
        return (decay_b[..., None, None] * state_carry + state_b, None)

    dev_state, _ = lax.scan(
        fold_local, jnp.zeros(blk_states.shape[1:], jnp.float32), (blk_decay, blk_states)
    )
    dev_decay = jnp.prod(blk_decay, axis=0)
    incoming = prefix_states(dev_decay, dev_state, ctx_axes, ctx_count)

    def advance(state_carry, block_in):
        scaled_k, b_k, c_k, cum_k, decay_k, state_k = block_in
        block_y = intra_block(scaled_k, b_k, c_k, cum_k) + inter_block(c_k, cum_k, state_carry)
        return (decay_k[..., None, None] * state_carry + state_k, block_y)

    _, ssm_y = lax.scan(
        advance, incoming, (scaled_b, b_rows, c_rows, cum_log, blk_decay, blk_states)
    )
    mixed_y = ssm_y.reshape(tok_rows, groups_here, per_group, head_dim)
    mixed_y = mixed_y + skip_gain.reshape(groups_here, per_group)[..., None] * x_heads
    gated_y = mixed_y.reshape(tok_rows, width_x) * jax.nn.silu(gate_in.astype(jnp.float32))
    grouped = gated_y.reshape(tok_rows, groups_here, width_x // groups_here)
    inv_root = lax.rsqrt(jnp.mean(grouped * grouped, axis=-1, keepdims=True) + 1e-05)
    hidden = ((grouped * inv_root).reshape(tok_rows, width_x) * norm_gain).astype(jnp.bfloat16)
    if outer_axis is None:
        partial_out = jnp.dot(
            hidden,
            lax.all_gather(out_weight, ctx_axes, axis=1, tiled=True),
            preferred_element_type=jnp.float32,
        )
        return lax.psum_scatter(partial_out, "tp", scatter_dimension=1, tiled=True).astype(
            jnp.bfloat16
        )
    outer_at = lax.axis_index(outer_axis)
    tp_at = lax.axis_index("tp")
    arrived = [hidden] + [
        lax.ppermute(hidden, outer_axis, [(s, (s + d) % tp_count) for s in range(tp_count)])
        for d in range(1, tp_count)
    ]
    cols_all = lax.all_gather(out_weight, inner_axis, axis=1, tiled=True)
    by_source = jnp.stack(
        [jnp.dot(rows, cols_all, preferred_element_type=jnp.float32) for rows in arrived]
    )

    def for_target(target):
        return lax.dynamic_index_in_dim(
            by_source, (outer_at - target + tp_count) % tp_count, 0, keepdims=False
        )

    held = {m: for_target(tp_at ^ m) for m in range(tp_count)}
    bit = 1
    while bit < tp_count:
        going = sorted(m for m in held if m & bit)
        got = lax.ppermute(
            jnp.stack([held[m] for m in going]),
            "tp",
            [(s, s ^ bit) for s in range(tp_count)],
        )
        held = {m: held[m] for m in held if not m & bit}
        for index, m in enumerate(going):
            held[m ^ bit] = held[m ^ bit] + got[index]
        bit *= 2
    swap = [(o * tp_count + t, t * tp_count + o) for o in range(tp_count) for t in range(tp_count)]
    return lax.ppermute(held[0].astype(jnp.bfloat16), (outer_axis, "tp"), swap)


def solution(mesh):
    ctx_count = mesh.shape["ctx"]
    tp_count = mesh.shape["tp"]
    if ctx_count % tp_count == 0 and tp_count & (tp_count - 1) == 0:
        inner = ctx_count // tp_count
        grid = mesh.devices.reshape(tp_count, inner, tp_count)
        mesh = jax.sharding.Mesh(grid, ("outer", "inner", "tp"))
        ctx_axes = ("outer", "inner")
        layout = (ctx_axes, ctx_count, "outer", "inner", tp_count)
    else:
        ctx_axes = "ctx"
        layout = (ctx_axes, ctx_count, None, None, tp_count)
    placed = (
        P(ctx_axes, "tp"),
        P(ctx_axes, "tp"),
        P(ctx_axes, "tp"),
        P(ctx_axes, "tp"),
        P(None, "tp"),
        P(None, "tp"),
        P(None, "tp"),
        P(ctx_axes, "tp"),
        P(ctx_axes, "tp"),
        P("tp"),
        P("tp"),
        P("tp", ctx_axes),
    )
    return jax.shard_map(
        functools.partial(on_device, layout),
        mesh=mesh,
        in_specs=placed,
        out_specs=P(ctx_axes, "tp"),
        check_vma=False,
    )
```

```python
import functools

import jax
import jax.numpy as jnp
from jax import lax
from jax.sharding import PartitionSpec as P

N = 128
BLOCK = 256


def shifted(value, axis, steps, count):
    first, last = (max(0, -steps), min(count, count - steps))
    return lax.ppermute(value, axis, [(source, source + steps) for source in range(first, last)])


def local_conv(packed, kernel, tok_rows):
    tail_len = kernel.shape[0] - 1
    padded = jnp.pad(packed.astype(jnp.float32), ((tail_len, 0), (0, 0)))
    pre_act = jnp.zeros((tok_rows, kernel.shape[1]), jnp.float32)
    for tap_index in range(kernel.shape[0]):
        pre_act = pre_act + kernel[tap_index] * padded[tap_index : tap_index + tok_rows]
    return pre_act


def edge_partial(tail_rows, kernel):
    tail_len = kernel.shape[0] - 1
    tail_vals = tail_rows.astype(jnp.float32)
    outputs = []
    for row_index in range(tail_len):
        accum = jnp.zeros((kernel.shape[1],), jnp.float32)
        for tap_index in range(tail_len - row_index):
            accum = accum + kernel[tap_index] * tail_vals[row_index + tap_index]
        outputs.append(accum)
    return jnp.stack(outputs, axis=0)


def intra_block(scaled, b_rows, c_rows, cum_log):
    scores = jnp.einsum("tgn,sgn->gts", c_rows, b_rows, preferred_element_type=jnp.float32)
    cum_cols = jnp.moveaxis(cum_log, 0, -1)
    log_gap = cum_cols[..., :, None] - cum_cols[..., None, :]
    block_len = cum_log.shape[0]
    causal = jnp.arange(block_len)[:, None] >= jnp.arange(block_len)[None, :]
    decays = jnp.exp(jnp.where(causal, log_gap, -jnp.inf))
    weights = (scores[:, None] * decays).astype(jnp.bfloat16)
    return jnp.einsum("gjts,sgjp->tgjp", weights, scaled, preferred_element_type=jnp.float32)


def block_state(scaled, b_rows, cum_log):
    end_decay = jnp.exp(cum_log[-1][None] - cum_log)
    b_weighted = (b_rows.astype(jnp.float32)[:, :, None, :] * end_decay[..., None]).astype(
        jnp.bfloat16
    )
    return jnp.einsum("sgjp,sgjn->gjpn", scaled, b_weighted, preferred_element_type=jnp.float32)


def inter_block(c_rows, cum_log, state_carry):
    rounded = state_carry.astype(jnp.bfloat16)
    inner = jnp.einsum("tgn,gjpn->tgjp", c_rows, rounded, preferred_element_type=jnp.float32)
    return inner * jnp.exp(cum_log)[..., None]


def combine(first_part, second_part):
    decay_first, state_first = first_part
    decay_second, state_second = second_part
    return (decay_first * decay_second, decay_second[..., None, None] * state_first + state_second)


def prefix_states(dev_decay, dev_state, axis, count):
    own = (dev_decay, dev_state)
    if count == 1:
        return jnp.zeros_like(dev_state)
    got = shifted(own, axis, 1, count)
    before = got
    upto = combine(got, own)
    step = 2
    while step < count:
        got = shifted(upto, axis, step, count)
        before = combine(got, before)
        if step * 2 < count:
            upto = combine(got, upto)
        step *= 2
    return before[1]


def on_device(
    layout,
    features,
    input_map,
    output_map,
    gate_in,
    conv_feat,
    conv_input,
    conv_output,
    step_size,
    log_decay,
    skip_gain,
    norm_gain,
    out_weight,
):
    tok_rows, width_x = features.shape
    width_b = input_map.shape[1]
    head_count = step_size.shape[1]
    head_dim = width_x // head_count
    groups_here = width_b // N
    per_group = head_count // groups_here
    tail_len = conv_feat.shape[0] - 1
    n_blocks = tok_rows // BLOCK
    packed = jnp.concatenate([features, input_map, output_map], axis=1)
    kernel = jnp.concatenate([conv_feat, conv_input, conv_output], axis=1)
    pre_act = local_conv(packed, kernel, tok_rows)
    ctx_axes, ctx_count, outer_axis, inner_axis, tp_count = layout
    tail_rows = shifted(packed[tok_rows - tail_len :], ctx_axes, 1, ctx_count)
    edge_sums = edge_partial(tail_rows, kernel)
    pre_act = pre_act + jnp.pad(edge_sums, ((0, tok_rows - tail_len), (0, 0)))
    conv_out = jax.nn.silu(pre_act).astype(jnp.bfloat16)
    x_conv = conv_out[:, :width_x]
    b_conv = conv_out[:, width_x : width_x + width_b]
    c_conv = conv_out[:, width_x + width_b :]
    x_heads = x_conv.astype(jnp.float32).reshape(tok_rows, groups_here, per_group, head_dim)
    scaled = (x_heads * step_size.reshape(tok_rows, groups_here, per_group)[..., None]).astype(
        jnp.bfloat16
    )

    def blocked(value_entries):
        return value_entries.reshape((n_blocks, BLOCK) + value_entries.shape[1:])

    scaled_b = blocked(scaled)
    b_rows = blocked(b_conv.reshape(tok_rows, groups_here, N))
    c_rows = blocked(c_conv.reshape(tok_rows, groups_here, N))
    cum_log = jnp.cumsum(blocked(log_decay.reshape(tok_rows, groups_here, per_group)), axis=1)
    blk_states = jax.vmap(block_state)(scaled_b, b_rows, cum_log)
    blk_decay = jnp.exp(cum_log[:, -1])

    def fold_local(state_carry, block_in):
        decay_b, state_b = block_in
        return (decay_b[..., None, None] * state_carry + state_b, None)

    dev_state, _ = lax.scan(
        fold_local, jnp.zeros(blk_states.shape[1:], jnp.float32), (blk_decay, blk_states)
    )
    dev_decay = jnp.prod(blk_decay, axis=0)
    incoming = prefix_states(dev_decay, dev_state, ctx_axes, ctx_count)

    def advance(state_carry, block_in):
        scaled_k, b_k, c_k, cum_k, decay_k, state_k = block_in
        block_y = intra_block(scaled_k, b_k, c_k, cum_k) + inter_block(c_k, cum_k, state_carry)
        return (decay_k[..., None, None] * state_carry + state_k, block_y)

    _, ssm_y = lax.scan(
        advance, incoming, (scaled_b, b_rows, c_rows, cum_log, blk_decay, blk_states)
    )
    mixed_y = ssm_y.reshape(tok_rows, groups_here, per_group, head_dim)
    mixed_y = mixed_y + skip_gain.reshape(groups_here, per_group)[..., None] * x_heads
    gated_y = mixed_y.reshape(tok_rows, width_x) * jax.nn.silu(gate_in.astype(jnp.float32))
    grouped = gated_y.reshape(tok_rows, groups_here, width_x // groups_here)
    inv_root = lax.rsqrt(jnp.mean(grouped * grouped, axis=-1, keepdims=True) + 1e-05)
    hidden = ((grouped * inv_root).reshape(tok_rows, width_x) * norm_gain).astype(jnp.bfloat16)
    if outer_axis is None:
        partial_out = jnp.dot(
            hidden,
            lax.all_gather(out_weight, ctx_axes, axis=1, tiled=True),
            preferred_element_type=jnp.float32,
        )
        return lax.psum_scatter(partial_out, "tp", scatter_dimension=1, tiled=True).astype(
            jnp.bfloat16
        )
    outer_at = lax.axis_index(outer_axis)
    tp_at = lax.axis_index("tp")
    from_left, from_right = {}, {}
    going_right = going_left = hidden
    for step in range(1, tp_count):
        going_right = lax.ppermute(
            going_right, outer_axis, [(s, s + 1) for s in range(step - 1, tp_count - 1)]
        )
        going_left = lax.ppermute(
            going_left, outer_axis, [(s, s - 1) for s in range(1, tp_count - step + 1)]
        )
        from_left[step], from_right[step] = going_right, going_left
    arrived = [hidden] + [
        jnp.where(outer_at >= d, from_left[d], from_right[tp_count - d])
        for d in range(1, tp_count)
    ]
    cols_all = lax.all_gather(out_weight, inner_axis, axis=1, tiled=True)
    by_source = jnp.stack(
        [jnp.dot(rows, cols_all, preferred_element_type=jnp.float32) for rows in arrived]
    )

    def for_target(target):
        return lax.dynamic_index_in_dim(
            by_source, (outer_at - target + tp_count) % tp_count, 0, keepdims=False
        )

    held = {m: for_target(tp_at ^ m) for m in range(tp_count)}
    bit = 1
    while bit < tp_count:
        going = sorted(m for m in held if m & bit)
        got = lax.ppermute(
            jnp.stack([held[m] for m in going]),
            "tp",
            [(s, s ^ bit) for s in range(tp_count)],
        )
        held = {m: held[m] for m in held if not m & bit}
        for index, m in enumerate(going):
            held[m ^ bit] = held[m ^ bit] + got[index]
        bit *= 2
    swap = [(o * tp_count + t, t * tp_count + o) for o in range(tp_count) for t in range(tp_count)]
    return lax.ppermute(held[0].astype(jnp.bfloat16), (outer_axis, "tp"), swap)


def solution(mesh):
    ctx_count = mesh.shape["ctx"]
    tp_count = mesh.shape["tp"]
    if ctx_count % tp_count == 0 and tp_count & (tp_count - 1) == 0:
        inner = ctx_count // tp_count
        grid = mesh.devices.reshape(tp_count, inner, tp_count)
        mesh = jax.sharding.Mesh(grid, ("outer", "inner", "tp"))
        ctx_axes = ("outer", "inner")
        layout = (ctx_axes, ctx_count, "outer", "inner", tp_count)
    else:
        ctx_axes = "ctx"
        layout = (ctx_axes, ctx_count, None, None, tp_count)
    placed = (
        P(ctx_axes, "tp"),
        P(ctx_axes, "tp"),
        P(ctx_axes, "tp"),
        P(ctx_axes, "tp"),
        P(None, "tp"),
        P(None, "tp"),
        P(None, "tp"),
        P(ctx_axes, "tp"),
        P(ctx_axes, "tp"),
        P("tp"),
        P("tp"),
        P("tp", ctx_axes),
    )
    return jax.shard_map(
        functools.partial(on_device, layout),
        mesh=mesh,
        in_specs=placed,
        out_specs=P(ctx_axes, "tp"),
        check_vma=False,
    )
```

```python
import functools

import jax
import jax.numpy as jnp
from jax import lax
from jax.sharding import PartitionSpec as P

N = 128
BLOCK = 256


def shifted(value, axis, steps, count):
    first, last = (max(0, -steps), min(count, count - steps))
    return lax.ppermute(value, axis, [(source, source + steps) for source in range(first, last)])


def local_conv(packed, kernel, tok_rows):
    tail_len = kernel.shape[0] - 1
    padded = jnp.pad(packed.astype(jnp.float32), ((tail_len, 0), (0, 0)))
    pre_act = jnp.zeros((tok_rows, kernel.shape[1]), jnp.float32)
    for tap_index in range(kernel.shape[0]):
        pre_act = pre_act + kernel[tap_index] * padded[tap_index : tap_index + tok_rows]
    return pre_act


def edge_partial(tail_rows, kernel):
    tail_len = kernel.shape[0] - 1
    tail_vals = tail_rows.astype(jnp.float32)
    outputs = []
    for row_index in range(tail_len):
        accum = jnp.zeros((kernel.shape[1],), jnp.float32)
        for tap_index in range(tail_len - row_index):
            accum = accum + kernel[tap_index] * tail_vals[row_index + tap_index]
        outputs.append(accum)
    return jnp.stack(outputs, axis=0)


def intra_block(scaled, b_rows, c_rows, cum_log):
    scores = jnp.einsum("tgn,sgn->gts", c_rows, b_rows, preferred_element_type=jnp.float32)
    cum_cols = jnp.moveaxis(cum_log, 0, -1)
    log_gap = cum_cols[..., :, None] - cum_cols[..., None, :]
    block_len = cum_log.shape[0]
    causal = jnp.arange(block_len)[:, None] >= jnp.arange(block_len)[None, :]
    decays = jnp.exp(jnp.where(causal, log_gap, -jnp.inf))
    weights = (scores[:, None] * decays).astype(jnp.bfloat16)
    return jnp.einsum("gjts,sgjp->tgjp", weights, scaled, preferred_element_type=jnp.float32)


def block_state(scaled, b_rows, cum_log):
    end_decay = jnp.exp(cum_log[-1][None] - cum_log)
    b_weighted = (b_rows.astype(jnp.float32)[:, :, None, :] * end_decay[..., None]).astype(
        jnp.bfloat16
    )
    return jnp.einsum("sgjp,sgjn->gjpn", scaled, b_weighted, preferred_element_type=jnp.float32)


def inter_block(c_rows, cum_log, state_carry):
    rounded = state_carry.astype(jnp.bfloat16)
    inner = jnp.einsum("tgn,gjpn->tgjp", c_rows, rounded, preferred_element_type=jnp.float32)
    return inner * jnp.exp(cum_log)[..., None]


def combine(first_part, second_part):
    decay_first, state_first = first_part
    decay_second, state_second = second_part
    return (
        decay_first * decay_second,
        decay_second[..., None, None] * state_first.astype(jnp.float32) + state_second,
    )


def on_link(part):
    decay, state = part
    return (decay, state.astype(jnp.bfloat16))


def prefix_states(dev_decay, dev_state, axis, count):
    own = (dev_decay, dev_state)
    if count == 1:
        return jnp.zeros_like(dev_state)
    got = shifted(on_link(own), axis, 1, count)
    before = got
    upto = combine(got, own)
    step = 2
    while step < count:
        got = shifted(on_link(upto), axis, step, count)
        before = combine(got, before)
        if step * 2 < count:
            upto = combine(got, upto)
        step *= 2
    return before[1].astype(jnp.float32)


def on_device(
    layout,
    features,
    input_map,
    output_map,
    gate_in,
    conv_feat,
    conv_input,
    conv_output,
    step_size,
    log_decay,
    skip_gain,
    norm_gain,
    out_weight,
):
    tok_rows, width_x = features.shape
    width_b = input_map.shape[1]
    head_count = step_size.shape[1]
    head_dim = width_x // head_count
    groups_here = width_b // N
    per_group = head_count // groups_here
    tail_len = conv_feat.shape[0] - 1
    n_blocks = tok_rows // BLOCK
    packed = jnp.concatenate([features, input_map, output_map], axis=1)
    kernel = jnp.concatenate([conv_feat, conv_input, conv_output], axis=1)
    pre_act = local_conv(packed, kernel, tok_rows)
    ctx_axes, ctx_count, outer_axis, inner_axis, tp_count = layout
    tail_rows = shifted(packed[tok_rows - tail_len :], ctx_axes, 1, ctx_count)
    edge_sums = edge_partial(tail_rows, kernel)
    pre_act = pre_act + jnp.pad(edge_sums, ((0, tok_rows - tail_len), (0, 0)))
    conv_out = jax.nn.silu(pre_act).astype(jnp.bfloat16)
    x_conv = conv_out[:, :width_x]
    b_conv = conv_out[:, width_x : width_x + width_b]
    c_conv = conv_out[:, width_x + width_b :]
    x_heads = x_conv.astype(jnp.float32).reshape(tok_rows, groups_here, per_group, head_dim)
    scaled = (x_heads * step_size.reshape(tok_rows, groups_here, per_group)[..., None]).astype(
        jnp.bfloat16
    )

    def blocked(value_entries):
        return value_entries.reshape((n_blocks, BLOCK) + value_entries.shape[1:])

    scaled_b = blocked(scaled)
    b_rows = blocked(b_conv.reshape(tok_rows, groups_here, N))
    c_rows = blocked(c_conv.reshape(tok_rows, groups_here, N))
    cum_log = jnp.cumsum(blocked(log_decay.reshape(tok_rows, groups_here, per_group)), axis=1)
    blk_states = jax.vmap(block_state)(scaled_b, b_rows, cum_log)
    blk_decay = jnp.exp(cum_log[:, -1])

    def fold_local(state_carry, block_in):
        decay_b, state_b = block_in
        return (decay_b[..., None, None] * state_carry + state_b, None)

    dev_state, _ = lax.scan(
        fold_local, jnp.zeros(blk_states.shape[1:], jnp.float32), (blk_decay, blk_states)
    )
    dev_decay = jnp.prod(blk_decay, axis=0)
    incoming = prefix_states(dev_decay, dev_state, ctx_axes, ctx_count)

    def advance(state_carry, block_in):
        scaled_k, b_k, c_k, cum_k, decay_k, state_k = block_in
        block_y = intra_block(scaled_k, b_k, c_k, cum_k) + inter_block(c_k, cum_k, state_carry)
        return (decay_k[..., None, None] * state_carry + state_k, block_y)

    _, ssm_y = lax.scan(
        advance, incoming, (scaled_b, b_rows, c_rows, cum_log, blk_decay, blk_states)
    )
    mixed_y = ssm_y.reshape(tok_rows, groups_here, per_group, head_dim)
    mixed_y = mixed_y + skip_gain.reshape(groups_here, per_group)[..., None] * x_heads
    gated_y = mixed_y.reshape(tok_rows, width_x) * jax.nn.silu(gate_in.astype(jnp.float32))
    grouped = gated_y.reshape(tok_rows, groups_here, width_x // groups_here)
    inv_root = lax.rsqrt(jnp.mean(grouped * grouped, axis=-1, keepdims=True) + 1e-05)
    hidden = ((grouped * inv_root).reshape(tok_rows, width_x) * norm_gain).astype(jnp.bfloat16)
    if outer_axis is None:
        partial_out = jnp.dot(
            hidden,
            lax.all_gather(out_weight, ctx_axes, axis=1, tiled=True),
            preferred_element_type=jnp.float32,
        )
        return lax.psum_scatter(partial_out, "tp", scatter_dimension=1, tiled=True).astype(
            jnp.bfloat16
        )
    outer_at = lax.axis_index(outer_axis)
    tp_at = lax.axis_index("tp")
    from_left, from_right = {}, {}
    going_right = going_left = hidden
    for step in range(1, tp_count):
        going_right = lax.ppermute(
            going_right, outer_axis, [(s, s + 1) for s in range(step - 1, tp_count - 1)]
        )
        going_left = lax.ppermute(
            going_left, outer_axis, [(s, s - 1) for s in range(1, tp_count - step + 1)]
        )
        from_left[step], from_right[step] = going_right, going_left
    arrived = [hidden] + [
        jnp.where(outer_at >= d, from_left[d], from_right[tp_count - d])
        for d in range(1, tp_count)
    ]
    cols_all = lax.all_gather(out_weight, inner_axis, axis=1, tiled=True)
    by_source = jnp.stack(
        [jnp.dot(rows, cols_all, preferred_element_type=jnp.float32) for rows in arrived]
    )

    def for_target(target):
        return lax.dynamic_index_in_dim(
            by_source, (outer_at - target + tp_count) % tp_count, 0, keepdims=False
        )

    held = {m: for_target(tp_at ^ m) for m in range(tp_count)}
    bit = 1
    while bit < tp_count:
        going = sorted(m for m in held if m & bit)
        sent = jnp.stack([held[m] for m in going])
        got = lax.ppermute(
            sent if bit == 1 else sent.astype(jnp.bfloat16),
            "tp",
            [(s, s ^ bit) for s in range(tp_count)],
        )
        held = {m: held[m] for m in held if not m & bit}
        for index, m in enumerate(going):
            held[m ^ bit] = held[m ^ bit] + got[index].astype(jnp.float32)
        bit *= 2
    swap = [(o * tp_count + t, t * tp_count + o) for o in range(tp_count) for t in range(tp_count)]
    return lax.ppermute(held[0].astype(jnp.bfloat16), (outer_axis, "tp"), swap)


def solution(mesh):
    ctx_count = mesh.shape["ctx"]
    tp_count = mesh.shape["tp"]
    if ctx_count % tp_count == 0 and tp_count & (tp_count - 1) == 0:
        inner = ctx_count // tp_count
        grid = mesh.devices.reshape(tp_count, inner, tp_count)
        mesh = jax.sharding.Mesh(grid, ("outer", "inner", "tp"))
        ctx_axes = ("outer", "inner")
        layout = (ctx_axes, ctx_count, "outer", "inner", tp_count)
    else:
        ctx_axes = "ctx"
        layout = (ctx_axes, ctx_count, None, None, tp_count)
    placed = (
        P(ctx_axes, "tp"),
        P(ctx_axes, "tp"),
        P(ctx_axes, "tp"),
        P(ctx_axes, "tp"),
        P(None, "tp"),
        P(None, "tp"),
        P(None, "tp"),
        P(ctx_axes, "tp"),
        P(ctx_axes, "tp"),
        P("tp"),
        P("tp"),
        P("tp", ctx_axes),
    )
    return jax.shard_map(
        functools.partial(on_device, layout),
        mesh=mesh,
        in_specs=placed,
        out_specs=P(ctx_axes, "tp"),
        check_vma=False,
    )
```

```python
import functools

import jax
import jax.numpy as jnp
from jax import lax
from jax.sharding import PartitionSpec as P

N = 128
BLOCK = 256


def shifted(value, axis, steps, count):
    first, last = (max(0, -steps), min(count, count - steps))
    return lax.ppermute(value, axis, [(source, source + steps) for source in range(first, last)])


def local_conv(packed, kernel, tok_rows):
    tail_len = kernel.shape[0] - 1
    padded = jnp.pad(packed.astype(jnp.float32), ((tail_len, 0), (0, 0)))
    pre_act = jnp.zeros((tok_rows, kernel.shape[1]), jnp.float32)
    for tap_index in range(kernel.shape[0]):
        pre_act = pre_act + kernel[tap_index] * padded[tap_index : tap_index + tok_rows]
    return pre_act


def edge_partial(tail_rows, kernel):
    tail_len = kernel.shape[0] - 1
    tail_vals = tail_rows.astype(jnp.float32)
    outputs = []
    for row_index in range(tail_len):
        accum = jnp.zeros((kernel.shape[1],), jnp.float32)
        for tap_index in range(tail_len - row_index):
            accum = accum + kernel[tap_index] * tail_vals[row_index + tap_index]
        outputs.append(accum)
    return jnp.stack(outputs, axis=0)


def intra_block(scaled, b_rows, c_rows, cum_log):
    scores = jnp.einsum("tgn,sgn->gts", c_rows, b_rows, preferred_element_type=jnp.float32)
    cum_cols = jnp.moveaxis(cum_log, 0, -1)
    log_gap = cum_cols[..., :, None] - cum_cols[..., None, :]
    block_len = cum_log.shape[0]
    causal = jnp.arange(block_len)[:, None] >= jnp.arange(block_len)[None, :]
    decays = jnp.exp(jnp.where(causal, log_gap, -jnp.inf))
    weights = (scores[:, None] * decays).astype(jnp.bfloat16)
    return jnp.einsum("gjts,sgjp->tgjp", weights, scaled, preferred_element_type=jnp.float32)


def block_state(scaled, b_rows, cum_log):
    end_decay = jnp.exp(cum_log[-1][None] - cum_log)
    b_weighted = (b_rows.astype(jnp.float32)[:, :, None, :] * end_decay[..., None]).astype(
        jnp.bfloat16
    )
    return jnp.einsum("sgjp,sgjn->gjpn", scaled, b_weighted, preferred_element_type=jnp.float32)


def inter_block(c_rows, cum_log, state_carry):
    rounded = state_carry.astype(jnp.bfloat16)
    inner = jnp.einsum("tgn,gjpn->tgjp", c_rows, rounded, preferred_element_type=jnp.float32)
    return inner * jnp.exp(cum_log)[..., None]


def combine(first_part, second_part):
    decay_first, state_first = first_part
    decay_second, state_second = second_part
    return (
        decay_first * decay_second,
        decay_second[..., None, None] * state_first.astype(jnp.float32) + state_second,
    )


def on_link(part):
    decay, state = part
    return (decay, state.astype(jnp.bfloat16))


def prefix_states(dev_decay, dev_state, axis, count):
    own = (dev_decay, dev_state)
    if count == 1:
        return jnp.zeros_like(dev_state)
    got = shifted(on_link(own), axis, 1, count)
    before = got
    upto = combine(got, own)
    step = 2
    while step < count:
        got = shifted(on_link(upto), axis, step, count)
        before = combine(got, before)
        if step * 2 < count:
            upto = combine(got, upto)
        step *= 2
    return before[1].astype(jnp.float32)


def on_device(
    layout,
    features,
    input_map,
    output_map,
    gate_in,
    conv_feat,
    conv_input,
    conv_output,
    step_size,
    log_decay,
    skip_gain,
    norm_gain,
    out_weight,
):
    tok_rows, width_x = features.shape
    width_b = input_map.shape[1]
    head_count = step_size.shape[1]
    head_dim = width_x // head_count
    groups_here = width_b // N
    per_group = head_count // groups_here
    tail_len = conv_feat.shape[0] - 1
    n_blocks = tok_rows // BLOCK
    packed = jnp.concatenate([features, input_map, output_map], axis=1)
    kernel = jnp.concatenate([conv_feat, conv_input, conv_output], axis=1)
    pre_act = local_conv(packed, kernel, tok_rows)
    ctx_axes, ctx_count, outer_axis, inner_axis, tp_count = layout
    tail_rows = shifted(packed[tok_rows - tail_len :], ctx_axes, 1, ctx_count)
    edge_sums = edge_partial(tail_rows, kernel)
    pre_act = pre_act + jnp.pad(edge_sums, ((0, tok_rows - tail_len), (0, 0)))
    conv_out = jax.nn.silu(pre_act).astype(jnp.bfloat16)
    x_conv = conv_out[:, :width_x]
    b_conv = conv_out[:, width_x : width_x + width_b]
    c_conv = conv_out[:, width_x + width_b :]
    x_heads = x_conv.astype(jnp.float32).reshape(tok_rows, groups_here, per_group, head_dim)
    scaled = (x_heads * step_size.reshape(tok_rows, groups_here, per_group)[..., None]).astype(
        jnp.bfloat16
    )

    def blocked(value_entries):
        return value_entries.reshape((n_blocks, BLOCK) + value_entries.shape[1:])

    scaled_b = blocked(scaled)
    b_rows = blocked(b_conv.reshape(tok_rows, groups_here, N))
    c_rows = blocked(c_conv.reshape(tok_rows, groups_here, N))
    cum_log = jnp.cumsum(blocked(log_decay.reshape(tok_rows, groups_here, per_group)), axis=1)
    blk_states = jax.vmap(block_state)(scaled_b, b_rows, cum_log)
    blk_decay = jnp.exp(cum_log[:, -1])

    def fold_local(state_carry, block_in):
        decay_b, state_b = block_in
        return (decay_b[..., None, None] * state_carry + state_b, None)

    dev_state, _ = lax.scan(
        fold_local, jnp.zeros(blk_states.shape[1:], jnp.float32), (blk_decay, blk_states)
    )
    dev_decay = jnp.prod(blk_decay, axis=0)
    incoming = prefix_states(dev_decay, dev_state, ctx_axes, ctx_count)

    def advance(state_carry, block_in):
        scaled_k, b_k, c_k, cum_k, decay_k, state_k = block_in
        block_y = intra_block(scaled_k, b_k, c_k, cum_k) + inter_block(c_k, cum_k, state_carry)
        return (decay_k[..., None, None] * state_carry + state_k, block_y)

    _, ssm_y = lax.scan(
        advance, incoming, (scaled_b, b_rows, c_rows, cum_log, blk_decay, blk_states)
    )
    mixed_y = ssm_y.reshape(tok_rows, groups_here, per_group, head_dim)
    mixed_y = mixed_y + skip_gain.reshape(groups_here, per_group)[..., None] * x_heads
    gated_y = mixed_y.reshape(tok_rows, width_x) * jax.nn.silu(gate_in.astype(jnp.float32))
    grouped = gated_y.reshape(tok_rows, groups_here, width_x // groups_here)
    inv_root = lax.rsqrt(jnp.mean(grouped * grouped, axis=-1, keepdims=True) + 1e-05)
    hidden = ((grouped * inv_root).reshape(tok_rows, width_x) * norm_gain).astype(jnp.bfloat16)
    if outer_axis is None:
        partial_out = jnp.dot(
            hidden,
            lax.all_gather(out_weight, ctx_axes, axis=1, tiled=True),
            preferred_element_type=jnp.float32,
        )
        return lax.psum_scatter(partial_out, "tp", scatter_dimension=1, tiled=True).astype(
            jnp.bfloat16
        )
    outer_at = lax.axis_index(outer_axis)
    tp_at = lax.axis_index("tp")
    half = tok_rows // 2
    across_y = lax.ppermute(hidden, outer_axis, [(s, s ^ 1) for s in range(tp_count)])
    across_z = lax.ppermute(hidden, outer_axis, [(s, s ^ 2) for s in range(tp_count)])
    first_half = lax.ppermute(across_y[:half], outer_axis, [(s, s ^ 2) for s in range(tp_count)])
    second_half = lax.ppermute(across_z[half:], outer_axis, [(s, s ^ 1) for s in range(tp_count)])
    arrived = [hidden, across_y, across_z, jnp.concatenate([first_half, second_half], axis=0)]
    cols_all = lax.all_gather(out_weight, inner_axis, axis=1, tiled=True)
    by_source = jnp.stack(
        [jnp.dot(rows, cols_all, preferred_element_type=jnp.float32) for rows in arrived]
    )

    def for_target(target):
        return lax.dynamic_index_in_dim(
            by_source, outer_at ^ target, 0, keepdims=False
        )

    held = {m: for_target(tp_at ^ m) for m in range(tp_count)}
    bit = 1
    while bit < tp_count:
        going = sorted(m for m in held if m & bit)
        sent = jnp.stack([held[m] for m in going])
        got = lax.ppermute(
            sent if bit == 1 else sent.astype(jnp.bfloat16),
            "tp",
            [(s, s ^ bit) for s in range(tp_count)],
        )
        held = {m: held[m] for m in held if not m & bit}
        for index, m in enumerate(going):
            held[m ^ bit] = held[m ^ bit] + got[index].astype(jnp.float32)
        bit *= 2
    inner_count = ctx_count // tp_count
    width = out_weight.shape[1]
    final = held[0].astype(jnp.bfloat16)
    placed = [[] for _ in range(inner_count)]
    for piece in range(inner_count):
        for source in range(tp_count):
            column = piece * tp_count + source
            pairs = [
                (source * tp_count + t, t * tp_count + column // inner_count)
                for t in range(tp_count)
            ]
            placed[column % inner_count].append(
                lax.ppermute(
                    final[:, piece * width : (piece + 1) * width], (outer_axis, "tp"), pairs
                )
            )
    return jnp.concatenate([sum(parts[1:], parts[0]) for parts in placed], axis=1)


def solution(mesh):
    ctx_count = mesh.shape["ctx"]
    tp_count = mesh.shape["tp"]
    if ctx_count % tp_count == 0 and tp_count == 4:
        inner = ctx_count // tp_count
        grid = mesh.devices.reshape(inner, tp_count, tp_count)
        mesh = jax.sharding.Mesh(grid, ("inner", "outer", "tp"))
        ctx_axes = ("inner", "outer")
        layout = (ctx_axes, ctx_count, "outer", "inner", tp_count)
    else:
        ctx_axes = "ctx"
        layout = (ctx_axes, ctx_count, None, None, tp_count)
    placed = (
        P(ctx_axes, "tp"),
        P(ctx_axes, "tp"),
        P(ctx_axes, "tp"),
        P(ctx_axes, "tp"),
        P(None, "tp"),
        P(None, "tp"),
        P(None, "tp"),
        P(ctx_axes, "tp"),
        P(ctx_axes, "tp"),
        P("tp"),
        P("tp"),
        P("tp", ctx_axes),
    )
    return jax.shard_map(
        functools.partial(on_device, layout),
        mesh=mesh,
        in_specs=placed,
        out_specs=P(ctx_axes, "tp"),
        check_vma=False,
    )
```

```python
import functools

import jax
import jax.numpy as jnp
from jax import lax
from jax.sharding import PartitionSpec as P

N = 128
BLOCK = 256


def shifted(value, axis, steps, count):
    first, last = (max(0, -steps), min(count, count - steps))
    return lax.ppermute(value, axis, [(source, source + steps) for source in range(first, last)])


def local_conv(packed, kernel, tok_rows):
    tail_len = kernel.shape[0] - 1
    padded = jnp.pad(packed.astype(jnp.float32), ((tail_len, 0), (0, 0)))
    pre_act = jnp.zeros((tok_rows, kernel.shape[1]), jnp.float32)
    for tap_index in range(kernel.shape[0]):
        pre_act = pre_act + kernel[tap_index] * padded[tap_index : tap_index + tok_rows]
    return pre_act


def edge_partial(tail_rows, kernel):
    tail_len = kernel.shape[0] - 1
    tail_vals = tail_rows.astype(jnp.float32)
    outputs = []
    for row_index in range(tail_len):
        accum = jnp.zeros((kernel.shape[1],), jnp.float32)
        for tap_index in range(tail_len - row_index):
            accum = accum + kernel[tap_index] * tail_vals[row_index + tap_index]
        outputs.append(accum)
    return jnp.stack(outputs, axis=0)


def intra_block(scaled, b_rows, c_rows, cum_log):
    scores = jnp.einsum("tgn,sgn->gts", c_rows, b_rows, preferred_element_type=jnp.float32)
    cum_cols = jnp.moveaxis(cum_log, 0, -1)
    log_gap = cum_cols[..., :, None] - cum_cols[..., None, :]
    block_len = cum_log.shape[0]
    causal = jnp.arange(block_len)[:, None] >= jnp.arange(block_len)[None, :]
    decays = jnp.exp(jnp.where(causal, log_gap, -jnp.inf))
    weights = (scores[:, None] * decays).astype(jnp.bfloat16)
    return jnp.einsum("gjts,sgjp->tgjp", weights, scaled, preferred_element_type=jnp.float32)


def block_state(scaled, b_rows, cum_log):
    end_decay = jnp.exp(cum_log[-1][None] - cum_log)
    b_weighted = (b_rows.astype(jnp.float32)[:, :, None, :] * end_decay[..., None]).astype(
        jnp.bfloat16
    )
    return jnp.einsum("sgjp,sgjn->gjpn", scaled, b_weighted, preferred_element_type=jnp.float32)


def inter_block(c_rows, cum_log, state_carry):
    rounded = state_carry.astype(jnp.bfloat16)
    inner = jnp.einsum("tgn,gjpn->tgjp", c_rows, rounded, preferred_element_type=jnp.float32)
    return inner * jnp.exp(cum_log)[..., None]


def combine(first_part, second_part):
    decay_first, state_first = first_part
    decay_second, state_second = second_part
    return (
        decay_first * decay_second,
        decay_second[..., None, None] * state_first.astype(jnp.float32) + state_second,
    )


def on_link(part):
    decay, state = part
    return (decay, state.astype(jnp.bfloat16))


def prefix_states(dev_decay, dev_state, axis, count):
    own = (dev_decay, dev_state)
    if count == 1:
        return jnp.zeros_like(dev_state)
    got = shifted(on_link(own), axis, 1, count)
    before = got
    upto = combine(got, own)
    step = 2
    while step < count:
        got = shifted(on_link(upto), axis, step, count)
        before = combine(got, before)
        if step * 2 < count:
            upto = combine(got, upto)
        step *= 2
    return before[1].astype(jnp.float32)


def on_device(
    layout,
    features,
    input_map,
    output_map,
    gate_in,
    conv_feat,
    conv_input,
    conv_output,
    step_size,
    log_decay,
    skip_gain,
    norm_gain,
    out_weight,
):
    tok_rows, width_x = features.shape
    width_b = input_map.shape[1]
    head_count = step_size.shape[1]
    head_dim = width_x // head_count
    groups_here = width_b // N
    per_group = head_count // groups_here
    tail_len = conv_feat.shape[0] - 1
    n_blocks = tok_rows // BLOCK
    packed = jnp.concatenate([features, input_map, output_map], axis=1)
    kernel = jnp.concatenate([conv_feat, conv_input, conv_output], axis=1)
    pre_act = local_conv(packed, kernel, tok_rows)
    ctx_axes, ctx_count, outer_axis, inner_axis, tp_count = layout
    tail_rows = shifted(packed[tok_rows - tail_len :], ctx_axes, 1, ctx_count)
    edge_sums = edge_partial(tail_rows, kernel)
    pre_act = pre_act + jnp.pad(edge_sums, ((0, tok_rows - tail_len), (0, 0)))
    conv_out = jax.nn.silu(pre_act).astype(jnp.bfloat16)
    x_conv = conv_out[:, :width_x]
    b_conv = conv_out[:, width_x : width_x + width_b]
    c_conv = conv_out[:, width_x + width_b :]
    x_heads = x_conv.astype(jnp.float32).reshape(tok_rows, groups_here, per_group, head_dim)
    scaled = (x_heads * step_size.reshape(tok_rows, groups_here, per_group)[..., None]).astype(
        jnp.bfloat16
    )

    def blocked(value_entries):
        return value_entries.reshape((n_blocks, BLOCK) + value_entries.shape[1:])

    scaled_b = blocked(scaled)
    b_rows = blocked(b_conv.reshape(tok_rows, groups_here, N))
    c_rows = blocked(c_conv.reshape(tok_rows, groups_here, N))
    cum_log = jnp.cumsum(blocked(log_decay.reshape(tok_rows, groups_here, per_group)), axis=1)
    blk_states = jax.vmap(block_state)(scaled_b, b_rows, cum_log)
    blk_decay = jnp.exp(cum_log[:, -1])

    def fold_local(state_carry, block_in):
        decay_b, state_b = block_in
        return (decay_b[..., None, None] * state_carry + state_b, None)

    dev_state, _ = lax.scan(
        fold_local, jnp.zeros(blk_states.shape[1:], jnp.float32), (blk_decay, blk_states)
    )
    dev_decay = jnp.prod(blk_decay, axis=0)
    incoming = prefix_states(dev_decay, dev_state, ctx_axes, ctx_count)

    def advance(state_carry, block_in):
        scaled_k, b_k, c_k, cum_k, decay_k, state_k = block_in
        block_y = intra_block(scaled_k, b_k, c_k, cum_k) + inter_block(c_k, cum_k, state_carry)
        return (decay_k[..., None, None] * state_carry + state_k, block_y)

    _, ssm_y = lax.scan(
        advance, incoming, (scaled_b, b_rows, c_rows, cum_log, blk_decay, blk_states)
    )
    mixed_y = ssm_y.reshape(tok_rows, groups_here, per_group, head_dim)
    mixed_y = mixed_y + skip_gain.reshape(groups_here, per_group)[..., None] * x_heads
    gated_y = mixed_y.reshape(tok_rows, width_x) * jax.nn.silu(gate_in.astype(jnp.float32))
    grouped = gated_y.reshape(tok_rows, groups_here, width_x // groups_here)
    inv_root = lax.rsqrt(jnp.mean(grouped * grouped, axis=-1, keepdims=True) + 1e-05)
    hidden = ((grouped * inv_root).reshape(tok_rows, width_x) * norm_gain).astype(jnp.bfloat16)
    if outer_axis is None:
        partial_out = jnp.dot(
            hidden,
            lax.all_gather(out_weight, ctx_axes, axis=1, tiled=True),
            preferred_element_type=jnp.float32,
        )
        return lax.psum_scatter(partial_out, "tp", scatter_dimension=1, tiled=True).astype(
            jnp.bfloat16
        )
    outer_at = lax.axis_index(outer_axis)
    tp_at = lax.axis_index("tp")
    inner_count = ctx_count // tp_count
    inner_at = lax.axis_index(inner_axis)
    shifted_cols = jnp.stack(
        [out_weight]
        + [
            lax.ppermute(
                out_weight, inner_axis, [(s, (s + d) % inner_count) for s in range(inner_count)]
            )
            for d in range(1, inner_count)
        ]
    )
    cols_all = jnp.concatenate(
        [
            lax.dynamic_index_in_dim(
                shifted_cols, (inner_at - place + inner_count) % inner_count, 0, keepdims=False
            )
            for place in range(inner_count)
        ],
        axis=1,
    )
    cols_all, hidden = lax.optimization_barrier((cols_all, hidden))
    from_left, from_right = {}, {}
    going_right = going_left = hidden
    for step in range(1, tp_count):
        going_right = lax.ppermute(
            going_right, outer_axis, [(s, s + 1) for s in range(step - 1, tp_count - 1)]
        )
        going_left = lax.ppermute(
            going_left, outer_axis, [(s, s - 1) for s in range(1, tp_count - step + 1)]
        )
        from_left[step], from_right[step] = going_right, going_left
    arrived = [hidden] + [
        jnp.where(outer_at >= d, from_left[d], from_right[tp_count - d])
        for d in range(1, tp_count)
    ]
    by_source = jnp.stack(
        [jnp.dot(rows, cols_all, preferred_element_type=jnp.float32) for rows in arrived]
    )

    def for_target(target):
        return lax.dynamic_index_in_dim(
            by_source, (outer_at - target + tp_count) % tp_count, 0, keepdims=False
        )

    held = {m: for_target(tp_at ^ m) for m in range(tp_count)}
    bit = 1
    while bit < tp_count:
        going = sorted(m for m in held if m & bit)
        sent = jnp.stack([held[m] for m in going])
        got = lax.ppermute(
            sent if bit == 1 else sent.astype(jnp.bfloat16),
            "tp",
            [(s, s ^ bit) for s in range(tp_count)],
        )
        held = {m: held[m] for m in held if not m & bit}
        for index, m in enumerate(going):
            held[m ^ bit] = held[m ^ bit] + got[index].astype(jnp.float32)
        bit *= 2
    swap = [(o * tp_count + t, t * tp_count + o) for o in range(tp_count) for t in range(tp_count)]
    return lax.ppermute(held[0].astype(jnp.bfloat16), (outer_axis, "tp"), swap)


def solution(mesh):
    ctx_count = mesh.shape["ctx"]
    tp_count = mesh.shape["tp"]
    if ctx_count % tp_count == 0 and tp_count & (tp_count - 1) == 0:
        inner = ctx_count // tp_count
        grid = mesh.devices.reshape(tp_count, inner, tp_count)
        mesh = jax.sharding.Mesh(grid, ("outer", "inner", "tp"))
        ctx_axes = ("outer", "inner")
        layout = (ctx_axes, ctx_count, "outer", "inner", tp_count)
    else:
        ctx_axes = "ctx"
        layout = (ctx_axes, ctx_count, None, None, tp_count)
    placed = (
        P(ctx_axes, "tp"),
        P(ctx_axes, "tp"),
        P(ctx_axes, "tp"),
        P(ctx_axes, "tp"),
        P(None, "tp"),
        P(None, "tp"),
        P(None, "tp"),
        P(ctx_axes, "tp"),
        P(ctx_axes, "tp"),
        P("tp"),
        P("tp"),
        P("tp", ctx_axes),
    )
    return jax.shard_map(
        functools.partial(on_device, layout),
        mesh=mesh,
        in_specs=placed,
        out_specs=P(ctx_axes, "tp"),
        check_vma=False,
    )
```

```python
import functools

import jax
import jax.numpy as jnp
from jax import lax
from jax.sharding import PartitionSpec as P

N = 128
BLOCK = 256


def shifted(value, axis, steps, count):
    first, last = (max(0, -steps), min(count, count - steps))
    return lax.ppermute(value, axis, [(source, source + steps) for source in range(first, last)])


def local_conv(packed, kernel, tok_rows):
    tail_len = kernel.shape[0] - 1
    padded = jnp.pad(packed.astype(jnp.float32), ((tail_len, 0), (0, 0)))
    pre_act = jnp.zeros((tok_rows, kernel.shape[1]), jnp.float32)
    for tap_index in range(kernel.shape[0]):
        pre_act = pre_act + kernel[tap_index] * padded[tap_index : tap_index + tok_rows]
    return pre_act


def edge_partial(tail_rows, kernel):
    tail_len = kernel.shape[0] - 1
    tail_vals = tail_rows.astype(jnp.float32)
    outputs = []
    for row_index in range(tail_len):
        accum = jnp.zeros((kernel.shape[1],), jnp.float32)
        for tap_index in range(tail_len - row_index):
            accum = accum + kernel[tap_index] * tail_vals[row_index + tap_index]
        outputs.append(accum)
    return jnp.stack(outputs, axis=0)


def intra_block(scaled, b_rows, c_rows, cum_log):
    scores = jnp.einsum("tgn,sgn->gts", c_rows, b_rows, preferred_element_type=jnp.float32)
    cum_cols = jnp.moveaxis(cum_log, 0, -1)
    log_gap = cum_cols[..., :, None] - cum_cols[..., None, :]
    block_len = cum_log.shape[0]
    causal = jnp.arange(block_len)[:, None] >= jnp.arange(block_len)[None, :]
    decays = jnp.exp(jnp.where(causal, log_gap, -jnp.inf))
    weights = (scores[:, None] * decays).astype(jnp.bfloat16)
    return jnp.einsum("gjts,sgjp->tgjp", weights, scaled, preferred_element_type=jnp.float32)


def block_state(scaled, b_rows, cum_log):
    end_decay = jnp.exp(cum_log[-1][None] - cum_log)
    b_weighted = (b_rows.astype(jnp.float32)[:, :, None, :] * end_decay[..., None]).astype(
        jnp.bfloat16
    )
    return jnp.einsum("sgjp,sgjn->gjpn", scaled, b_weighted, preferred_element_type=jnp.float32)


def inter_block(c_rows, cum_log, state_carry):
    rounded = state_carry.astype(jnp.bfloat16)
    inner = jnp.einsum("tgn,gjpn->tgjp", c_rows, rounded, preferred_element_type=jnp.float32)
    return inner * jnp.exp(cum_log)[..., None]


def combine(first_part, second_part):
    decay_first, state_first = first_part
    decay_second, state_second = second_part
    return (
        decay_first * decay_second,
        decay_second[..., None, None] * state_first.astype(jnp.float32) + state_second,
    )


def on_link(part):
    decay, state = part
    return (decay, state.astype(jnp.bfloat16))


def prefix_states(dev_decay, dev_state, axis, count):
    own = (dev_decay, dev_state)
    if count == 1:
        return jnp.zeros_like(dev_state)
    got = shifted(on_link(own), axis, 1, count)
    before = got
    upto = combine(got, own)
    step = 2
    while step < count:
        got = shifted(on_link(upto), axis, step, count)
        before = combine(got, before)
        if step * 2 < count:
            upto = combine(got, upto)
        step *= 2
    return before[1].astype(jnp.float32)


def on_device(
    layout,
    features,
    input_map,
    output_map,
    gate_in,
    conv_feat,
    conv_input,
    conv_output,
    step_size,
    log_decay,
    skip_gain,
    norm_gain,
    out_weight,
):
    tok_rows, width_x = features.shape
    width_b = input_map.shape[1]
    head_count = step_size.shape[1]
    head_dim = width_x // head_count
    groups_here = width_b // N
    per_group = head_count // groups_here
    tail_len = conv_feat.shape[0] - 1
    n_blocks = tok_rows // BLOCK
    packed = jnp.concatenate([features, input_map, output_map], axis=1)
    kernel = jnp.concatenate([conv_feat, conv_input, conv_output], axis=1)
    pre_act = local_conv(packed, kernel, tok_rows)
    ctx_axes, ctx_count, outer_axis, inner_axis, tp_count = layout
    tail_rows = shifted(packed[tok_rows - tail_len :], ctx_axes, 1, ctx_count)
    edge_sums = edge_partial(tail_rows, kernel)
    pre_act = pre_act + jnp.pad(edge_sums, ((0, tok_rows - tail_len), (0, 0)))
    conv_out = jax.nn.silu(pre_act).astype(jnp.bfloat16)
    x_conv = conv_out[:, :width_x]
    b_conv = conv_out[:, width_x : width_x + width_b]
    c_conv = conv_out[:, width_x + width_b :]
    x_heads = x_conv.astype(jnp.float32).reshape(tok_rows, groups_here, per_group, head_dim)
    scaled = (x_heads * step_size.reshape(tok_rows, groups_here, per_group)[..., None]).astype(
        jnp.bfloat16
    )

    def blocked(value_entries):
        return value_entries.reshape((n_blocks, BLOCK) + value_entries.shape[1:])

    scaled_b = blocked(scaled)
    b_rows = blocked(b_conv.reshape(tok_rows, groups_here, N))
    c_rows = blocked(c_conv.reshape(tok_rows, groups_here, N))
    cum_log = jnp.cumsum(blocked(log_decay.reshape(tok_rows, groups_here, per_group)), axis=1)
    blk_states = jax.vmap(block_state)(scaled_b, b_rows, cum_log)
    blk_decay = jnp.exp(cum_log[:, -1])

    def fold_local(state_carry, block_in):
        decay_b, state_b = block_in
        return (decay_b[..., None, None] * state_carry + state_b, None)

    dev_state, _ = lax.scan(
        fold_local, jnp.zeros(blk_states.shape[1:], jnp.float32), (blk_decay, blk_states)
    )
    dev_decay = jnp.prod(blk_decay, axis=0)
    incoming = prefix_states(dev_decay, dev_state, ctx_axes, ctx_count)
    if outer_axis is not None:
        inner_count = ctx_count // tp_count
        weight_pieces = [out_weight] + [
            lax.ppermute(
                out_weight, inner_axis, [(s, (s + d) % inner_count) for s in range(inner_count)]
            )
            for d in range(1, inner_count)
        ]
        weight_pieces, incoming = lax.optimization_barrier((weight_pieces, incoming))

    def advance(state_carry, block_in):
        scaled_k, b_k, c_k, cum_k, decay_k, state_k = block_in
        block_y = intra_block(scaled_k, b_k, c_k, cum_k) + inter_block(c_k, cum_k, state_carry)
        return (decay_k[..., None, None] * state_carry + state_k, block_y)

    _, ssm_y = lax.scan(
        advance, incoming, (scaled_b, b_rows, c_rows, cum_log, blk_decay, blk_states)
    )
    mixed_y = ssm_y.reshape(tok_rows, groups_here, per_group, head_dim)
    mixed_y = mixed_y + skip_gain.reshape(groups_here, per_group)[..., None] * x_heads
    gated_y = mixed_y.reshape(tok_rows, width_x) * jax.nn.silu(gate_in.astype(jnp.float32))
    grouped = gated_y.reshape(tok_rows, groups_here, width_x // groups_here)
    inv_root = lax.rsqrt(jnp.mean(grouped * grouped, axis=-1, keepdims=True) + 1e-05)
    hidden = ((grouped * inv_root).reshape(tok_rows, width_x) * norm_gain).astype(jnp.bfloat16)
    if outer_axis is None:
        partial_out = jnp.dot(
            hidden,
            lax.all_gather(out_weight, ctx_axes, axis=1, tiled=True),
            preferred_element_type=jnp.float32,
        )
        return lax.psum_scatter(partial_out, "tp", scatter_dimension=1, tiled=True).astype(
            jnp.bfloat16
        )
    outer_at = lax.axis_index(outer_axis)
    tp_at = lax.axis_index("tp")
    inner_count = ctx_count // tp_count
    inner_at = lax.axis_index(inner_axis)
    from_left, from_right = {}, {}
    going_right = going_left = hidden
    for step in range(1, tp_count):
        going_right = lax.ppermute(
            going_right, outer_axis, [(s, s + 1) for s in range(step - 1, tp_count - 1)]
        )
        going_left = lax.ppermute(
            going_left, outer_axis, [(s, s - 1) for s in range(1, tp_count - step + 1)]
        )
        from_left[step], from_right[step] = going_right, going_left
    arrived = [hidden] + [
        jnp.where(outer_at >= d, from_left[d], from_right[tp_count - d])
        for d in range(1, tp_count)
    ]
    by_source = jnp.stack(
        [
            jnp.concatenate(
                [
                    jnp.dot(rows, piece, preferred_element_type=jnp.float32)
                    for piece in weight_pieces
                ],
                axis=1,
            )
            for rows in arrived
        ]
    )

    def for_target(target):
        return lax.dynamic_index_in_dim(
            by_source, (outer_at - target + tp_count) % tp_count, 0, keepdims=False
        )

    held = {m: for_target(tp_at ^ m) for m in range(tp_count)}
    bit = 1
    while bit < tp_count:
        going = sorted(m for m in held if m & bit)
        sent = jnp.stack([held[m] for m in going])
        got = lax.ppermute(
            sent if bit == 1 else sent.astype(jnp.bfloat16),
            "tp",
            [(s, s ^ bit) for s in range(tp_count)],
        )
        held = {m: held[m] for m in held if not m & bit}
        for index, m in enumerate(going):
            held[m ^ bit] = held[m ^ bit] + got[index].astype(jnp.float32)
        bit *= 2
    swap = [(o * tp_count + t, t * tp_count + o) for o in range(tp_count) for t in range(tp_count)]
    rotated = lax.ppermute(held[0].astype(jnp.bfloat16), (outer_axis, "tp"), swap)
    width = out_weight.shape[1]
    pieces = jnp.stack([rotated[:, d * width : (d + 1) * width] for d in range(inner_count)])
    inner_at = lax.axis_index(inner_axis)
    return jnp.concatenate(
        [
            lax.dynamic_index_in_dim(
                pieces, (inner_at - place + inner_count) % inner_count, 0, keepdims=False
            )
            for place in range(inner_count)
        ],
        axis=1,
    )


def solution(mesh):
    ctx_count = mesh.shape["ctx"]
    tp_count = mesh.shape["tp"]
    if ctx_count % tp_count == 0 and tp_count & (tp_count - 1) == 0:
        inner = ctx_count // tp_count
        grid = mesh.devices.reshape(tp_count, inner, tp_count)
        mesh = jax.sharding.Mesh(grid, ("outer", "inner", "tp"))
        ctx_axes = ("outer", "inner")
        layout = (ctx_axes, ctx_count, "outer", "inner", tp_count)
    else:
        ctx_axes = "ctx"
        layout = (ctx_axes, ctx_count, None, None, tp_count)
    placed = (
        P(ctx_axes, "tp"),
        P(ctx_axes, "tp"),
        P(ctx_axes, "tp"),
        P(ctx_axes, "tp"),
        P(None, "tp"),
        P(None, "tp"),
        P(None, "tp"),
        P(ctx_axes, "tp"),
        P(ctx_axes, "tp"),
        P("tp"),
        P("tp"),
        P("tp", ctx_axes),
    )
    return jax.shard_map(
        functools.partial(on_device, layout),
        mesh=mesh,
        in_specs=placed,
        out_specs=P(ctx_axes, "tp"),
        check_vma=False,
    )
```

```python
import functools

import jax
import jax.numpy as jnp
from jax import lax
from jax.sharding import PartitionSpec as P

N = 128
BLOCK = 256


def shifted(value, axis, steps, count):
    first, last = (max(0, -steps), min(count, count - steps))
    return lax.ppermute(value, axis, [(source, source + steps) for source in range(first, last)])


def local_conv(packed, kernel, tok_rows):
    tail_len = kernel.shape[0] - 1
    padded = jnp.pad(packed.astype(jnp.float32), ((tail_len, 0), (0, 0)))
    pre_act = jnp.zeros((tok_rows, kernel.shape[1]), jnp.float32)
    for tap_index in range(kernel.shape[0]):
        pre_act = pre_act + kernel[tap_index] * padded[tap_index : tap_index + tok_rows]
    return pre_act


def edge_partial(tail_rows, kernel):
    tail_len = kernel.shape[0] - 1
    tail_vals = tail_rows.astype(jnp.float32)
    outputs = []
    for row_index in range(tail_len):
        accum = jnp.zeros((kernel.shape[1],), jnp.float32)
        for tap_index in range(tail_len - row_index):
            accum = accum + kernel[tap_index] * tail_vals[row_index + tap_index]
        outputs.append(accum)
    return jnp.stack(outputs, axis=0)


def intra_block(scaled, b_rows, c_rows, cum_log):
    scores = jnp.einsum("tgn,sgn->gts", c_rows, b_rows, preferred_element_type=jnp.float32)
    cum_cols = jnp.moveaxis(cum_log, 0, -1)
    log_gap = cum_cols[..., :, None] - cum_cols[..., None, :]
    block_len = cum_log.shape[0]
    causal = jnp.arange(block_len)[:, None] >= jnp.arange(block_len)[None, :]
    decays = jnp.exp(jnp.where(causal, log_gap, -jnp.inf))
    weights = (scores[:, None] * decays).astype(jnp.bfloat16)
    return jnp.einsum("gjts,sgjp->tgjp", weights, scaled, preferred_element_type=jnp.float32)


def block_state(scaled, b_rows, cum_log):
    end_decay = jnp.exp(cum_log[-1][None] - cum_log)
    b_weighted = (b_rows.astype(jnp.float32)[:, :, None, :] * end_decay[..., None]).astype(
        jnp.bfloat16
    )
    return jnp.einsum("sgjp,sgjn->gjpn", scaled, b_weighted, preferred_element_type=jnp.float32)


def inter_block(c_rows, cum_log, state_carry):
    rounded = state_carry.astype(jnp.bfloat16)
    inner = jnp.einsum("tgn,gjpn->tgjp", c_rows, rounded, preferred_element_type=jnp.float32)
    return inner * jnp.exp(cum_log)[..., None]


def combine(first_part, second_part):
    decay_first, state_first = first_part
    decay_second, state_second = second_part
    return (
        decay_first * decay_second,
        decay_second[..., None, None] * state_first.astype(jnp.float32) + state_second,
    )


def on_link(part):
    decay, state = part
    return (decay, state.astype(jnp.bfloat16))


def prefix_states(dev_decay, dev_state, axis, count):
    own = (dev_decay, dev_state)
    if count == 1:
        return jnp.zeros_like(dev_state)
    got = shifted(on_link(own), axis, 1, count)
    before = got
    upto = combine(got, own)
    step = 2
    while step < count:
        got = shifted(on_link(upto), axis, step, count)
        before = combine(got, before)
        if step * 2 < count:
            upto = combine(got, upto)
        step *= 2
    return before[1].astype(jnp.float32)


def on_device(
    layout,
    features,
    input_map,
    output_map,
    gate_in,
    conv_feat,
    conv_input,
    conv_output,
    step_size,
    log_decay,
    skip_gain,
    norm_gain,
    out_weight,
):
    tok_rows, width_x = features.shape
    width_b = input_map.shape[1]
    head_count = step_size.shape[1]
    head_dim = width_x // head_count
    groups_here = width_b // N
    per_group = head_count // groups_here
    tail_len = conv_feat.shape[0] - 1
    n_blocks = tok_rows // BLOCK
    packed = jnp.concatenate([features, input_map, output_map], axis=1)
    kernel = jnp.concatenate([conv_feat, conv_input, conv_output], axis=1)
    pre_act = local_conv(packed, kernel, tok_rows)
    ctx_axes, ctx_count, outer_axis, inner_axis, tp_count = layout
    tail_rows = shifted(packed[tok_rows - tail_len :], ctx_axes, 1, ctx_count)
    edge_sums = edge_partial(tail_rows, kernel)
    pre_act = pre_act + jnp.pad(edge_sums, ((0, tok_rows - tail_len), (0, 0)))
    conv_out = jax.nn.silu(pre_act).astype(jnp.bfloat16)
    x_conv = conv_out[:, :width_x]
    b_conv = conv_out[:, width_x : width_x + width_b]
    c_conv = conv_out[:, width_x + width_b :]
    x_heads = x_conv.astype(jnp.float32).reshape(tok_rows, groups_here, per_group, head_dim)
    scaled = (x_heads * step_size.reshape(tok_rows, groups_here, per_group)[..., None]).astype(
        jnp.bfloat16
    )

    def blocked(value_entries):
        return value_entries.reshape((n_blocks, BLOCK) + value_entries.shape[1:])

    scaled_b = blocked(scaled)
    b_rows = blocked(b_conv.reshape(tok_rows, groups_here, N))
    c_rows = blocked(c_conv.reshape(tok_rows, groups_here, N))
    cum_log = jnp.cumsum(blocked(log_decay.reshape(tok_rows, groups_here, per_group)), axis=1)
    blk_states = jax.vmap(block_state)(scaled_b, b_rows, cum_log)
    blk_decay = jnp.exp(cum_log[:, -1])

    def fold_local(state_carry, block_in):
        decay_b, state_b = block_in
        return (decay_b[..., None, None] * state_carry + state_b, None)

    dev_state, _ = lax.scan(
        fold_local, jnp.zeros(blk_states.shape[1:], jnp.float32), (blk_decay, blk_states)
    )
    dev_decay = jnp.prod(blk_decay, axis=0)
    incoming = prefix_states(dev_decay, dev_state, ctx_axes, ctx_count)

    def advance(state_carry, block_in):
        scaled_k, b_k, c_k, cum_k, decay_k, state_k = block_in
        block_y = intra_block(scaled_k, b_k, c_k, cum_k) + inter_block(c_k, cum_k, state_carry)
        return (decay_k[..., None, None] * state_carry + state_k, block_y)

    _, ssm_y = lax.scan(
        advance, incoming, (scaled_b, b_rows, c_rows, cum_log, blk_decay, blk_states)
    )
    mixed_y = ssm_y.reshape(tok_rows, groups_here, per_group, head_dim)
    mixed_y = mixed_y + skip_gain.reshape(groups_here, per_group)[..., None] * x_heads
    gated_y = mixed_y.reshape(tok_rows, width_x) * jax.nn.silu(gate_in.astype(jnp.float32))
    grouped = gated_y.reshape(tok_rows, groups_here, width_x // groups_here)
    inv_root = lax.rsqrt(jnp.mean(grouped * grouped, axis=-1, keepdims=True) + 1e-05)
    hidden = ((grouped * inv_root).reshape(tok_rows, width_x) * norm_gain).astype(jnp.bfloat16)
    if outer_axis is None:
        partial_out = jnp.dot(
            hidden,
            lax.all_gather(out_weight, ctx_axes, axis=1, tiled=True),
            preferred_element_type=jnp.float32,
        )
        return lax.psum_scatter(partial_out, "tp", scatter_dimension=1, tiled=True).astype(
            jnp.bfloat16
        )
    outer_at = lax.axis_index(outer_axis)
    tp_at = lax.axis_index("tp")
    inner_count = ctx_count // tp_count
    weight_pieces = [out_weight] + [
        lax.ppermute(
            out_weight, inner_axis, [(s, (s + d) % inner_count) for s in range(inner_count)]
        )
        for d in range(1, inner_count)
    ]
    weight_pieces, hidden = lax.optimization_barrier((weight_pieces, hidden))
    from_left, from_right = {}, {}
    going_right = going_left = hidden
    for step in range(1, tp_count):
        going_right = lax.ppermute(
            going_right, outer_axis, [(s, s + 1) for s in range(step - 1, tp_count - 1)]
        )
        going_left = lax.ppermute(
            going_left, outer_axis, [(s, s - 1) for s in range(1, tp_count - step + 1)]
        )
        from_left[step], from_right[step] = going_right, going_left
    arrived = [hidden] + [
        jnp.where(outer_at >= d, from_left[d], from_right[tp_count - d])
        for d in range(1, tp_count)
    ]
    by_source = jnp.stack(
        [
            jnp.concatenate(
                [
                    jnp.dot(rows, piece, preferred_element_type=jnp.float32)
                    for piece in weight_pieces
                ],
                axis=1,
            )
            for rows in arrived
        ]
    )

    def for_target(target):
        return lax.dynamic_index_in_dim(
            by_source, (outer_at - target + tp_count) % tp_count, 0, keepdims=False
        )

    held = {m: for_target(tp_at ^ m) for m in range(tp_count)}
    bit = 1
    while bit < tp_count:
        going = sorted(m for m in held if m & bit)
        sent = jnp.stack([held[m] for m in going])
        got = lax.ppermute(
            sent if bit == 1 else sent.astype(jnp.bfloat16),
            "tp",
            [(s, s ^ bit) for s in range(tp_count)],
        )
        held = {m: held[m] for m in held if not m & bit}
        for index, m in enumerate(going):
            held[m ^ bit] = held[m ^ bit] + got[index].astype(jnp.float32)
        bit *= 2
    swap = [(o * tp_count + t, t * tp_count + o) for o in range(tp_count) for t in range(tp_count)]
    rotated = lax.ppermute(held[0].astype(jnp.bfloat16), (outer_axis, "tp"), swap)
    width = out_weight.shape[1]
    pieces = jnp.stack([rotated[:, d * width : (d + 1) * width] for d in range(inner_count)])
    inner_at = lax.axis_index(inner_axis)
    return jnp.concatenate(
        [
            lax.dynamic_index_in_dim(
                pieces, (inner_at - place + inner_count) % inner_count, 0, keepdims=False
            )
            for place in range(inner_count)
        ],
        axis=1,
    )


def solution(mesh):
    ctx_count = mesh.shape["ctx"]
    tp_count = mesh.shape["tp"]
    if ctx_count % tp_count == 0 and tp_count & (tp_count - 1) == 0:
        inner = ctx_count // tp_count
        grid = mesh.devices.reshape(tp_count, inner, tp_count)
        mesh = jax.sharding.Mesh(grid, ("outer", "inner", "tp"))
        ctx_axes = ("outer", "inner")
        layout = (ctx_axes, ctx_count, "outer", "inner", tp_count)
    else:
        ctx_axes = "ctx"
        layout = (ctx_axes, ctx_count, None, None, tp_count)
    placed = (
        P(ctx_axes, "tp"),
        P(ctx_axes, "tp"),
        P(ctx_axes, "tp"),
        P(ctx_axes, "tp"),
        P(None, "tp"),
        P(None, "tp"),
        P(None, "tp"),
        P(ctx_axes, "tp"),
        P(ctx_axes, "tp"),
        P("tp"),
        P("tp"),
        P("tp", ctx_axes),
    )
    return jax.shard_map(
        functools.partial(on_device, layout),
        mesh=mesh,
        in_specs=placed,
        out_specs=P(ctx_axes, "tp"),
        check_vma=False,
    )
```

```python
import functools

import jax
import jax.numpy as jnp
from jax import lax
from jax.sharding import PartitionSpec as P

N = 128
BLOCK = 256


def shifted(value, axis, steps, count):
    first, last = (max(0, -steps), min(count, count - steps))
    return lax.ppermute(value, axis, [(source, source + steps) for source in range(first, last)])


def local_conv(packed, kernel, tok_rows):
    tail_len = kernel.shape[0] - 1
    padded = jnp.pad(packed.astype(jnp.float32), ((tail_len, 0), (0, 0)))
    pre_act = jnp.zeros((tok_rows, kernel.shape[1]), jnp.float32)
    for tap_index in range(kernel.shape[0]):
        pre_act = pre_act + kernel[tap_index] * padded[tap_index : tap_index + tok_rows]
    return pre_act


def edge_partial(tail_rows, kernel):
    tail_len = kernel.shape[0] - 1
    tail_vals = tail_rows.astype(jnp.float32)
    outputs = []
    for row_index in range(tail_len):
        accum = jnp.zeros((kernel.shape[1],), jnp.float32)
        for tap_index in range(tail_len - row_index):
            accum = accum + kernel[tap_index] * tail_vals[row_index + tap_index]
        outputs.append(accum)
    return jnp.stack(outputs, axis=0)


def intra_block(scaled, b_rows, c_rows, cum_log):
    scores = jnp.einsum("tgn,sgn->gts", c_rows, b_rows, preferred_element_type=jnp.float32)
    cum_cols = jnp.moveaxis(cum_log, 0, -1)
    log_gap = cum_cols[..., :, None] - cum_cols[..., None, :]
    block_len = cum_log.shape[0]
    causal = jnp.arange(block_len)[:, None] >= jnp.arange(block_len)[None, :]
    decays = jnp.exp(jnp.where(causal, log_gap, -jnp.inf))
    weights = (scores[:, None] * decays).astype(jnp.bfloat16)
    return jnp.einsum("gjts,sgjp->tgjp", weights, scaled, preferred_element_type=jnp.float32)


def block_state(scaled, b_rows, cum_log):
    end_decay = jnp.exp(cum_log[-1][None] - cum_log)
    b_weighted = (b_rows.astype(jnp.float32)[:, :, None, :] * end_decay[..., None]).astype(
        jnp.bfloat16
    )
    return jnp.einsum("sgjp,sgjn->gjpn", scaled, b_weighted, preferred_element_type=jnp.float32)


def inter_block(c_rows, cum_log, state_carry):
    rounded = state_carry.astype(jnp.bfloat16)
    inner = jnp.einsum("tgn,gjpn->tgjp", c_rows, rounded, preferred_element_type=jnp.float32)
    return inner * jnp.exp(cum_log)[..., None]


def combine(first_part, second_part):
    decay_first, state_first = first_part
    decay_second, state_second = second_part
    return (
        decay_first * decay_second,
        decay_second[..., None, None] * state_first.astype(jnp.float32) + state_second,
    )


def on_link(part):
    decay, state = part
    return (decay, state.astype(jnp.bfloat16))


def prefix_states(dev_decay, dev_state, axis, count):
    own = (dev_decay, dev_state)
    if count == 1:
        return jnp.zeros_like(dev_state)
    got = shifted(on_link(own), axis, 1, count)
    before = got
    upto = combine(got, own)
    step = 2
    while step < count:
        got = shifted(on_link(upto), axis, step, count)
        before = combine(got, before)
        if step * 2 < count:
            upto = combine(got, upto)
        step *= 2
    return before[1].astype(jnp.float32)


def on_device(
    layout,
    features,
    input_map,
    output_map,
    gate_in,
    conv_feat,
    conv_input,
    conv_output,
    step_size,
    log_decay,
    skip_gain,
    norm_gain,
    out_weight,
):
    tok_rows, width_x = features.shape
    width_b = input_map.shape[1]
    head_count = step_size.shape[1]
    head_dim = width_x // head_count
    groups_here = width_b // N
    per_group = head_count // groups_here
    tail_len = conv_feat.shape[0] - 1
    n_blocks = tok_rows // BLOCK
    packed = jnp.concatenate([features, input_map, output_map], axis=1)
    kernel = jnp.concatenate([conv_feat, conv_input, conv_output], axis=1)
    pre_act = local_conv(packed, kernel, tok_rows)
    ctx_axes, ctx_count, outer_axis, inner_axis, tp_count = layout
    tail_rows = shifted(packed[tok_rows - tail_len :], ctx_axes, 1, ctx_count)
    edge_sums = edge_partial(tail_rows, kernel)
    pre_act = pre_act + jnp.pad(edge_sums, ((0, tok_rows - tail_len), (0, 0)))
    conv_out = jax.nn.silu(pre_act).astype(jnp.bfloat16)
    x_conv = conv_out[:, :width_x]
    b_conv = conv_out[:, width_x : width_x + width_b]
    c_conv = conv_out[:, width_x + width_b :]
    x_heads = x_conv.astype(jnp.float32).reshape(tok_rows, groups_here, per_group, head_dim)
    scaled = (x_heads * step_size.reshape(tok_rows, groups_here, per_group)[..., None]).astype(
        jnp.bfloat16
    )

    def blocked(value_entries):
        return value_entries.reshape((n_blocks, BLOCK) + value_entries.shape[1:])

    scaled_b = blocked(scaled)
    b_rows = blocked(b_conv.reshape(tok_rows, groups_here, N))
    c_rows = blocked(c_conv.reshape(tok_rows, groups_here, N))
    cum_log = jnp.cumsum(blocked(log_decay.reshape(tok_rows, groups_here, per_group)), axis=1)
    blk_states = jax.vmap(block_state)(scaled_b, b_rows, cum_log)
    blk_decay = jnp.exp(cum_log[:, -1])

    def fold_local(state_carry, block_in):
        decay_b, state_b = block_in
        return (decay_b[..., None, None] * state_carry + state_b, None)

    dev_state, _ = lax.scan(
        fold_local, jnp.zeros(blk_states.shape[1:], jnp.float32), (blk_decay, blk_states)
    )
    dev_decay = jnp.prod(blk_decay, axis=0)
    incoming = prefix_states(dev_decay, dev_state, ctx_axes, ctx_count)

    def advance(state_carry, block_in):
        scaled_k, b_k, c_k, cum_k, decay_k, state_k = block_in
        block_y = intra_block(scaled_k, b_k, c_k, cum_k) + inter_block(c_k, cum_k, state_carry)
        return (decay_k[..., None, None] * state_carry + state_k, block_y)

    _, ssm_y = lax.scan(
        advance, incoming, (scaled_b, b_rows, c_rows, cum_log, blk_decay, blk_states)
    )
    mixed_y = ssm_y.reshape(tok_rows, groups_here, per_group, head_dim)
    mixed_y = mixed_y + skip_gain.reshape(groups_here, per_group)[..., None] * x_heads
    gated_y = mixed_y.reshape(tok_rows, width_x) * jax.nn.silu(gate_in.astype(jnp.float32))
    grouped = gated_y.reshape(tok_rows, groups_here, width_x // groups_here)
    inv_root = lax.rsqrt(jnp.mean(grouped * grouped, axis=-1, keepdims=True) + 1e-05)
    hidden = ((grouped * inv_root).reshape(tok_rows, width_x) * norm_gain).astype(jnp.bfloat16)
    if outer_axis is None:
        partial_out = jnp.dot(
            hidden,
            lax.all_gather(out_weight, ctx_axes, axis=1, tiled=True),
            preferred_element_type=jnp.float32,
        )
        return lax.psum_scatter(partial_out, "tp", scatter_dimension=1, tiled=True).astype(
            jnp.bfloat16
        )
    outer_at = lax.axis_index(outer_axis)
    tp_at = lax.axis_index("tp")
    inner_count = ctx_count // tp_count
    weight_pieces = [out_weight] + [
        lax.ppermute(
            out_weight, inner_axis, [(s, (s + d) % inner_count) for s in range(inner_count)]
        )
        for d in range(1, inner_count)
    ]
    from_left, from_right = {}, {}
    going_right = going_left = hidden
    for step in range(1, tp_count):
        going_right = lax.ppermute(
            going_right, outer_axis, [(s, s + 1) for s in range(step - 1, tp_count - 1)]
        )
        going_left = lax.ppermute(
            going_left, outer_axis, [(s, s - 1) for s in range(1, tp_count - step + 1)]
        )
        if step == 1:
            weight_pieces, going_right, going_left = lax.optimization_barrier(
                (weight_pieces, going_right, going_left)
            )
        from_left[step], from_right[step] = going_right, going_left
    arrived = [hidden] + [
        jnp.where(outer_at >= d, from_left[d], from_right[tp_count - d])
        for d in range(1, tp_count)
    ]
    by_source = jnp.stack(
        [
            jnp.concatenate(
                [
                    jnp.dot(rows, piece, preferred_element_type=jnp.float32)
                    for piece in weight_pieces
                ],
                axis=1,
            )
            for rows in arrived
        ]
    )

    def for_target(target):
        return lax.dynamic_index_in_dim(
            by_source, (outer_at - target + tp_count) % tp_count, 0, keepdims=False
        )

    held = {m: for_target(tp_at ^ m) for m in range(tp_count)}
    bit = 1
    while bit < tp_count:
        going = sorted(m for m in held if m & bit)
        sent = jnp.stack([held[m] for m in going])
        got = lax.ppermute(
            sent if bit == 1 else sent.astype(jnp.bfloat16),
            "tp",
            [(s, s ^ bit) for s in range(tp_count)],
        )
        held = {m: held[m] for m in held if not m & bit}
        for index, m in enumerate(going):
            held[m ^ bit] = held[m ^ bit] + got[index].astype(jnp.float32)
        bit *= 2
    swap = [(o * tp_count + t, t * tp_count + o) for o in range(tp_count) for t in range(tp_count)]
    rotated = lax.ppermute(held[0].astype(jnp.bfloat16), (outer_axis, "tp"), swap)
    width = out_weight.shape[1]
    pieces = jnp.stack([rotated[:, d * width : (d + 1) * width] for d in range(inner_count)])
    inner_at = lax.axis_index(inner_axis)
    return jnp.concatenate(
        [
            lax.dynamic_index_in_dim(
                pieces, (inner_at - place + inner_count) % inner_count, 0, keepdims=False
            )
            for place in range(inner_count)
        ],
        axis=1,
    )


def solution(mesh):
    ctx_count = mesh.shape["ctx"]
    tp_count = mesh.shape["tp"]
    if ctx_count % tp_count == 0 and tp_count & (tp_count - 1) == 0:
        inner = ctx_count // tp_count
        grid = mesh.devices.reshape(tp_count, inner, tp_count)
        mesh = jax.sharding.Mesh(grid, ("outer", "inner", "tp"))
        ctx_axes = ("outer", "inner")
        layout = (ctx_axes, ctx_count, "outer", "inner", tp_count)
    else:
        ctx_axes = "ctx"
        layout = (ctx_axes, ctx_count, None, None, tp_count)
    placed = (
        P(ctx_axes, "tp"),
        P(ctx_axes, "tp"),
        P(ctx_axes, "tp"),
        P(ctx_axes, "tp"),
        P(None, "tp"),
        P(None, "tp"),
        P(None, "tp"),
        P(ctx_axes, "tp"),
        P(ctx_axes, "tp"),
        P("tp"),
        P("tp"),
        P("tp", ctx_axes),
    )
    return jax.shard_map(
        functools.partial(on_device, layout),
        mesh=mesh,
        in_specs=placed,
        out_specs=P(ctx_axes, "tp"),
        check_vma=False,
    )
```

```python
import functools

import jax
import jax.numpy as jnp
from jax import lax
from jax.sharding import PartitionSpec as P

N = 128
BLOCK = 256


def shifted(value, axis, steps, count):
    first, last = (max(0, -steps), min(count, count - steps))
    return lax.ppermute(value, axis, [(source, source + steps) for source in range(first, last)])


def local_conv(packed, kernel, tok_rows):
    tail_len = kernel.shape[0] - 1
    padded = jnp.pad(packed.astype(jnp.float32), ((tail_len, 0), (0, 0)))
    pre_act = jnp.zeros((tok_rows, kernel.shape[1]), jnp.float32)
    for tap_index in range(kernel.shape[0]):
        pre_act = pre_act + kernel[tap_index] * padded[tap_index : tap_index + tok_rows]
    return pre_act


def edge_partial(tail_rows, kernel):
    tail_len = kernel.shape[0] - 1
    tail_vals = tail_rows.astype(jnp.float32)
    outputs = []
    for row_index in range(tail_len):
        accum = jnp.zeros((kernel.shape[1],), jnp.float32)
        for tap_index in range(tail_len - row_index):
            accum = accum + kernel[tap_index] * tail_vals[row_index + tap_index]
        outputs.append(accum)
    return jnp.stack(outputs, axis=0)


def intra_block(scaled, b_rows, c_rows, cum_log):
    scores = jnp.einsum("tgn,sgn->gts", c_rows, b_rows, preferred_element_type=jnp.float32)
    cum_cols = jnp.moveaxis(cum_log, 0, -1)
    log_gap = cum_cols[..., :, None] - cum_cols[..., None, :]
    block_len = cum_log.shape[0]
    causal = jnp.arange(block_len)[:, None] >= jnp.arange(block_len)[None, :]
    decays = jnp.exp(jnp.where(causal, log_gap, -jnp.inf))
    weights = (scores[:, None] * decays).astype(jnp.bfloat16)
    return jnp.einsum("gjts,sgjp->tgjp", weights, scaled, preferred_element_type=jnp.float32)


def block_state(scaled, b_rows, cum_log):
    end_decay = jnp.exp(cum_log[-1][None] - cum_log)
    b_weighted = (b_rows.astype(jnp.float32)[:, :, None, :] * end_decay[..., None]).astype(
        jnp.bfloat16
    )
    return jnp.einsum("sgjp,sgjn->gjpn", scaled, b_weighted, preferred_element_type=jnp.float32)


def inter_block(c_rows, cum_log, state_carry):
    rounded = state_carry.astype(jnp.bfloat16)
    inner = jnp.einsum("tgn,gjpn->tgjp", c_rows, rounded, preferred_element_type=jnp.float32)
    return inner * jnp.exp(cum_log)[..., None]


def combine(first_part, second_part):
    decay_first, state_first = first_part
    decay_second, state_second = second_part
    return (
        decay_first * decay_second,
        decay_second[..., None, None] * state_first.astype(jnp.float32) + state_second,
    )


def on_link(part):
    decay, state = part
    return (decay, state.astype(jnp.bfloat16))


def prefix_states(dev_decay, dev_state, axis, count):
    own = (dev_decay, dev_state)
    if count == 1:
        return jnp.zeros_like(dev_state)
    got = shifted(on_link(own), axis, 1, count)
    before = got
    upto = combine(got, own)
    step = 2
    while step < count:
        got = shifted(on_link(upto), axis, step, count)
        before = combine(got, before)
        if step * 2 < count:
            upto = combine(got, upto)
        step *= 2
    return before[1].astype(jnp.float32)


def on_device(
    layout,
    features,
    input_map,
    output_map,
    gate_in,
    conv_feat,
    conv_input,
    conv_output,
    step_size,
    log_decay,
    skip_gain,
    norm_gain,
    out_weight,
):
    tok_rows, width_x = features.shape
    width_b = input_map.shape[1]
    head_count = step_size.shape[1]
    head_dim = width_x // head_count
    groups_here = width_b // N
    per_group = head_count // groups_here
    tail_len = conv_feat.shape[0] - 1
    n_blocks = tok_rows // BLOCK
    packed = jnp.concatenate([features, input_map, output_map], axis=1)
    kernel = jnp.concatenate([conv_feat, conv_input, conv_output], axis=1)
    pre_act = local_conv(packed, kernel, tok_rows)
    ctx_axes, ctx_count, outer_axis, inner_axis, tp_count = layout
    tail_rows = shifted(packed[tok_rows - tail_len :], ctx_axes, 1, ctx_count)
    edge_sums = edge_partial(tail_rows, kernel)
    pre_act = pre_act + jnp.pad(edge_sums, ((0, tok_rows - tail_len), (0, 0)))
    conv_out = jax.nn.silu(pre_act).astype(jnp.bfloat16)
    x_conv = conv_out[:, :width_x]
    b_conv = conv_out[:, width_x : width_x + width_b]
    c_conv = conv_out[:, width_x + width_b :]
    x_heads = x_conv.astype(jnp.float32).reshape(tok_rows, groups_here, per_group, head_dim)
    scaled = (x_heads * step_size.reshape(tok_rows, groups_here, per_group)[..., None]).astype(
        jnp.bfloat16
    )

    def blocked(value_entries):
        return value_entries.reshape((n_blocks, BLOCK) + value_entries.shape[1:])

    scaled_b = blocked(scaled)
    b_rows = blocked(b_conv.reshape(tok_rows, groups_here, N))
    c_rows = blocked(c_conv.reshape(tok_rows, groups_here, N))
    cum_log = jnp.cumsum(blocked(log_decay.reshape(tok_rows, groups_here, per_group)), axis=1)
    blk_states = jax.vmap(block_state)(scaled_b, b_rows, cum_log)
    blk_decay = jnp.exp(cum_log[:, -1])

    def fold_local(state_carry, block_in):
        decay_b, state_b = block_in
        return (decay_b[..., None, None] * state_carry + state_b, None)

    dev_state, _ = lax.scan(
        fold_local, jnp.zeros(blk_states.shape[1:], jnp.float32), (blk_decay, blk_states)
    )
    dev_decay = jnp.prod(blk_decay, axis=0)
    incoming = prefix_states(dev_decay, dev_state, ctx_axes, ctx_count)

    def advance(state_carry, block_in):
        scaled_k, b_k, c_k, cum_k, decay_k, state_k = block_in
        block_y = intra_block(scaled_k, b_k, c_k, cum_k) + inter_block(c_k, cum_k, state_carry)
        return (decay_k[..., None, None] * state_carry + state_k, block_y)

    _, ssm_y = lax.scan(
        advance, incoming, (scaled_b, b_rows, c_rows, cum_log, blk_decay, blk_states)
    )
    mixed_y = ssm_y.reshape(tok_rows, groups_here, per_group, head_dim)
    mixed_y = mixed_y + skip_gain.reshape(groups_here, per_group)[..., None] * x_heads
    gated_y = mixed_y.reshape(tok_rows, width_x) * jax.nn.silu(gate_in.astype(jnp.float32))
    grouped = gated_y.reshape(tok_rows, groups_here, width_x // groups_here)
    inv_root = lax.rsqrt(jnp.mean(grouped * grouped, axis=-1, keepdims=True) + 1e-05)
    hidden = ((grouped * inv_root).reshape(tok_rows, width_x) * norm_gain).astype(jnp.bfloat16)
    if outer_axis is None:
        partial_out = jnp.dot(
            hidden,
            lax.all_gather(out_weight, ctx_axes, axis=1, tiled=True),
            preferred_element_type=jnp.float32,
        )
        return lax.psum_scatter(partial_out, "tp", scatter_dimension=1, tiled=True).astype(
            jnp.bfloat16
        )
    outer_at = lax.axis_index(outer_axis)
    tp_at = lax.axis_index("tp")
    inner_count = ctx_count // tp_count
    weight_pieces = [out_weight] + [
        lax.ppermute(
            out_weight, inner_axis, [(s, (s + d) % inner_count) for s in range(inner_count)]
        )
        for d in range(1, inner_count)
    ]
    weight_pieces, hidden = lax.optimization_barrier((weight_pieces, hidden))
    def times_weight(rows):
        return jnp.concatenate(
            [jnp.dot(rows, piece, preferred_element_type=jnp.float32) for piece in weight_pieces],
            axis=1,
        )

    from_left, from_right = {}, {}
    going_right = going_left = hidden
    for step in range(1, tp_count - 1):
        going_right = lax.ppermute(
            going_right, outer_axis, [(s, s + 1) for s in range(step - 1, tp_count - 1)]
        )
        going_left = lax.ppermute(
            going_left, outer_axis, [(s, s - 1) for s in range(1, tp_count - step + 1)]
        )
        from_left[step], from_right[step] = going_right, going_left
    far = lax.ppermute(
        jnp.where(outer_at == tp_count - 2, going_right, going_left),
        outer_axis,
        [(tp_count - 2, tp_count - 1), (1, 0)],
    )
    far_part = times_weight(far)
    by_source = jnp.stack(
        [times_weight(hidden)]
        + [
            jnp.where(
                outer_at >= d,
                times_weight(from_left[d]) if d < tp_count - 1 else far_part,
                times_weight(from_right[tp_count - d]) if d > 1 else far_part,
            )
            if d != tp_count // 2
            else times_weight(jnp.where(outer_at >= d, from_left[d], from_right[d]))
            for d in range(1, tp_count)
        ]
    )

    def for_target(target):
        return lax.dynamic_index_in_dim(
            by_source, (outer_at - target + tp_count) % tp_count, 0, keepdims=False
        )

    held = {m: for_target(tp_at ^ m) for m in range(tp_count)}
    bit = 1
    while bit < tp_count:
        going = sorted(m for m in held if m & bit)
        sent = jnp.stack([held[m] for m in going])
        got = lax.ppermute(
            sent if bit == 1 else sent.astype(jnp.bfloat16),
            "tp",
            [(s, s ^ bit) for s in range(tp_count)],
        )
        held = {m: held[m] for m in held if not m & bit}
        for index, m in enumerate(going):
            held[m ^ bit] = held[m ^ bit] + got[index].astype(jnp.float32)
        bit *= 2
    swap = [(o * tp_count + t, t * tp_count + o) for o in range(tp_count) for t in range(tp_count)]
    rotated = lax.ppermute(held[0].astype(jnp.bfloat16), (outer_axis, "tp"), swap)
    width = out_weight.shape[1]
    pieces = jnp.stack([rotated[:, d * width : (d + 1) * width] for d in range(inner_count)])
    inner_at = lax.axis_index(inner_axis)
    return jnp.concatenate(
        [
            lax.dynamic_index_in_dim(
                pieces, (inner_at - place + inner_count) % inner_count, 0, keepdims=False
            )
            for place in range(inner_count)
        ],
        axis=1,
    )


def solution(mesh):
    ctx_count = mesh.shape["ctx"]
    tp_count = mesh.shape["tp"]
    if ctx_count % tp_count == 0 and tp_count == 4:
        inner = ctx_count // tp_count
        grid = mesh.devices.reshape(tp_count, inner, tp_count)
        mesh = jax.sharding.Mesh(grid, ("outer", "inner", "tp"))
        ctx_axes = ("outer", "inner")
        layout = (ctx_axes, ctx_count, "outer", "inner", tp_count)
    else:
        ctx_axes = "ctx"
        layout = (ctx_axes, ctx_count, None, None, tp_count)
    placed = (
        P(ctx_axes, "tp"),
        P(ctx_axes, "tp"),
        P(ctx_axes, "tp"),
        P(ctx_axes, "tp"),
        P(None, "tp"),
        P(None, "tp"),
        P(None, "tp"),
        P(ctx_axes, "tp"),
        P(ctx_axes, "tp"),
        P("tp"),
        P("tp"),
        P("tp", ctx_axes),
    )
    return jax.shard_map(
        functools.partial(on_device, layout),
        mesh=mesh,
        in_specs=placed,
        out_specs=P(ctx_axes, "tp"),
        check_vma=False,
    )
```

```python
import functools

import jax
import jax.numpy as jnp
from jax import lax
from jax.sharding import PartitionSpec as P

N = 128
BLOCK = 256


def shifted(value, axis, steps, count):
    first, last = (max(0, -steps), min(count, count - steps))
    return lax.ppermute(value, axis, [(source, source + steps) for source in range(first, last)])


def local_conv(packed, kernel, tok_rows):
    tail_len = kernel.shape[0] - 1
    padded = jnp.pad(packed.astype(jnp.float32), ((tail_len, 0), (0, 0)))
    pre_act = jnp.zeros((tok_rows, kernel.shape[1]), jnp.float32)
    for tap_index in range(kernel.shape[0]):
        pre_act = pre_act + kernel[tap_index] * padded[tap_index : tap_index + tok_rows]
    return pre_act


def edge_partial(tail_rows, kernel):
    tail_len = kernel.shape[0] - 1
    tail_vals = tail_rows.astype(jnp.float32)
    outputs = []
    for row_index in range(tail_len):
        accum = jnp.zeros((kernel.shape[1],), jnp.float32)
        for tap_index in range(tail_len - row_index):
            accum = accum + kernel[tap_index] * tail_vals[row_index + tap_index]
        outputs.append(accum)
    return jnp.stack(outputs, axis=0)


def intra_block(scaled, b_rows, c_rows, cum_log):
    scores = jnp.einsum("tgn,sgn->gts", c_rows, b_rows, preferred_element_type=jnp.float32)
    cum_cols = jnp.moveaxis(cum_log, 0, -1)
    log_gap = cum_cols[..., :, None] - cum_cols[..., None, :]
    block_len = cum_log.shape[0]
    causal = jnp.arange(block_len)[:, None] >= jnp.arange(block_len)[None, :]
    decays = jnp.exp(jnp.where(causal, log_gap, -jnp.inf))
    weights = (scores[:, None] * decays).astype(jnp.bfloat16)
    return jnp.einsum("gjts,sgjp->tgjp", weights, scaled, preferred_element_type=jnp.float32)


def block_state(scaled, b_rows, cum_log):
    end_decay = jnp.exp(cum_log[-1][None] - cum_log)
    b_weighted = (b_rows.astype(jnp.float32)[:, :, None, :] * end_decay[..., None]).astype(
        jnp.bfloat16
    )
    return jnp.einsum("sgjp,sgjn->gjpn", scaled, b_weighted, preferred_element_type=jnp.float32)


def inter_block(c_rows, cum_log, state_carry):
    rounded = state_carry.astype(jnp.bfloat16)
    inner = jnp.einsum("tgn,gjpn->tgjp", c_rows, rounded, preferred_element_type=jnp.float32)
    return inner * jnp.exp(cum_log)[..., None]


def combine(first_part, second_part):
    decay_first, state_first = first_part
    decay_second, state_second = second_part
    return (
        decay_first * decay_second,
        decay_second[..., None, None] * state_first.astype(jnp.float32) + state_second,
    )


def on_link(part):
    decay, state = part
    return (decay, state.astype(jnp.bfloat16))


def prefix_states(dev_decay, dev_state, axis, count):
    own = (dev_decay, dev_state)
    if count == 1:
        return jnp.zeros_like(dev_state)
    got = shifted(on_link(own), axis, 1, count)
    before = got
    upto = combine(got, own)
    step = 2
    while step < count:
        got = shifted(on_link(upto), axis, step, count)
        before = combine(got, before)
        if step * 2 < count:
            upto = combine(got, upto)
        step *= 2
    return before[1].astype(jnp.float32)


def on_device(
    layout,
    features,
    input_map,
    output_map,
    gate_in,
    conv_feat,
    conv_input,
    conv_output,
    step_size,
    log_decay,
    skip_gain,
    norm_gain,
    out_weight,
):
    tok_rows, width_x = features.shape
    width_b = input_map.shape[1]
    head_count = step_size.shape[1]
    head_dim = width_x // head_count
    groups_here = width_b // N
    per_group = head_count // groups_here
    tail_len = conv_feat.shape[0] - 1
    n_blocks = tok_rows // BLOCK
    packed = jnp.concatenate([features, input_map, output_map], axis=1)
    kernel = jnp.concatenate([conv_feat, conv_input, conv_output], axis=1)
    pre_act = local_conv(packed, kernel, tok_rows)
    ctx_axes, ctx_count, outer_axis, inner_axis, tp_count = layout
    tail_rows = shifted(packed[tok_rows - tail_len :], ctx_axes, 1, ctx_count)
    edge_sums = edge_partial(tail_rows, kernel)
    pre_act = pre_act + jnp.pad(edge_sums, ((0, tok_rows - tail_len), (0, 0)))
    conv_out = jax.nn.silu(pre_act).astype(jnp.bfloat16)
    x_conv = conv_out[:, :width_x]
    b_conv = conv_out[:, width_x : width_x + width_b]
    c_conv = conv_out[:, width_x + width_b :]
    x_heads = x_conv.astype(jnp.float32).reshape(tok_rows, groups_here, per_group, head_dim)
    scaled = (x_heads * step_size.reshape(tok_rows, groups_here, per_group)[..., None]).astype(
        jnp.bfloat16
    )

    def blocked(value_entries):
        return value_entries.reshape((n_blocks, BLOCK) + value_entries.shape[1:])

    scaled_b = blocked(scaled)
    b_rows = blocked(b_conv.reshape(tok_rows, groups_here, N))
    c_rows = blocked(c_conv.reshape(tok_rows, groups_here, N))
    cum_log = jnp.cumsum(blocked(log_decay.reshape(tok_rows, groups_here, per_group)), axis=1)
    blk_states = jax.vmap(block_state)(scaled_b, b_rows, cum_log)
    blk_decay = jnp.exp(cum_log[:, -1])

    def fold_local(state_carry, block_in):
        decay_b, state_b = block_in
        return (decay_b[..., None, None] * state_carry + state_b, None)

    dev_state, _ = lax.scan(
        fold_local, jnp.zeros(blk_states.shape[1:], jnp.float32), (blk_decay, blk_states)
    )
    dev_decay = jnp.prod(blk_decay, axis=0)
    if outer_axis is not None:
        inner_count = ctx_count // tp_count
        split = out_weight.shape[1] // 2
        early, late = [], []
        for d in range(1, inner_count):
            pairs = [(s, (s + d) % inner_count) for s in range(inner_count)]
            early.append(lax.ppermute(out_weight[:, :split], inner_axis, pairs))
            late.append(lax.ppermute(out_weight[:, split:], inner_axis, pairs))
        early, dev_state = lax.optimization_barrier((early, dev_state))
        weight_pieces = [out_weight]
        for first, second in zip(early, late):
            weight_pieces += [first, second]
    incoming = prefix_states(dev_decay, dev_state, ctx_axes, ctx_count)

    def advance(state_carry, block_in):
        scaled_k, b_k, c_k, cum_k, decay_k, state_k = block_in
        block_y = intra_block(scaled_k, b_k, c_k, cum_k) + inter_block(c_k, cum_k, state_carry)
        return (decay_k[..., None, None] * state_carry + state_k, block_y)

    _, ssm_y = lax.scan(
        advance, incoming, (scaled_b, b_rows, c_rows, cum_log, blk_decay, blk_states)
    )
    mixed_y = ssm_y.reshape(tok_rows, groups_here, per_group, head_dim)
    mixed_y = mixed_y + skip_gain.reshape(groups_here, per_group)[..., None] * x_heads
    gated_y = mixed_y.reshape(tok_rows, width_x) * jax.nn.silu(gate_in.astype(jnp.float32))
    grouped = gated_y.reshape(tok_rows, groups_here, width_x // groups_here)
    inv_root = lax.rsqrt(jnp.mean(grouped * grouped, axis=-1, keepdims=True) + 1e-05)
    hidden = ((grouped * inv_root).reshape(tok_rows, width_x) * norm_gain).astype(jnp.bfloat16)
    if outer_axis is None:
        partial_out = jnp.dot(
            hidden,
            lax.all_gather(out_weight, ctx_axes, axis=1, tiled=True),
            preferred_element_type=jnp.float32,
        )
        return lax.psum_scatter(partial_out, "tp", scatter_dimension=1, tiled=True).astype(
            jnp.bfloat16
        )
    outer_at = lax.axis_index(outer_axis)
    tp_at = lax.axis_index("tp")
    inner_count = ctx_count // tp_count
    weight_pieces, hidden = lax.optimization_barrier((weight_pieces, hidden))
    def times_weight(rows):
        return jnp.concatenate(
            [jnp.dot(rows, piece, preferred_element_type=jnp.float32) for piece in weight_pieces],
            axis=1,
        )

    from_left, from_right = {}, {}
    going_right = going_left = hidden
    for step in range(1, tp_count - 1):
        going_right = lax.ppermute(
            going_right, outer_axis, [(s, s + 1) for s in range(step - 1, tp_count - 1)]
        )
        going_left = lax.ppermute(
            going_left, outer_axis, [(s, s - 1) for s in range(1, tp_count - step + 1)]
        )
        from_left[step], from_right[step] = going_right, going_left
    far = lax.ppermute(
        jnp.where(outer_at == tp_count - 2, going_right, going_left),
        outer_axis,
        [(tp_count - 2, tp_count - 1), (1, 0)],
    )
    far_part = times_weight(far)
    by_source = jnp.stack(
        [times_weight(hidden)]
        + [
            jnp.where(
                outer_at >= d,
                times_weight(from_left[d]) if d < tp_count - 1 else far_part,
                times_weight(from_right[tp_count - d]) if d > 1 else far_part,
            )
            if d != tp_count // 2
            else times_weight(jnp.where(outer_at >= d, from_left[d], from_right[d]))
            for d in range(1, tp_count)
        ]
    )

    def for_target(target):
        return lax.dynamic_index_in_dim(
            by_source, (outer_at - target + tp_count) % tp_count, 0, keepdims=False
        )

    held = {m: for_target(tp_at ^ m) for m in range(tp_count)}
    bit = 1
    while bit < tp_count:
        going = sorted(m for m in held if m & bit)
        sent = jnp.stack([held[m] for m in going])
        got = lax.ppermute(
            sent if bit == 1 else sent.astype(jnp.bfloat16),
            "tp",
            [(s, s ^ bit) for s in range(tp_count)],
        )
        held = {m: held[m] for m in held if not m & bit}
        for index, m in enumerate(going):
            held[m ^ bit] = held[m ^ bit] + got[index].astype(jnp.float32)
        bit *= 2
    swap = [(o * tp_count + t, t * tp_count + o) for o in range(tp_count) for t in range(tp_count)]
    rotated = lax.ppermute(held[0].astype(jnp.bfloat16), (outer_axis, "tp"), swap)
    width = out_weight.shape[1]
    pieces = jnp.stack([rotated[:, d * width : (d + 1) * width] for d in range(inner_count)])
    inner_at = lax.axis_index(inner_axis)
    return jnp.concatenate(
        [
            lax.dynamic_index_in_dim(
                pieces, (inner_at - place + inner_count) % inner_count, 0, keepdims=False
            )
            for place in range(inner_count)
        ],
        axis=1,
    )


def solution(mesh):
    ctx_count = mesh.shape["ctx"]
    tp_count = mesh.shape["tp"]
    if ctx_count % tp_count == 0 and tp_count == 4:
        inner = ctx_count // tp_count
        grid = mesh.devices.reshape(tp_count, inner, tp_count)
        mesh = jax.sharding.Mesh(grid, ("outer", "inner", "tp"))
        ctx_axes = ("outer", "inner")
        layout = (ctx_axes, ctx_count, "outer", "inner", tp_count)
    else:
        ctx_axes = "ctx"
        layout = (ctx_axes, ctx_count, None, None, tp_count)
    placed = (
        P(ctx_axes, "tp"),
        P(ctx_axes, "tp"),
        P(ctx_axes, "tp"),
        P(ctx_axes, "tp"),
        P(None, "tp"),
        P(None, "tp"),
        P(None, "tp"),
        P(ctx_axes, "tp"),
        P(ctx_axes, "tp"),
        P("tp"),
        P("tp"),
        P("tp", ctx_axes),
    )
    return jax.shard_map(
        functools.partial(on_device, layout),
        mesh=mesh,
        in_specs=placed,
        out_specs=P(ctx_axes, "tp"),
        check_vma=False,
    )
```

```python
import functools

import jax
import jax.numpy as jnp
from jax import lax
from jax.sharding import PartitionSpec as P

N = 128
BLOCK = 256


def shifted(value, axis, steps, count):
    first, last = (max(0, -steps), min(count, count - steps))
    return lax.ppermute(value, axis, [(source, source + steps) for source in range(first, last)])


def local_conv(packed, kernel, tok_rows):
    tail_len = kernel.shape[0] - 1
    padded = jnp.pad(packed.astype(jnp.float32), ((tail_len, 0), (0, 0)))
    pre_act = jnp.zeros((tok_rows, kernel.shape[1]), jnp.float32)
    for tap_index in range(kernel.shape[0]):
        pre_act = pre_act + kernel[tap_index] * padded[tap_index : tap_index + tok_rows]
    return pre_act


def edge_partial(tail_rows, kernel):
    tail_len = kernel.shape[0] - 1
    tail_vals = tail_rows.astype(jnp.float32)
    outputs = []
    for row_index in range(tail_len):
        accum = jnp.zeros((kernel.shape[1],), jnp.float32)
        for tap_index in range(tail_len - row_index):
            accum = accum + kernel[tap_index] * tail_vals[row_index + tap_index]
        outputs.append(accum)
    return jnp.stack(outputs, axis=0)


def intra_block(scaled, b_rows, c_rows, cum_log):
    scores = jnp.einsum("tgn,sgn->gts", c_rows, b_rows, preferred_element_type=jnp.float32)
    cum_cols = jnp.moveaxis(cum_log, 0, -1)
    log_gap = cum_cols[..., :, None] - cum_cols[..., None, :]
    block_len = cum_log.shape[0]
    causal = jnp.arange(block_len)[:, None] >= jnp.arange(block_len)[None, :]
    decays = jnp.exp(jnp.where(causal, log_gap, -jnp.inf))
    weights = (scores[:, None] * decays).astype(jnp.bfloat16)
    return jnp.einsum("gjts,sgjp->tgjp", weights, scaled, preferred_element_type=jnp.float32)


def block_state(scaled, b_rows, cum_log):
    end_decay = jnp.exp(cum_log[-1][None] - cum_log)
    b_weighted = (b_rows.astype(jnp.float32)[:, :, None, :] * end_decay[..., None]).astype(
        jnp.bfloat16
    )
    return jnp.einsum("sgjp,sgjn->gjpn", scaled, b_weighted, preferred_element_type=jnp.float32)


def inter_block(c_rows, cum_log, state_carry):
    rounded = state_carry.astype(jnp.bfloat16)
    inner = jnp.einsum("tgn,gjpn->tgjp", c_rows, rounded, preferred_element_type=jnp.float32)
    return inner * jnp.exp(cum_log)[..., None]


def combine(first_part, second_part):
    decay_first, state_first = first_part
    decay_second, state_second = second_part
    return (
        decay_first * decay_second,
        decay_second[..., None, None] * state_first.astype(jnp.float32) + state_second,
    )


def on_link(part):
    decay, state = part
    return (decay, state.astype(jnp.bfloat16))


def prefix_states(dev_decay, dev_state, axis, count):
    own = (dev_decay, dev_state)
    if count == 1:
        return jnp.zeros_like(dev_state)
    radix = 4
    before = (jnp.ones_like(dev_decay), jnp.zeros_like(dev_state))
    upto = own
    span = 1
    while span < count:
        got = [
            shifted(on_link(upto), axis, d * span, count)
            for d in range(1, radix)
            if d * span < count
        ]
        for item in got:
            before = combine(item, before)
        span *= radix
        if span < count:
            upto = combine(before, own)
    return before[1].astype(jnp.float32)


def on_device(
    layout,
    features,
    input_map,
    output_map,
    gate_in,
    conv_feat,
    conv_input,
    conv_output,
    step_size,
    log_decay,
    skip_gain,
    norm_gain,
    out_weight,
):
    tok_rows, width_x = features.shape
    width_b = input_map.shape[1]
    head_count = step_size.shape[1]
    head_dim = width_x // head_count
    groups_here = width_b // N
    per_group = head_count // groups_here
    tail_len = conv_feat.shape[0] - 1
    n_blocks = tok_rows // BLOCK
    packed = jnp.concatenate([features, input_map, output_map], axis=1)
    kernel = jnp.concatenate([conv_feat, conv_input, conv_output], axis=1)
    pre_act = local_conv(packed, kernel, tok_rows)
    ctx_axes, ctx_count, outer_axis, inner_axis, tp_count = layout
    tail_rows = shifted(packed[tok_rows - tail_len :], ctx_axes, 1, ctx_count)
    edge_sums = edge_partial(tail_rows, kernel)
    pre_act = pre_act + jnp.pad(edge_sums, ((0, tok_rows - tail_len), (0, 0)))
    conv_out = jax.nn.silu(pre_act).astype(jnp.bfloat16)
    x_conv = conv_out[:, :width_x]
    b_conv = conv_out[:, width_x : width_x + width_b]
    c_conv = conv_out[:, width_x + width_b :]
    x_heads = x_conv.astype(jnp.float32).reshape(tok_rows, groups_here, per_group, head_dim)
    scaled = (x_heads * step_size.reshape(tok_rows, groups_here, per_group)[..., None]).astype(
        jnp.bfloat16
    )

    def blocked(value_entries):
        return value_entries.reshape((n_blocks, BLOCK) + value_entries.shape[1:])

    scaled_b = blocked(scaled)
    b_rows = blocked(b_conv.reshape(tok_rows, groups_here, N))
    c_rows = blocked(c_conv.reshape(tok_rows, groups_here, N))
    cum_log = jnp.cumsum(blocked(log_decay.reshape(tok_rows, groups_here, per_group)), axis=1)
    blk_states = jax.vmap(block_state)(scaled_b, b_rows, cum_log)
    blk_decay = jnp.exp(cum_log[:, -1])

    def fold_local(state_carry, block_in):
        decay_b, state_b = block_in
        return (decay_b[..., None, None] * state_carry + state_b, None)

    dev_state, _ = lax.scan(
        fold_local, jnp.zeros(blk_states.shape[1:], jnp.float32), (blk_decay, blk_states)
    )
    dev_decay = jnp.prod(blk_decay, axis=0)
    incoming = prefix_states(dev_decay, dev_state, ctx_axes, ctx_count)

    def advance(state_carry, block_in):
        scaled_k, b_k, c_k, cum_k, decay_k, state_k = block_in
        block_y = intra_block(scaled_k, b_k, c_k, cum_k) + inter_block(c_k, cum_k, state_carry)
        return (decay_k[..., None, None] * state_carry + state_k, block_y)

    _, ssm_y = lax.scan(
        advance, incoming, (scaled_b, b_rows, c_rows, cum_log, blk_decay, blk_states)
    )
    mixed_y = ssm_y.reshape(tok_rows, groups_here, per_group, head_dim)
    mixed_y = mixed_y + skip_gain.reshape(groups_here, per_group)[..., None] * x_heads
    gated_y = mixed_y.reshape(tok_rows, width_x) * jax.nn.silu(gate_in.astype(jnp.float32))
    grouped = gated_y.reshape(tok_rows, groups_here, width_x // groups_here)
    inv_root = lax.rsqrt(jnp.mean(grouped * grouped, axis=-1, keepdims=True) + 1e-05)
    hidden = ((grouped * inv_root).reshape(tok_rows, width_x) * norm_gain).astype(jnp.bfloat16)
    if outer_axis is None:
        partial_out = jnp.dot(
            hidden,
            lax.all_gather(out_weight, ctx_axes, axis=1, tiled=True),
            preferred_element_type=jnp.float32,
        )
        return lax.psum_scatter(partial_out, "tp", scatter_dimension=1, tiled=True).astype(
            jnp.bfloat16
        )
    outer_at = lax.axis_index(outer_axis)
    tp_at = lax.axis_index("tp")
    inner_count = ctx_count // tp_count
    weight_pieces = [out_weight] + [
        lax.ppermute(
            out_weight, inner_axis, [(s, (s + d) % inner_count) for s in range(inner_count)]
        )
        for d in range(1, inner_count)
    ]
    weight_pieces, hidden = lax.optimization_barrier((weight_pieces, hidden))
    def times_weight(rows):
        return jnp.concatenate(
            [jnp.dot(rows, piece, preferred_element_type=jnp.float32) for piece in weight_pieces],
            axis=1,
        )

    from_left, from_right = {}, {}
    going_right = going_left = hidden
    for step in range(1, tp_count - 1):
        going_right = lax.ppermute(
            going_right, outer_axis, [(s, s + 1) for s in range(step - 1, tp_count - 1)]
        )
        going_left = lax.ppermute(
            going_left, outer_axis, [(s, s - 1) for s in range(1, tp_count - step + 1)]
        )
        from_left[step], from_right[step] = going_right, going_left
    far = lax.ppermute(
        jnp.where(outer_at == tp_count - 2, going_right, going_left),
        outer_axis,
        [(tp_count - 2, tp_count - 1), (1, 0)],
    )
    far_part = times_weight(far)
    by_source = jnp.stack(
        [times_weight(hidden)]
        + [
            jnp.where(
                outer_at >= d,
                times_weight(from_left[d]) if d < tp_count - 1 else far_part,
                times_weight(from_right[tp_count - d]) if d > 1 else far_part,
            )
            if d != tp_count // 2
            else times_weight(jnp.where(outer_at >= d, from_left[d], from_right[d]))
            for d in range(1, tp_count)
        ]
    )

    def for_target(target):
        return lax.dynamic_index_in_dim(
            by_source, (outer_at - target + tp_count) % tp_count, 0, keepdims=False
        )

    held = {m: for_target(tp_at ^ m) for m in range(tp_count)}
    bit = 1
    while bit < tp_count:
        going = sorted(m for m in held if m & bit)
        sent = jnp.stack([held[m] for m in going])
        got = lax.ppermute(
            sent if bit == 1 else sent.astype(jnp.bfloat16),
            "tp",
            [(s, s ^ bit) for s in range(tp_count)],
        )
        held = {m: held[m] for m in held if not m & bit}
        for index, m in enumerate(going):
            held[m ^ bit] = held[m ^ bit] + got[index].astype(jnp.float32)
        bit *= 2
    swap = [(o * tp_count + t, t * tp_count + o) for o in range(tp_count) for t in range(tp_count)]
    rotated = lax.ppermute(held[0].astype(jnp.bfloat16), (outer_axis, "tp"), swap)
    width = out_weight.shape[1]
    pieces = jnp.stack([rotated[:, d * width : (d + 1) * width] for d in range(inner_count)])
    inner_at = lax.axis_index(inner_axis)
    return jnp.concatenate(
        [
            lax.dynamic_index_in_dim(
                pieces, (inner_at - place + inner_count) % inner_count, 0, keepdims=False
            )
            for place in range(inner_count)
        ],
        axis=1,
    )


def solution(mesh):
    ctx_count = mesh.shape["ctx"]
    tp_count = mesh.shape["tp"]
    if ctx_count % tp_count == 0 and tp_count == 4:
        inner = ctx_count // tp_count
        grid = mesh.devices.reshape(tp_count, inner, tp_count)
        mesh = jax.sharding.Mesh(grid, ("outer", "inner", "tp"))
        ctx_axes = ("outer", "inner")
        layout = (ctx_axes, ctx_count, "outer", "inner", tp_count)
    else:
        ctx_axes = "ctx"
        layout = (ctx_axes, ctx_count, None, None, tp_count)
    placed = (
        P(ctx_axes, "tp"),
        P(ctx_axes, "tp"),
        P(ctx_axes, "tp"),
        P(ctx_axes, "tp"),
        P(None, "tp"),
        P(None, "tp"),
        P(None, "tp"),
        P(ctx_axes, "tp"),
        P(ctx_axes, "tp"),
        P("tp"),
        P("tp"),
        P("tp", ctx_axes),
    )
    return jax.shard_map(
        functools.partial(on_device, layout),
        mesh=mesh,
        in_specs=placed,
        out_specs=P(ctx_axes, "tp"),
        check_vma=False,
    )
```

```python
import functools

import jax
import jax.numpy as jnp
from jax import lax
from jax.sharding import PartitionSpec as P

N = 128
BLOCK = 256


def shifted(value, axis, steps, count):
    first, last = (max(0, -steps), min(count, count - steps))
    return lax.ppermute(value, axis, [(source, source + steps) for source in range(first, last)])


def local_conv(packed, kernel, tok_rows):
    tail_len = kernel.shape[0] - 1
    padded = jnp.pad(packed.astype(jnp.float32), ((tail_len, 0), (0, 0)))
    pre_act = jnp.zeros((tok_rows, kernel.shape[1]), jnp.float32)
    for tap_index in range(kernel.shape[0]):
        pre_act = pre_act + kernel[tap_index] * padded[tap_index : tap_index + tok_rows]
    return pre_act


def edge_partial(tail_rows, kernel):
    tail_len = kernel.shape[0] - 1
    tail_vals = tail_rows.astype(jnp.float32)
    outputs = []
    for row_index in range(tail_len):
        accum = jnp.zeros((kernel.shape[1],), jnp.float32)
        for tap_index in range(tail_len - row_index):
            accum = accum + kernel[tap_index] * tail_vals[row_index + tap_index]
        outputs.append(accum)
    return jnp.stack(outputs, axis=0)


def intra_block(scaled, b_rows, c_rows, cum_log):
    scores = jnp.einsum("tgn,sgn->gts", c_rows, b_rows, preferred_element_type=jnp.float32)
    cum_cols = jnp.moveaxis(cum_log, 0, -1)
    log_gap = cum_cols[..., :, None] - cum_cols[..., None, :]
    block_len = cum_log.shape[0]
    causal = jnp.arange(block_len)[:, None] >= jnp.arange(block_len)[None, :]
    decays = jnp.exp(jnp.where(causal, log_gap, -jnp.inf))
    weights = (scores[:, None] * decays).astype(jnp.bfloat16)
    return jnp.einsum("gjts,sgjp->tgjp", weights, scaled, preferred_element_type=jnp.float32)


def block_state(scaled, b_rows, cum_log):
    end_decay = jnp.exp(cum_log[-1][None] - cum_log)
    b_weighted = (b_rows.astype(jnp.float32)[:, :, None, :] * end_decay[..., None]).astype(
        jnp.bfloat16
    )
    return jnp.einsum("sgjp,sgjn->gjpn", scaled, b_weighted, preferred_element_type=jnp.float32)


def inter_block(c_rows, cum_log, state_carry):
    rounded = state_carry.astype(jnp.bfloat16)
    inner = jnp.einsum("tgn,gjpn->tgjp", c_rows, rounded, preferred_element_type=jnp.float32)
    return inner * jnp.exp(cum_log)[..., None]


def combine(first_part, second_part):
    decay_first, state_first = first_part
    decay_second, state_second = second_part
    return (
        decay_first * decay_second,
        decay_second[..., None, None] * state_first.astype(jnp.float32) + state_second,
    )


def on_link(part):
    decay, state = part
    return (decay, state.astype(jnp.bfloat16))


def prefix_states(dev_decay, dev_state, axis, count):
    if count == 1:
        return jnp.zeros_like(dev_state)
    got = shifted(dev_decay, axis, 1, count)
    decay_before, decay_upto = got, got * dev_decay
    scales = []
    step = 2
    while step < count:
        scales.append((decay_before, decay_upto))
        got = shifted(decay_upto, axis, step, count)
        decay_before, decay_upto = got * decay_before, got * decay_upto
        step *= 2
    scales, dev_state = lax.optimization_barrier((scales, dev_state))
    got = shifted(dev_state.astype(jnp.bfloat16), axis, 1, count).astype(jnp.float32)
    before = got
    upto = dev_decay[..., None, None] * got + dev_state
    step = 2
    for scale_before, scale_upto in scales:
        got = shifted(upto.astype(jnp.bfloat16), axis, step, count).astype(jnp.float32)
        before = scale_before[..., None, None] * got + before
        if step * 2 < count:
            upto = scale_upto[..., None, None] * got + upto
        step *= 2
    return before


def on_device(
    layout,
    features,
    input_map,
    output_map,
    gate_in,
    conv_feat,
    conv_input,
    conv_output,
    step_size,
    log_decay,
    skip_gain,
    norm_gain,
    out_weight,
):
    tok_rows, width_x = features.shape
    width_b = input_map.shape[1]
    head_count = step_size.shape[1]
    head_dim = width_x // head_count
    groups_here = width_b // N
    per_group = head_count // groups_here
    tail_len = conv_feat.shape[0] - 1
    n_blocks = tok_rows // BLOCK
    packed = jnp.concatenate([features, input_map, output_map], axis=1)
    kernel = jnp.concatenate([conv_feat, conv_input, conv_output], axis=1)
    pre_act = local_conv(packed, kernel, tok_rows)
    ctx_axes, ctx_count, outer_axis, inner_axis, tp_count = layout
    tail_rows = shifted(packed[tok_rows - tail_len :], ctx_axes, 1, ctx_count)
    edge_sums = edge_partial(tail_rows, kernel)
    pre_act = pre_act + jnp.pad(edge_sums, ((0, tok_rows - tail_len), (0, 0)))
    conv_out = jax.nn.silu(pre_act).astype(jnp.bfloat16)
    x_conv = conv_out[:, :width_x]
    b_conv = conv_out[:, width_x : width_x + width_b]
    c_conv = conv_out[:, width_x + width_b :]
    x_heads = x_conv.astype(jnp.float32).reshape(tok_rows, groups_here, per_group, head_dim)
    scaled = (x_heads * step_size.reshape(tok_rows, groups_here, per_group)[..., None]).astype(
        jnp.bfloat16
    )

    def blocked(value_entries):
        return value_entries.reshape((n_blocks, BLOCK) + value_entries.shape[1:])

    scaled_b = blocked(scaled)
    b_rows = blocked(b_conv.reshape(tok_rows, groups_here, N))
    c_rows = blocked(c_conv.reshape(tok_rows, groups_here, N))
    cum_log = jnp.cumsum(blocked(log_decay.reshape(tok_rows, groups_here, per_group)), axis=1)
    blk_states = jax.vmap(block_state)(scaled_b, b_rows, cum_log)
    blk_decay = jnp.exp(cum_log[:, -1])

    def fold_local(state_carry, block_in):
        decay_b, state_b = block_in
        return (decay_b[..., None, None] * state_carry + state_b, None)

    dev_state, _ = lax.scan(
        fold_local, jnp.zeros(blk_states.shape[1:], jnp.float32), (blk_decay, blk_states)
    )
    dev_decay = jnp.prod(blk_decay, axis=0)
    incoming = prefix_states(dev_decay, dev_state, ctx_axes, ctx_count)

    def advance(state_carry, block_in):
        scaled_k, b_k, c_k, cum_k, decay_k, state_k = block_in
        block_y = intra_block(scaled_k, b_k, c_k, cum_k) + inter_block(c_k, cum_k, state_carry)
        return (decay_k[..., None, None] * state_carry + state_k, block_y)

    _, ssm_y = lax.scan(
        advance, incoming, (scaled_b, b_rows, c_rows, cum_log, blk_decay, blk_states)
    )
    mixed_y = ssm_y.reshape(tok_rows, groups_here, per_group, head_dim)
    mixed_y = mixed_y + skip_gain.reshape(groups_here, per_group)[..., None] * x_heads
    gated_y = mixed_y.reshape(tok_rows, width_x) * jax.nn.silu(gate_in.astype(jnp.float32))
    grouped = gated_y.reshape(tok_rows, groups_here, width_x // groups_here)
    inv_root = lax.rsqrt(jnp.mean(grouped * grouped, axis=-1, keepdims=True) + 1e-05)
    hidden = ((grouped * inv_root).reshape(tok_rows, width_x) * norm_gain).astype(jnp.bfloat16)
    if outer_axis is None:
        partial_out = jnp.dot(
            hidden,
            lax.all_gather(out_weight, ctx_axes, axis=1, tiled=True),
            preferred_element_type=jnp.float32,
        )
        return lax.psum_scatter(partial_out, "tp", scatter_dimension=1, tiled=True).astype(
            jnp.bfloat16
        )
    outer_at = lax.axis_index(outer_axis)
    tp_at = lax.axis_index("tp")
    inner_count = ctx_count // tp_count
    weight_pieces = [out_weight] + [
        lax.ppermute(
            out_weight, inner_axis, [(s, (s + d) % inner_count) for s in range(inner_count)]
        )
        for d in range(1, inner_count)
    ]
    weight_pieces, hidden = lax.optimization_barrier((weight_pieces, hidden))
    def times_weight(rows):
        return jnp.concatenate(
            [jnp.dot(rows, piece, preferred_element_type=jnp.float32) for piece in weight_pieces],
            axis=1,
        )

    from_left, from_right = {}, {}
    going_right = going_left = hidden
    for step in range(1, tp_count - 1):
        going_right = lax.ppermute(
            going_right, outer_axis, [(s, s + 1) for s in range(step - 1, tp_count - 1)]
        )
        going_left = lax.ppermute(
            going_left, outer_axis, [(s, s - 1) for s in range(1, tp_count - step + 1)]
        )
        from_left[step], from_right[step] = going_right, going_left
    far = lax.ppermute(
        jnp.where(outer_at == tp_count - 2, going_right, going_left),
        outer_axis,
        [(tp_count - 2, tp_count - 1), (1, 0)],
    )
    far_part = times_weight(far)
    by_source = jnp.stack(
        [times_weight(hidden)]
        + [
            jnp.where(
                outer_at >= d,
                times_weight(from_left[d]) if d < tp_count - 1 else far_part,
                times_weight(from_right[tp_count - d]) if d > 1 else far_part,
            )
            if d != tp_count // 2
            else times_weight(jnp.where(outer_at >= d, from_left[d], from_right[d]))
            for d in range(1, tp_count)
        ]
    )

    def for_target(target):
        return lax.dynamic_index_in_dim(
            by_source, (outer_at - target + tp_count) % tp_count, 0, keepdims=False
        )

    held = {m: for_target(tp_at ^ m) for m in range(tp_count)}
    bit = 1
    while bit < tp_count:
        going = sorted(m for m in held if m & bit)
        sent = jnp.stack([held[m] for m in going])
        got = lax.ppermute(
            sent if bit == 1 else sent.astype(jnp.bfloat16),
            "tp",
            [(s, s ^ bit) for s in range(tp_count)],
        )
        held = {m: held[m] for m in held if not m & bit}
        for index, m in enumerate(going):
            held[m ^ bit] = held[m ^ bit] + got[index].astype(jnp.float32)
        bit *= 2
    swap = [(o * tp_count + t, t * tp_count + o) for o in range(tp_count) for t in range(tp_count)]
    rotated = lax.ppermute(held[0].astype(jnp.bfloat16), (outer_axis, "tp"), swap)
    width = out_weight.shape[1]
    pieces = jnp.stack([rotated[:, d * width : (d + 1) * width] for d in range(inner_count)])
    inner_at = lax.axis_index(inner_axis)
    return jnp.concatenate(
        [
            lax.dynamic_index_in_dim(
                pieces, (inner_at - place + inner_count) % inner_count, 0, keepdims=False
            )
            for place in range(inner_count)
        ],
        axis=1,
    )


def solution(mesh):
    ctx_count = mesh.shape["ctx"]
    tp_count = mesh.shape["tp"]
    if ctx_count % tp_count == 0 and tp_count == 4:
        inner = ctx_count // tp_count
        grid = mesh.devices.reshape(tp_count, inner, tp_count)
        mesh = jax.sharding.Mesh(grid, ("outer", "inner", "tp"))
        ctx_axes = ("outer", "inner")
        layout = (ctx_axes, ctx_count, "outer", "inner", tp_count)
    else:
        ctx_axes = "ctx"
        layout = (ctx_axes, ctx_count, None, None, tp_count)
    placed = (
        P(ctx_axes, "tp"),
        P(ctx_axes, "tp"),
        P(ctx_axes, "tp"),
        P(ctx_axes, "tp"),
        P(None, "tp"),
        P(None, "tp"),
        P(None, "tp"),
        P(ctx_axes, "tp"),
        P(ctx_axes, "tp"),
        P("tp"),
        P("tp"),
        P("tp", ctx_axes),
    )
    return jax.shard_map(
        functools.partial(on_device, layout),
        mesh=mesh,
        in_specs=placed,
        out_specs=P(ctx_axes, "tp"),
        check_vma=False,
    )
```

```python
import functools

import jax
import jax.numpy as jnp
from jax import lax
from jax.sharding import PartitionSpec as P

N = 128
BLOCK = 256


def shifted(value, axis, steps, count):
    first, last = (max(0, -steps), min(count, count - steps))
    return lax.ppermute(value, axis, [(source, source + steps) for source in range(first, last)])


def local_conv(packed, kernel, tok_rows):
    tail_len = kernel.shape[0] - 1
    padded = jnp.pad(packed.astype(jnp.float32), ((tail_len, 0), (0, 0)))
    pre_act = jnp.zeros((tok_rows, kernel.shape[1]), jnp.float32)
    for tap_index in range(kernel.shape[0]):
        pre_act = pre_act + kernel[tap_index] * padded[tap_index : tap_index + tok_rows]
    return pre_act


def edge_partial(tail_rows, kernel):
    tail_len = kernel.shape[0] - 1
    tail_vals = tail_rows.astype(jnp.float32)
    outputs = []
    for row_index in range(tail_len):
        accum = jnp.zeros((kernel.shape[1],), jnp.float32)
        for tap_index in range(tail_len - row_index):
            accum = accum + kernel[tap_index] * tail_vals[row_index + tap_index]
        outputs.append(accum)
    return jnp.stack(outputs, axis=0)


def intra_block(scaled, b_rows, c_rows, cum_log):
    scores = jnp.einsum("tgn,sgn->gts", c_rows, b_rows, preferred_element_type=jnp.float32)
    cum_cols = jnp.moveaxis(cum_log, 0, -1)
    log_gap = cum_cols[..., :, None] - cum_cols[..., None, :]
    block_len = cum_log.shape[0]
    causal = jnp.arange(block_len)[:, None] >= jnp.arange(block_len)[None, :]
    decays = jnp.exp(jnp.where(causal, log_gap, -jnp.inf))
    weights = (scores[:, None] * decays).astype(jnp.bfloat16)
    return jnp.einsum("gjts,sgjp->tgjp", weights, scaled, preferred_element_type=jnp.float32)


def block_state(scaled, b_rows, cum_log):
    end_decay = jnp.exp(cum_log[-1][None] - cum_log)
    b_weighted = (b_rows.astype(jnp.float32)[:, :, None, :] * end_decay[..., None]).astype(
        jnp.bfloat16
    )
    return jnp.einsum("sgjp,sgjn->gjpn", scaled, b_weighted, preferred_element_type=jnp.float32)


def inter_block(c_rows, cum_log, state_carry):
    rounded = state_carry.astype(jnp.bfloat16)
    inner = jnp.einsum("tgn,gjpn->tgjp", c_rows, rounded, preferred_element_type=jnp.float32)
    return inner * jnp.exp(cum_log)[..., None]


def combine(first_part, second_part):
    decay_first, state_first = first_part
    decay_second, state_second = second_part
    return (
        decay_first * decay_second,
        decay_second[..., None, None] * state_first.astype(jnp.float32) + state_second,
    )


def on_link(part):
    decay, state = part
    heads = decay.shape[-1]
    high = decay.astype(jnp.bfloat16)
    low = (decay - high.astype(jnp.float32)).astype(jnp.bfloat16)
    rows = jnp.concatenate([high, low], axis=0)
    carrier = jnp.pad(rows, ((0, state.shape[-2] - 2), (0, state.shape[-1] - heads)))
    return jnp.concatenate([state.astype(jnp.bfloat16), carrier[None, None]], axis=1)


def off_link(packed):
    heads = packed.shape[1] - 1
    carrier = packed[0, heads].astype(jnp.float32)
    decay = (carrier[0, :heads] + carrier[1, :heads])[None]
    return (decay, packed[:, :heads])


def prefix_states(dev_decay, dev_state, axis, count):
    own = (dev_decay, dev_state)
    if count == 1:
        return jnp.zeros_like(dev_state)
    got = off_link(shifted(on_link(own), axis, 1, count))
    before = got
    upto = combine(got, own)
    step = 2
    while step < count:
        got = off_link(shifted(on_link(upto), axis, step, count))
        before = combine(got, before)
        if step * 2 < count:
            upto = combine(got, upto)
        step *= 2
    return before[1].astype(jnp.float32)


def on_device(
    layout,
    features,
    input_map,
    output_map,
    gate_in,
    conv_feat,
    conv_input,
    conv_output,
    step_size,
    log_decay,
    skip_gain,
    norm_gain,
    out_weight,
):
    tok_rows, width_x = features.shape
    width_b = input_map.shape[1]
    head_count = step_size.shape[1]
    head_dim = width_x // head_count
    groups_here = width_b // N
    per_group = head_count // groups_here
    tail_len = conv_feat.shape[0] - 1
    n_blocks = tok_rows // BLOCK
    packed = jnp.concatenate([features, input_map, output_map], axis=1)
    kernel = jnp.concatenate([conv_feat, conv_input, conv_output], axis=1)
    pre_act = local_conv(packed, kernel, tok_rows)
    ctx_axes, ctx_count, outer_axis, inner_axis, tp_count = layout
    tail_rows = shifted(packed[tok_rows - tail_len :], ctx_axes, 1, ctx_count)
    edge_sums = edge_partial(tail_rows, kernel)
    pre_act = pre_act + jnp.pad(edge_sums, ((0, tok_rows - tail_len), (0, 0)))
    conv_out = jax.nn.silu(pre_act).astype(jnp.bfloat16)
    x_conv = conv_out[:, :width_x]
    b_conv = conv_out[:, width_x : width_x + width_b]
    c_conv = conv_out[:, width_x + width_b :]
    x_heads = x_conv.astype(jnp.float32).reshape(tok_rows, groups_here, per_group, head_dim)
    scaled = (x_heads * step_size.reshape(tok_rows, groups_here, per_group)[..., None]).astype(
        jnp.bfloat16
    )

    def blocked(value_entries):
        return value_entries.reshape((n_blocks, BLOCK) + value_entries.shape[1:])

    scaled_b = blocked(scaled)
    b_rows = blocked(b_conv.reshape(tok_rows, groups_here, N))
    c_rows = blocked(c_conv.reshape(tok_rows, groups_here, N))
    cum_log = jnp.cumsum(blocked(log_decay.reshape(tok_rows, groups_here, per_group)), axis=1)
    blk_states = jax.vmap(block_state)(scaled_b, b_rows, cum_log)
    blk_decay = jnp.exp(cum_log[:, -1])

    def fold_local(state_carry, block_in):
        decay_b, state_b = block_in
        return (decay_b[..., None, None] * state_carry + state_b, None)

    dev_state, _ = lax.scan(
        fold_local, jnp.zeros(blk_states.shape[1:], jnp.float32), (blk_decay, blk_states)
    )
    dev_decay = jnp.prod(blk_decay, axis=0)
    incoming = prefix_states(dev_decay, dev_state, ctx_axes, ctx_count)

    def advance(state_carry, block_in):
        scaled_k, b_k, c_k, cum_k, decay_k, state_k = block_in
        block_y = intra_block(scaled_k, b_k, c_k, cum_k) + inter_block(c_k, cum_k, state_carry)
        return (decay_k[..., None, None] * state_carry + state_k, block_y)

    _, ssm_y = lax.scan(
        advance, incoming, (scaled_b, b_rows, c_rows, cum_log, blk_decay, blk_states)
    )
    mixed_y = ssm_y.reshape(tok_rows, groups_here, per_group, head_dim)
    mixed_y = mixed_y + skip_gain.reshape(groups_here, per_group)[..., None] * x_heads
    gated_y = mixed_y.reshape(tok_rows, width_x) * jax.nn.silu(gate_in.astype(jnp.float32))
    grouped = gated_y.reshape(tok_rows, groups_here, width_x // groups_here)
    inv_root = lax.rsqrt(jnp.mean(grouped * grouped, axis=-1, keepdims=True) + 1e-05)
    hidden = ((grouped * inv_root).reshape(tok_rows, width_x) * norm_gain).astype(jnp.bfloat16)
    if outer_axis is None:
        partial_out = jnp.dot(
            hidden,
            lax.all_gather(out_weight, ctx_axes, axis=1, tiled=True),
            preferred_element_type=jnp.float32,
        )
        return lax.psum_scatter(partial_out, "tp", scatter_dimension=1, tiled=True).astype(
            jnp.bfloat16
        )
    outer_at = lax.axis_index(outer_axis)
    tp_at = lax.axis_index("tp")
    inner_count = ctx_count // tp_count
    weight_pieces = [out_weight] + [
        lax.ppermute(
            out_weight, inner_axis, [(s, (s + d) % inner_count) for s in range(inner_count)]
        )
        for d in range(1, inner_count)
    ]
    weight_pieces, hidden = lax.optimization_barrier((weight_pieces, hidden))
    def times_weight(rows):
        return jnp.concatenate(
            [jnp.dot(rows, piece, preferred_element_type=jnp.float32) for piece in weight_pieces],
            axis=1,
        )

    from_left, from_right = {}, {}
    going_right = going_left = hidden
    for step in range(1, tp_count - 1):
        going_right = lax.ppermute(
            going_right, outer_axis, [(s, s + 1) for s in range(step - 1, tp_count - 1)]
        )
        going_left = lax.ppermute(
            going_left, outer_axis, [(s, s - 1) for s in range(1, tp_count - step + 1)]
        )
        from_left[step], from_right[step] = going_right, going_left
    far = lax.ppermute(
        jnp.where(outer_at == tp_count - 2, going_right, going_left),
        outer_axis,
        [(tp_count - 2, tp_count - 1), (1, 0)],
    )
    far_part = times_weight(far)
    by_source = jnp.stack(
        [times_weight(hidden)]
        + [
            jnp.where(
                outer_at >= d,
                times_weight(from_left[d]) if d < tp_count - 1 else far_part,
                times_weight(from_right[tp_count - d]) if d > 1 else far_part,
            )
            if d != tp_count // 2
            else times_weight(jnp.where(outer_at >= d, from_left[d], from_right[d]))
            for d in range(1, tp_count)
        ]
    )

    def for_target(target):
        return lax.dynamic_index_in_dim(
            by_source, (outer_at - target + tp_count) % tp_count, 0, keepdims=False
        )

    held = {m: for_target(tp_at ^ m) for m in range(tp_count)}
    bit = 1
    while bit < tp_count:
        going = sorted(m for m in held if m & bit)
        sent = jnp.stack([held[m] for m in going])
        got = lax.ppermute(
            sent if bit == 1 else sent.astype(jnp.bfloat16),
            "tp",
            [(s, s ^ bit) for s in range(tp_count)],
        )
        held = {m: held[m] for m in held if not m & bit}
        for index, m in enumerate(going):
            held[m ^ bit] = held[m ^ bit] + got[index].astype(jnp.float32)
        bit *= 2
    swap = [(o * tp_count + t, t * tp_count + o) for o in range(tp_count) for t in range(tp_count)]
    rotated = lax.ppermute(held[0].astype(jnp.bfloat16), (outer_axis, "tp"), swap)
    width = out_weight.shape[1]
    pieces = jnp.stack([rotated[:, d * width : (d + 1) * width] for d in range(inner_count)])
    inner_at = lax.axis_index(inner_axis)
    return jnp.concatenate(
        [
            lax.dynamic_index_in_dim(
                pieces, (inner_at - place + inner_count) % inner_count, 0, keepdims=False
            )
            for place in range(inner_count)
        ],
        axis=1,
    )


def solution(mesh):
    ctx_count = mesh.shape["ctx"]
    tp_count = mesh.shape["tp"]
    if ctx_count % tp_count == 0 and tp_count == 4:
        inner = ctx_count // tp_count
        grid = mesh.devices.reshape(tp_count, inner, tp_count)
        mesh = jax.sharding.Mesh(grid, ("outer", "inner", "tp"))
        ctx_axes = ("outer", "inner")
        layout = (ctx_axes, ctx_count, "outer", "inner", tp_count)
    else:
        ctx_axes = "ctx"
        layout = (ctx_axes, ctx_count, None, None, tp_count)
    placed = (
        P(ctx_axes, "tp"),
        P(ctx_axes, "tp"),
        P(ctx_axes, "tp"),
        P(ctx_axes, "tp"),
        P(None, "tp"),
        P(None, "tp"),
        P(None, "tp"),
        P(ctx_axes, "tp"),
        P(ctx_axes, "tp"),
        P("tp"),
        P("tp"),
        P("tp", ctx_axes),
    )
    return jax.shard_map(
        functools.partial(on_device, layout),
        mesh=mesh,
        in_specs=placed,
        out_specs=P(ctx_axes, "tp"),
        check_vma=False,
    )
```

```python
import functools

import jax
import jax.numpy as jnp
from jax import lax
from jax.sharding import PartitionSpec as P

N = 128
BLOCK = 256


def shifted(value, axis, steps, count):
    first, last = (max(0, -steps), min(count, count - steps))
    return lax.ppermute(value, axis, [(source, source + steps) for source in range(first, last)])


def local_conv(packed, kernel, tok_rows):
    tail_len = kernel.shape[0] - 1
    padded = jnp.pad(packed.astype(jnp.float32), ((tail_len, 0), (0, 0)))
    pre_act = jnp.zeros((tok_rows, kernel.shape[1]), jnp.float32)
    for tap_index in range(kernel.shape[0]):
        pre_act = pre_act + kernel[tap_index] * padded[tap_index : tap_index + tok_rows]
    return pre_act


def edge_partial(tail_rows, kernel):
    tail_len = kernel.shape[0] - 1
    tail_vals = tail_rows.astype(jnp.float32)
    outputs = []
    for row_index in range(tail_len):
        accum = jnp.zeros((kernel.shape[1],), jnp.float32)
        for tap_index in range(tail_len - row_index):
            accum = accum + kernel[tap_index] * tail_vals[row_index + tap_index]
        outputs.append(accum)
    return jnp.stack(outputs, axis=0)


def intra_block(scaled, b_rows, c_rows, cum_log):
    scores = jnp.einsum("tgn,sgn->gts", c_rows, b_rows, preferred_element_type=jnp.float32)
    cum_cols = jnp.moveaxis(cum_log, 0, -1)
    log_gap = cum_cols[..., :, None] - cum_cols[..., None, :]
    block_len = cum_log.shape[0]
    causal = jnp.arange(block_len)[:, None] >= jnp.arange(block_len)[None, :]
    decays = jnp.exp(jnp.where(causal, log_gap, -jnp.inf))
    weights = (scores[:, None] * decays).astype(jnp.bfloat16)
    return jnp.einsum("gjts,sgjp->tgjp", weights, scaled, preferred_element_type=jnp.float32)


def block_state(scaled, b_rows, cum_log):
    end_decay = jnp.exp(cum_log[-1][None] - cum_log)
    b_weighted = (b_rows.astype(jnp.float32)[:, :, None, :] * end_decay[..., None]).astype(
        jnp.bfloat16
    )
    return jnp.einsum("sgjp,sgjn->gjpn", scaled, b_weighted, preferred_element_type=jnp.float32)


def inter_block(c_rows, cum_log, state_carry):
    rounded = state_carry.astype(jnp.bfloat16)
    inner = jnp.einsum("tgn,gjpn->tgjp", c_rows, rounded, preferred_element_type=jnp.float32)
    return inner * jnp.exp(cum_log)[..., None]


def combine(first_part, second_part):
    decay_first, state_first = first_part
    decay_second, state_second = second_part
    return (
        decay_first * decay_second,
        decay_second[..., None, None] * state_first.astype(jnp.float32) + state_second,
    )


def on_link(part):
    decay, state = part
    return (decay, state.astype(jnp.bfloat16))


def prefix_states(dev_decay, dev_state, axis, count):
    own = (dev_decay, dev_state)
    if count == 1:
        return jnp.zeros_like(dev_state)
    got = shifted(on_link(own), axis, 1, count)
    before = got
    upto = combine(got, own)
    step = 2
    while step < count:
        got = shifted(on_link(upto), axis, step, count)
        before = combine(got, before)
        if step * 2 < count:
            upto = combine(got, upto)
        step *= 2
    return before[1].astype(jnp.float32)


def on_device(
    layout,
    features,
    input_map,
    output_map,
    gate_in,
    conv_feat,
    conv_input,
    conv_output,
    step_size,
    log_decay,
    skip_gain,
    norm_gain,
    out_weight,
):
    tok_rows, width_x = features.shape
    width_b = input_map.shape[1]
    head_count = step_size.shape[1]
    head_dim = width_x // head_count
    groups_here = width_b // N
    per_group = head_count // groups_here
    tail_len = conv_feat.shape[0] - 1
    n_blocks = tok_rows // BLOCK
    packed = jnp.concatenate([features, input_map, output_map], axis=1)
    kernel = jnp.concatenate([conv_feat, conv_input, conv_output], axis=1)
    pre_act = local_conv(packed, kernel, tok_rows)
    ctx_axes, ctx_count, outer_axis, inner_axis, tp_count = layout
    tail_rows = shifted(packed[tok_rows - tail_len :], ctx_axes, 1, ctx_count)
    edge_sums = edge_partial(tail_rows, kernel)
    pre_act = pre_act + jnp.pad(edge_sums, ((0, tok_rows - tail_len), (0, 0)))
    conv_out = jax.nn.silu(pre_act).astype(jnp.bfloat16)
    x_conv = conv_out[:, :width_x]
    b_conv = conv_out[:, width_x : width_x + width_b]
    c_conv = conv_out[:, width_x + width_b :]
    x_heads = x_conv.astype(jnp.float32).reshape(tok_rows, groups_here, per_group, head_dim)
    scaled = (x_heads * step_size.reshape(tok_rows, groups_here, per_group)[..., None]).astype(
        jnp.bfloat16
    )

    def blocked(value_entries):
        return value_entries.reshape((n_blocks, BLOCK) + value_entries.shape[1:])

    scaled_b = blocked(scaled)
    b_rows = blocked(b_conv.reshape(tok_rows, groups_here, N))
    c_rows = blocked(c_conv.reshape(tok_rows, groups_here, N))
    cum_log = jnp.cumsum(blocked(log_decay.reshape(tok_rows, groups_here, per_group)), axis=1)
    blk_states = jax.vmap(block_state)(scaled_b, b_rows, cum_log)
    blk_decay = jnp.exp(cum_log[:, -1])

    def fold_local(state_carry, block_in):
        decay_b, state_b = block_in
        return (decay_b[..., None, None] * state_carry + state_b, None)

    dev_state, _ = lax.scan(
        fold_local, jnp.zeros(blk_states.shape[1:], jnp.float32), (blk_decay, blk_states)
    )
    dev_decay = jnp.prod(blk_decay, axis=0)
    if outer_axis is not None:
        inner_count = ctx_count // tp_count
        split = out_weight.shape[1] // 4
        early, late = [], []
        for d in range(1, inner_count):
            pairs = [(s, (s + d) % inner_count) for s in range(inner_count)]
            early.append(lax.ppermute(out_weight[:, :split], inner_axis, pairs))
            late.append(lax.ppermute(out_weight[:, split:], inner_axis, pairs))
        early, dev_state = lax.optimization_barrier((early, dev_state))
        weight_pieces = [out_weight]
        for first, second in zip(early, late):
            weight_pieces += [first, second]
    incoming = prefix_states(dev_decay, dev_state, ctx_axes, ctx_count)

    def advance(state_carry, block_in):
        scaled_k, b_k, c_k, cum_k, decay_k, state_k = block_in
        block_y = intra_block(scaled_k, b_k, c_k, cum_k) + inter_block(c_k, cum_k, state_carry)
        return (decay_k[..., None, None] * state_carry + state_k, block_y)

    _, ssm_y = lax.scan(
        advance, incoming, (scaled_b, b_rows, c_rows, cum_log, blk_decay, blk_states)
    )
    mixed_y = ssm_y.reshape(tok_rows, groups_here, per_group, head_dim)
    mixed_y = mixed_y + skip_gain.reshape(groups_here, per_group)[..., None] * x_heads
    gated_y = mixed_y.reshape(tok_rows, width_x) * jax.nn.silu(gate_in.astype(jnp.float32))
    grouped = gated_y.reshape(tok_rows, groups_here, width_x // groups_here)
    inv_root = lax.rsqrt(jnp.mean(grouped * grouped, axis=-1, keepdims=True) + 1e-05)
    hidden = ((grouped * inv_root).reshape(tok_rows, width_x) * norm_gain).astype(jnp.bfloat16)
    if outer_axis is None:
        partial_out = jnp.dot(
            hidden,
            lax.all_gather(out_weight, ctx_axes, axis=1, tiled=True),
            preferred_element_type=jnp.float32,
        )
        return lax.psum_scatter(partial_out, "tp", scatter_dimension=1, tiled=True).astype(
            jnp.bfloat16
        )
    outer_at = lax.axis_index(outer_axis)
    tp_at = lax.axis_index("tp")
    inner_count = ctx_count // tp_count
    weight_pieces, hidden = lax.optimization_barrier((weight_pieces, hidden))
    def times_weight(rows):
        return jnp.concatenate(
            [jnp.dot(rows, piece, preferred_element_type=jnp.float32) for piece in weight_pieces],
            axis=1,
        )

    from_left, from_right = {}, {}
    going_right = going_left = hidden
    for step in range(1, tp_count - 1):
        going_right = lax.ppermute(
            going_right, outer_axis, [(s, s + 1) for s in range(step - 1, tp_count - 1)]
        )
        going_left = lax.ppermute(
            going_left, outer_axis, [(s, s - 1) for s in range(1, tp_count - step + 1)]
        )
        from_left[step], from_right[step] = going_right, going_left
    far = lax.ppermute(
        jnp.where(outer_at == tp_count - 2, going_right, going_left),
        outer_axis,
        [(tp_count - 2, tp_count - 1), (1, 0)],
    )
    far_part = times_weight(far)
    by_source = jnp.stack(
        [times_weight(hidden)]
        + [
            jnp.where(
                outer_at >= d,
                times_weight(from_left[d]) if d < tp_count - 1 else far_part,
                times_weight(from_right[tp_count - d]) if d > 1 else far_part,
            )
            if d != tp_count // 2
            else times_weight(jnp.where(outer_at >= d, from_left[d], from_right[d]))
            for d in range(1, tp_count)
        ]
    )

    def for_target(target):
        return lax.dynamic_index_in_dim(
            by_source, (outer_at - target + tp_count) % tp_count, 0, keepdims=False
        )

    held = {m: for_target(tp_at ^ m) for m in range(tp_count)}
    bit = 1
    while bit < tp_count:
        going = sorted(m for m in held if m & bit)
        sent = jnp.stack([held[m] for m in going])
        got = lax.ppermute(
            sent if bit == 1 else sent.astype(jnp.bfloat16),
            "tp",
            [(s, s ^ bit) for s in range(tp_count)],
        )
        held = {m: held[m] for m in held if not m & bit}
        for index, m in enumerate(going):
            held[m ^ bit] = held[m ^ bit] + got[index].astype(jnp.float32)
        bit *= 2
    swap = [(o * tp_count + t, t * tp_count + o) for o in range(tp_count) for t in range(tp_count)]
    rotated = lax.ppermute(held[0].astype(jnp.bfloat16), (outer_axis, "tp"), swap)
    width = out_weight.shape[1]
    pieces = jnp.stack([rotated[:, d * width : (d + 1) * width] for d in range(inner_count)])
    inner_at = lax.axis_index(inner_axis)
    return jnp.concatenate(
        [
            lax.dynamic_index_in_dim(
                pieces, (inner_at - place + inner_count) % inner_count, 0, keepdims=False
            )
            for place in range(inner_count)
        ],
        axis=1,
    )


def solution(mesh):
    ctx_count = mesh.shape["ctx"]
    tp_count = mesh.shape["tp"]
    if ctx_count % tp_count == 0 and tp_count == 4:
        inner = ctx_count // tp_count
        grid = mesh.devices.reshape(tp_count, inner, tp_count)
        mesh = jax.sharding.Mesh(grid, ("outer", "inner", "tp"))
        ctx_axes = ("outer", "inner")
        layout = (ctx_axes, ctx_count, "outer", "inner", tp_count)
    else:
        ctx_axes = "ctx"
        layout = (ctx_axes, ctx_count, None, None, tp_count)
    placed = (
        P(ctx_axes, "tp"),
        P(ctx_axes, "tp"),
        P(ctx_axes, "tp"),
        P(ctx_axes, "tp"),
        P(None, "tp"),
        P(None, "tp"),
        P(None, "tp"),
        P(ctx_axes, "tp"),
        P(ctx_axes, "tp"),
        P("tp"),
        P("tp"),
        P("tp", ctx_axes),
    )
    return jax.shard_map(
        functools.partial(on_device, layout),
        mesh=mesh,
        in_specs=placed,
        out_specs=P(ctx_axes, "tp"),
        check_vma=False,
    )
```

```python
import functools

import jax
import jax.numpy as jnp
from jax import lax
from jax.sharding import PartitionSpec as P

N = 128
BLOCK = 256


def shifted(value, axis, steps, count):
    first, last = (max(0, -steps), min(count, count - steps))
    return lax.ppermute(value, axis, [(source, source + steps) for source in range(first, last)])


def local_conv(packed, kernel, tok_rows):
    tail_len = kernel.shape[0] - 1
    padded = jnp.pad(packed.astype(jnp.float32), ((tail_len, 0), (0, 0)))
    pre_act = jnp.zeros((tok_rows, kernel.shape[1]), jnp.float32)
    for tap_index in range(kernel.shape[0]):
        pre_act = pre_act + kernel[tap_index] * padded[tap_index : tap_index + tok_rows]
    return pre_act


def edge_partial(tail_rows, kernel):
    tail_len = kernel.shape[0] - 1
    tail_vals = tail_rows.astype(jnp.float32)
    outputs = []
    for row_index in range(tail_len):
        accum = jnp.zeros((kernel.shape[1],), jnp.float32)
        for tap_index in range(tail_len - row_index):
            accum = accum + kernel[tap_index] * tail_vals[row_index + tap_index]
        outputs.append(accum)
    return jnp.stack(outputs, axis=0)


def intra_block(scaled, b_rows, c_rows, cum_log):
    scores = jnp.einsum("tgn,sgn->gts", c_rows, b_rows, preferred_element_type=jnp.float32)
    cum_cols = jnp.moveaxis(cum_log, 0, -1)
    log_gap = cum_cols[..., :, None] - cum_cols[..., None, :]
    block_len = cum_log.shape[0]
    causal = jnp.arange(block_len)[:, None] >= jnp.arange(block_len)[None, :]
    decays = jnp.exp(jnp.where(causal, log_gap, -jnp.inf))
    weights = (scores[:, None] * decays).astype(jnp.bfloat16)
    return jnp.einsum("gjts,sgjp->tgjp", weights, scaled, preferred_element_type=jnp.float32)


def block_state(scaled, b_rows, cum_log):
    end_decay = jnp.exp(cum_log[-1][None] - cum_log)
    b_weighted = (b_rows.astype(jnp.float32)[:, :, None, :] * end_decay[..., None]).astype(
        jnp.bfloat16
    )
    return jnp.einsum("sgjp,sgjn->gjpn", scaled, b_weighted, preferred_element_type=jnp.float32)


def inter_block(c_rows, cum_log, state_carry):
    rounded = state_carry.astype(jnp.bfloat16)
    inner = jnp.einsum("tgn,gjpn->tgjp", c_rows, rounded, preferred_element_type=jnp.float32)
    return inner * jnp.exp(cum_log)[..., None]


def combine(first_part, second_part):
    decay_first, state_first = first_part
    decay_second, state_second = second_part
    return (
        decay_first * decay_second,
        decay_second[..., None, None] * state_first.astype(jnp.float32) + state_second,
    )


def on_link(part):
    decay, state = part
    return (decay, state.astype(jnp.bfloat16))


def prefix_states(dev_decay, dev_state, axis, count):
    own = (dev_decay, dev_state)
    if count == 1:
        return jnp.zeros_like(dev_state)
    got = shifted(on_link(own), axis, 1, count)
    before = got
    upto = combine(got, own)
    step = 2
    while step < count:
        got = shifted(on_link(upto), axis, step, count)
        before = combine(got, before)
        if step * 2 < count:
            upto = combine(got, upto)
        step *= 2
    return before[1].astype(jnp.float32)


def on_device(
    layout,
    features,
    input_map,
    output_map,
    gate_in,
    conv_feat,
    conv_input,
    conv_output,
    step_size,
    log_decay,
    skip_gain,
    norm_gain,
    out_weight,
):
    tok_rows, width_x = features.shape
    width_b = input_map.shape[1]
    head_count = step_size.shape[1]
    head_dim = width_x // head_count
    groups_here = width_b // N
    per_group = head_count // groups_here
    tail_len = conv_feat.shape[0] - 1
    n_blocks = tok_rows // BLOCK
    packed = jnp.concatenate([features, input_map, output_map], axis=1)
    kernel = jnp.concatenate([conv_feat, conv_input, conv_output], axis=1)
    pre_act = local_conv(packed, kernel, tok_rows)
    ctx_axes, ctx_count, outer_axis, inner_axis, tp_count = layout
    tail_rows = shifted(packed[tok_rows - tail_len :], ctx_axes, 1, ctx_count)
    edge_sums = edge_partial(tail_rows, kernel)
    pre_act = pre_act + jnp.pad(edge_sums, ((0, tok_rows - tail_len), (0, 0)))
    conv_out = jax.nn.silu(pre_act).astype(jnp.bfloat16)
    x_conv = conv_out[:, :width_x]
    b_conv = conv_out[:, width_x : width_x + width_b]
    c_conv = conv_out[:, width_x + width_b :]
    x_heads = x_conv.astype(jnp.float32).reshape(tok_rows, groups_here, per_group, head_dim)
    scaled = (x_heads * step_size.reshape(tok_rows, groups_here, per_group)[..., None]).astype(
        jnp.bfloat16
    )

    def blocked(value_entries):
        return value_entries.reshape((n_blocks, BLOCK) + value_entries.shape[1:])

    scaled_b = blocked(scaled)
    b_rows = blocked(b_conv.reshape(tok_rows, groups_here, N))
    c_rows = blocked(c_conv.reshape(tok_rows, groups_here, N))
    cum_log = jnp.cumsum(blocked(log_decay.reshape(tok_rows, groups_here, per_group)), axis=1)
    blk_states = jax.vmap(block_state)(scaled_b, b_rows, cum_log)
    blk_decay = jnp.exp(cum_log[:, -1])

    def fold_local(state_carry, block_in):
        decay_b, state_b = block_in
        return (decay_b[..., None, None] * state_carry + state_b, None)

    dev_state, _ = lax.scan(
        fold_local, jnp.zeros(blk_states.shape[1:], jnp.float32), (blk_decay, blk_states)
    )
    dev_decay = jnp.prod(blk_decay, axis=0)
    incoming = prefix_states(dev_decay, dev_state, ctx_axes, ctx_count)

    def advance(state_carry, block_in):
        scaled_k, b_k, c_k, cum_k, decay_k, state_k = block_in
        block_y = intra_block(scaled_k, b_k, c_k, cum_k) + inter_block(c_k, cum_k, state_carry)
        return (decay_k[..., None, None] * state_carry + state_k, block_y)

    _, ssm_y = lax.scan(
        advance, incoming, (scaled_b, b_rows, c_rows, cum_log, blk_decay, blk_states)
    )
    mixed_y = ssm_y.reshape(tok_rows, groups_here, per_group, head_dim)
    mixed_y = mixed_y + skip_gain.reshape(groups_here, per_group)[..., None] * x_heads
    gated_y = mixed_y.reshape(tok_rows, width_x) * jax.nn.silu(gate_in.astype(jnp.float32))
    grouped = gated_y.reshape(tok_rows, groups_here, width_x // groups_here)
    inv_root = lax.rsqrt(jnp.mean(grouped * grouped, axis=-1, keepdims=True) + 1e-05)
    hidden = ((grouped * inv_root).reshape(tok_rows, width_x) * norm_gain).astype(jnp.bfloat16)
    if outer_axis is None:
        partial_out = jnp.dot(
            hidden,
            lax.all_gather(out_weight, ctx_axes, axis=1, tiled=True),
            preferred_element_type=jnp.float32,
        )
        return lax.psum_scatter(partial_out, "tp", scatter_dimension=1, tiled=True).astype(
            jnp.bfloat16
        )
    outer_at = lax.axis_index(outer_axis)
    tp_at = lax.axis_index("tp")
    inner_count = ctx_count // tp_count
    weight_pieces = [out_weight] + [
        lax.ppermute(
            out_weight, inner_axis, [(s, (s + d) % inner_count) for s in range(inner_count)]
        )
        for d in range(1, inner_count)
    ]
    weight_pieces, hidden = lax.optimization_barrier((weight_pieces, hidden))
    def times_weight(rows):
        return jnp.concatenate(
            [jnp.dot(rows, piece, preferred_element_type=jnp.float32) for piece in weight_pieces],
            axis=1,
        )

    from_left, from_right = {}, {}
    going_right = going_left = hidden
    for step in range(1, tp_count - 1):
        going_right = lax.ppermute(
            going_right, outer_axis, [(s, s + 1) for s in range(step - 1, tp_count - 1)]
        )
        going_left = lax.ppermute(
            going_left, outer_axis, [(s, s - 1) for s in range(1, tp_count - step + 1)]
        )
        from_left[step], from_right[step] = going_right, going_left
    far = lax.ppermute(
        jnp.where(outer_at == tp_count - 2, going_right, going_left),
        outer_axis,
        [(tp_count - 2, tp_count - 1), (1, 0)],
    )
    far_part = times_weight(far)
    by_source = (
        [times_weight(hidden)]
        + [
            jnp.where(
                outer_at >= d,
                times_weight(from_left[d]) if d < tp_count - 1 else far_part,
                times_weight(from_right[tp_count - d]) if d > 1 else far_part,
            )
            if d != tp_count // 2
            else times_weight(jnp.where(outer_at >= d, from_left[d], from_right[d]))
            for d in range(1, tp_count)
        ]
    )

    def for_target(target):
        return lax.select_n(
            ((outer_at - target + tp_count) % tp_count).astype(jnp.int32), *by_source
        )

    held = {m: for_target(tp_at ^ m) for m in range(tp_count)}
    bit = 1
    while bit < tp_count:
        going = sorted(m for m in held if m & bit)
        sent = jnp.stack([held[m] for m in going])
        got = lax.ppermute(
            sent if bit == 1 else sent.astype(jnp.bfloat16),
            "tp",
            [(s, s ^ bit) for s in range(tp_count)],
        )
        held = {m: held[m] for m in held if not m & bit}
        for index, m in enumerate(going):
            held[m ^ bit] = held[m ^ bit] + got[index].astype(jnp.float32)
        bit *= 2
    swap = [(o * tp_count + t, t * tp_count + o) for o in range(tp_count) for t in range(tp_count)]
    rotated = lax.ppermute(held[0].astype(jnp.bfloat16), (outer_axis, "tp"), swap)
    width = out_weight.shape[1]
    pieces = jnp.stack([rotated[:, d * width : (d + 1) * width] for d in range(inner_count)])
    inner_at = lax.axis_index(inner_axis)
    return jnp.concatenate(
        [
            lax.dynamic_index_in_dim(
                pieces, (inner_at - place + inner_count) % inner_count, 0, keepdims=False
            )
            for place in range(inner_count)
        ],
        axis=1,
    )


def solution(mesh):
    ctx_count = mesh.shape["ctx"]
    tp_count = mesh.shape["tp"]
    if ctx_count % tp_count == 0 and tp_count == 4:
        inner = ctx_count // tp_count
        grid = mesh.devices.reshape(tp_count, inner, tp_count)
        mesh = jax.sharding.Mesh(grid, ("outer", "inner", "tp"))
        ctx_axes = ("outer", "inner")
        layout = (ctx_axes, ctx_count, "outer", "inner", tp_count)
    else:
        ctx_axes = "ctx"
        layout = (ctx_axes, ctx_count, None, None, tp_count)
    placed = (
        P(ctx_axes, "tp"),
        P(ctx_axes, "tp"),
        P(ctx_axes, "tp"),
        P(ctx_axes, "tp"),
        P(None, "tp"),
        P(None, "tp"),
        P(None, "tp"),
        P(ctx_axes, "tp"),
        P(ctx_axes, "tp"),
        P("tp"),
        P("tp"),
        P("tp", ctx_axes),
    )
    return jax.shard_map(
        functools.partial(on_device, layout),
        mesh=mesh,
        in_specs=placed,
        out_specs=P(ctx_axes, "tp"),
        check_vma=False,
    )
```

```python
import functools

import jax
import jax.numpy as jnp
from jax import lax
from jax.sharding import PartitionSpec as P

N = 128
BLOCK = 256


def shifted(value, axis, steps, count):
    first, last = (max(0, -steps), min(count, count - steps))
    return lax.ppermute(value, axis, [(source, source + steps) for source in range(first, last)])


def local_conv(packed, kernel, tok_rows):
    tail_len = kernel.shape[0] - 1
    padded = jnp.pad(packed.astype(jnp.float32), ((tail_len, 0), (0, 0)))
    pre_act = jnp.zeros((tok_rows, kernel.shape[1]), jnp.float32)
    for tap_index in range(kernel.shape[0]):
        pre_act = pre_act + kernel[tap_index] * padded[tap_index : tap_index + tok_rows]
    return pre_act


def edge_partial(tail_rows, kernel):
    tail_len = kernel.shape[0] - 1
    tail_vals = tail_rows.astype(jnp.float32)
    outputs = []
    for row_index in range(tail_len):
        accum = jnp.zeros((kernel.shape[1],), jnp.float32)
        for tap_index in range(tail_len - row_index):
            accum = accum + kernel[tap_index] * tail_vals[row_index + tap_index]
        outputs.append(accum)
    return jnp.stack(outputs, axis=0)


def intra_block(scaled, b_rows, c_rows, cum_log):
    scores = jnp.einsum("tgn,sgn->gts", c_rows, b_rows, preferred_element_type=jnp.float32)
    cum_cols = jnp.moveaxis(cum_log, 0, -1)
    log_gap = cum_cols[..., :, None] - cum_cols[..., None, :]
    block_len = cum_log.shape[0]
    causal = jnp.arange(block_len)[:, None] >= jnp.arange(block_len)[None, :]
    decays = jnp.exp(jnp.where(causal, log_gap, -jnp.inf))
    weights = (scores[:, None] * decays).astype(jnp.bfloat16)
    return jnp.einsum("gjts,sgjp->tgjp", weights, scaled, preferred_element_type=jnp.float32)


def block_state(scaled, b_rows, cum_log):
    end_decay = jnp.exp(cum_log[-1][None] - cum_log)
    b_weighted = (b_rows.astype(jnp.float32)[:, :, None, :] * end_decay[..., None]).astype(
        jnp.bfloat16
    )
    return jnp.einsum("sgjp,sgjn->gjpn", scaled, b_weighted, preferred_element_type=jnp.float32)


def inter_block(c_rows, cum_log, state_carry):
    rounded = state_carry.astype(jnp.bfloat16)
    inner = jnp.einsum("tgn,gjpn->tgjp", c_rows, rounded, preferred_element_type=jnp.float32)
    return inner * jnp.exp(cum_log)[..., None]


def combine(first_part, second_part):
    decay_first, state_first = first_part
    decay_second, state_second = second_part
    return (
        decay_first * decay_second,
        decay_second[..., None, None] * state_first.astype(jnp.float32) + state_second,
    )


def on_link(part):
    decay, state = part
    return (decay, state.astype(jnp.bfloat16))


def prefix_states(dev_decay, dev_state, axis, count):
    own = (dev_decay, dev_state)
    if count == 1:
        return jnp.zeros_like(dev_state)
    got = shifted(on_link(own), axis, 1, count)
    before = got
    upto = combine(got, own)
    step = 2
    while step < count:
        got = shifted(on_link(upto), axis, step, count)
        before = combine(got, before)
        if step * 2 < count:
            upto = combine(got, upto)
        step *= 2
    return before[1].astype(jnp.float32)


def on_device(
    layout,
    features,
    input_map,
    output_map,
    gate_in,
    conv_feat,
    conv_input,
    conv_output,
    step_size,
    log_decay,
    skip_gain,
    norm_gain,
    out_weight,
):
    tok_rows, width_x = features.shape
    width_b = input_map.shape[1]
    head_count = step_size.shape[1]
    head_dim = width_x // head_count
    groups_here = width_b // N
    per_group = head_count // groups_here
    tail_len = conv_feat.shape[0] - 1
    n_blocks = tok_rows // BLOCK
    packed = jnp.concatenate([features, input_map, output_map], axis=1)
    kernel = jnp.concatenate([conv_feat, conv_input, conv_output], axis=1)
    pre_act = local_conv(packed, kernel, tok_rows)
    ctx_axes, ctx_count, outer_axis, inner_axis, tp_count = layout
    tail_rows = shifted(packed[tok_rows - tail_len :], ctx_axes, 1, ctx_count)
    edge_sums = edge_partial(tail_rows, kernel)
    pre_act = pre_act + jnp.pad(edge_sums, ((0, tok_rows - tail_len), (0, 0)))
    conv_out = jax.nn.silu(pre_act).astype(jnp.bfloat16)
    x_conv = conv_out[:, :width_x]
    b_conv = conv_out[:, width_x : width_x + width_b]
    c_conv = conv_out[:, width_x + width_b :]
    x_heads = x_conv.astype(jnp.float32).reshape(tok_rows, groups_here, per_group, head_dim)
    scaled = (x_heads * step_size.reshape(tok_rows, groups_here, per_group)[..., None]).astype(
        jnp.bfloat16
    )

    def blocked(value_entries):
        return value_entries.reshape((n_blocks, BLOCK) + value_entries.shape[1:])

    scaled_b = blocked(scaled)
    b_rows = blocked(b_conv.reshape(tok_rows, groups_here, N))
    c_rows = blocked(c_conv.reshape(tok_rows, groups_here, N))
    cum_log = jnp.cumsum(blocked(log_decay.reshape(tok_rows, groups_here, per_group)), axis=1)
    blk_states = jax.vmap(block_state)(scaled_b, b_rows, cum_log)
    blk_decay = jnp.exp(cum_log[:, -1])

    def fold_local(state_carry, block_in):
        decay_b, state_b = block_in
        return (decay_b[..., None, None] * state_carry + state_b, None)

    dev_state, _ = lax.scan(
        fold_local, jnp.zeros(blk_states.shape[1:], jnp.float32), (blk_decay, blk_states)
    )
    dev_decay = jnp.prod(blk_decay, axis=0)
    incoming = prefix_states(dev_decay, dev_state, ctx_axes, ctx_count)

    def advance(state_carry, block_in):
        scaled_k, b_k, c_k, cum_k, decay_k, state_k = block_in
        block_y = intra_block(scaled_k, b_k, c_k, cum_k) + inter_block(c_k, cum_k, state_carry)
        return (decay_k[..., None, None] * state_carry + state_k, block_y)

    _, ssm_y = lax.scan(
        advance, incoming, (scaled_b, b_rows, c_rows, cum_log, blk_decay, blk_states)
    )
    mixed_y = ssm_y.reshape(tok_rows, groups_here, per_group, head_dim)
    mixed_y = mixed_y + skip_gain.reshape(groups_here, per_group)[..., None] * x_heads
    gated_y = mixed_y.reshape(tok_rows, width_x) * jax.nn.silu(gate_in.astype(jnp.float32))
    grouped = gated_y.reshape(tok_rows, groups_here, width_x // groups_here)
    inv_root = lax.rsqrt(jnp.mean(grouped * grouped, axis=-1, keepdims=True) + 1e-05)
    hidden = ((grouped * inv_root).reshape(tok_rows, width_x) * norm_gain).astype(jnp.bfloat16)
    if outer_axis is None:
        partial_out = jnp.dot(
            hidden,
            lax.all_gather(out_weight, ctx_axes, axis=1, tiled=True),
            preferred_element_type=jnp.float32,
        )
        return lax.psum_scatter(partial_out, "tp", scatter_dimension=1, tiled=True).astype(
            jnp.bfloat16
        )
    outer_at = lax.axis_index(outer_axis)
    tp_at = lax.axis_index("tp")
    inner_count = ctx_count // tp_count
    weight_pieces = [out_weight] + [
        lax.ppermute(
            out_weight, inner_axis, [(s, (s + d) % inner_count) for s in range(inner_count)]
        )
        for d in range(1, inner_count)
    ]
    weight_pieces, hidden = lax.optimization_barrier((weight_pieces, hidden))
    def times_weight(rows):
        return jnp.concatenate(
            [jnp.dot(rows, piece, preferred_element_type=jnp.float32) for piece in weight_pieces],
            axis=1,
        )

    from_left, from_right = {}, {}
    going_right = going_left = hidden
    for step in range(1, tp_count - 1):
        going_right = lax.ppermute(
            going_right, outer_axis, [(s, s + 1) for s in range(step - 1, tp_count - 1)]
        )
        going_left = lax.ppermute(
            going_left, outer_axis, [(s, s - 1) for s in range(1, tp_count - step + 1)]
        )
        from_left[step], from_right[step] = going_right, going_left
    far = lax.ppermute(
        jnp.where(outer_at == tp_count - 2, going_right, going_left),
        outer_axis,
        [(tp_count - 2, tp_count - 1), (1, 0)],
    )
    far_part = times_weight(far)
    by_source = jnp.stack(
        [times_weight(hidden)]
        + [
            jnp.where(
                outer_at >= d,
                times_weight(from_left[d]) if d < tp_count - 1 else far_part,
                times_weight(from_right[tp_count - d]) if d > 1 else far_part,
            )
            if d != tp_count // 2
            else times_weight(jnp.where(outer_at >= d, from_left[d], from_right[d]))
            for d in range(1, tp_count)
        ]
    )

    def for_target(target):
        return lax.dynamic_index_in_dim(
            by_source, (outer_at - target + tp_count) % tp_count, 0, keepdims=False
        )

    held = {m: for_target(tp_at ^ m) for m in range(tp_count)}
    bit = 1
    while bit < tp_count:
        going = sorted(m for m in held if m & bit)
        sent = jnp.stack([held[m] for m in going])
        got = lax.ppermute(
            sent.astype(jnp.bfloat16),
            "tp",
            [(s, s ^ bit) for s in range(tp_count)],
        )
        held = {m: held[m] for m in held if not m & bit}
        for index, m in enumerate(going):
            held[m ^ bit] = held[m ^ bit] + got[index].astype(jnp.float32)
        bit *= 2
    swap = [(o * tp_count + t, t * tp_count + o) for o in range(tp_count) for t in range(tp_count)]
    rotated = lax.ppermute(held[0].astype(jnp.bfloat16), (outer_axis, "tp"), swap)
    width = out_weight.shape[1]
    pieces = jnp.stack([rotated[:, d * width : (d + 1) * width] for d in range(inner_count)])
    inner_at = lax.axis_index(inner_axis)
    return jnp.concatenate(
        [
            lax.dynamic_index_in_dim(
                pieces, (inner_at - place + inner_count) % inner_count, 0, keepdims=False
            )
            for place in range(inner_count)
        ],
        axis=1,
    )


def solution(mesh):
    ctx_count = mesh.shape["ctx"]
    tp_count = mesh.shape["tp"]
    if ctx_count % tp_count == 0 and tp_count == 4:
        inner = ctx_count // tp_count
        grid = mesh.devices.reshape(tp_count, inner, tp_count)
        mesh = jax.sharding.Mesh(grid, ("outer", "inner", "tp"))
        ctx_axes = ("outer", "inner")
        layout = (ctx_axes, ctx_count, "outer", "inner", tp_count)
    else:
        ctx_axes = "ctx"
        layout = (ctx_axes, ctx_count, None, None, tp_count)
    placed = (
        P(ctx_axes, "tp"),
        P(ctx_axes, "tp"),
        P(ctx_axes, "tp"),
        P(ctx_axes, "tp"),
        P(None, "tp"),
        P(None, "tp"),
        P(None, "tp"),
        P(ctx_axes, "tp"),
        P(ctx_axes, "tp"),
        P("tp"),
        P("tp"),
        P("tp", ctx_axes),
    )
    return jax.shard_map(
        functools.partial(on_device, layout),
        mesh=mesh,
        in_specs=placed,
        out_specs=P(ctx_axes, "tp"),
        check_vma=False,
    )
```

```python
import functools

import jax
import jax.numpy as jnp
from jax import lax
from jax.sharding import PartitionSpec as P

N = 128
BLOCK = 256


def shifted(value, axis, steps, count):
    first, last = (max(0, -steps), min(count, count - steps))
    return lax.ppermute(value, axis, [(source, source + steps) for source in range(first, last)])


def local_conv(packed, kernel, tok_rows):
    tail_len = kernel.shape[0] - 1
    padded = jnp.pad(packed.astype(jnp.float32), ((tail_len, 0), (0, 0)))
    pre_act = jnp.zeros((tok_rows, kernel.shape[1]), jnp.float32)
    for tap_index in range(kernel.shape[0]):
        pre_act = pre_act + kernel[tap_index] * padded[tap_index : tap_index + tok_rows]
    return pre_act


def edge_partial(tail_rows, kernel):
    tail_len = kernel.shape[0] - 1
    tail_vals = tail_rows.astype(jnp.float32)
    outputs = []
    for row_index in range(tail_len):
        accum = jnp.zeros((kernel.shape[1],), jnp.float32)
        for tap_index in range(tail_len - row_index):
            accum = accum + kernel[tap_index] * tail_vals[row_index + tap_index]
        outputs.append(accum)
    return jnp.stack(outputs, axis=0)


def intra_block(scaled, b_rows, c_rows, cum_log):
    scores = jnp.einsum("tgn,sgn->gts", c_rows, b_rows, preferred_element_type=jnp.float32)
    cum_cols = jnp.moveaxis(cum_log, 0, -1)
    log_gap = cum_cols[..., :, None] - cum_cols[..., None, :]
    block_len = cum_log.shape[0]
    causal = jnp.arange(block_len)[:, None] >= jnp.arange(block_len)[None, :]
    decays = jnp.exp(jnp.where(causal, log_gap, -jnp.inf))
    weights = (scores[:, None] * decays).astype(jnp.bfloat16)
    return jnp.einsum("gjts,sgjp->tgjp", weights, scaled, preferred_element_type=jnp.float32)


def block_state(scaled, b_rows, cum_log):
    end_decay = jnp.exp(cum_log[-1][None] - cum_log)
    b_weighted = (b_rows.astype(jnp.float32)[:, :, None, :] * end_decay[..., None]).astype(
        jnp.bfloat16
    )
    return jnp.einsum("sgjp,sgjn->gjpn", scaled, b_weighted, preferred_element_type=jnp.float32)


def inter_block(c_rows, cum_log, state_carry):
    rounded = state_carry.astype(jnp.bfloat16)
    inner = jnp.einsum("tgn,gjpn->tgjp", c_rows, rounded, preferred_element_type=jnp.float32)
    return inner * jnp.exp(cum_log)[..., None]


def combine(first_part, second_part):
    decay_first, state_first = first_part
    decay_second, state_second = second_part
    return (
        decay_first * decay_second,
        decay_second[..., None, None] * state_first.astype(jnp.float32) + state_second,
    )


def on_link(part):
    decay, state = part
    return (decay, state.astype(jnp.bfloat16))


def prefix_states(dev_decay, dev_state, axis, count):
    own = (dev_decay, dev_state)
    if count == 1:
        return jnp.zeros_like(dev_state)
    got = shifted(on_link(own), axis, 1, count)
    before = got
    upto = combine(got, own)
    step = 2
    while step < count:
        got = shifted(on_link(upto), axis, step, count)
        before = combine(got, before)
        if step * 2 < count:
            upto = combine(got, upto)
        step *= 2
    return before[1].astype(jnp.float32)


def on_device(
    layout,
    features,
    input_map,
    output_map,
    gate_in,
    conv_feat,
    conv_input,
    conv_output,
    step_size,
    log_decay,
    skip_gain,
    norm_gain,
    out_weight,
):
    tok_rows, width_x = features.shape
    width_b = input_map.shape[1]
    head_count = step_size.shape[1]
    head_dim = width_x // head_count
    groups_here = width_b // N
    per_group = head_count // groups_here
    tail_len = conv_feat.shape[0] - 1
    n_blocks = tok_rows // BLOCK
    packed = jnp.concatenate([features, input_map, output_map], axis=1)
    kernel = jnp.concatenate([conv_feat, conv_input, conv_output], axis=1)
    pre_act = local_conv(packed, kernel, tok_rows)
    ctx_axes, ctx_count, outer_axis, inner_axis, tp_count = layout
    tail_rows = shifted(packed[tok_rows - tail_len :], ctx_axes, 1, ctx_count)
    edge_sums = edge_partial(tail_rows, kernel)
    pre_act = pre_act + jnp.pad(edge_sums, ((0, tok_rows - tail_len), (0, 0)))
    conv_out = jax.nn.silu(pre_act).astype(jnp.bfloat16)
    x_conv = conv_out[:, :width_x]
    b_conv = conv_out[:, width_x : width_x + width_b]
    c_conv = conv_out[:, width_x + width_b :]
    x_heads = x_conv.astype(jnp.float32).reshape(tok_rows, groups_here, per_group, head_dim)
    scaled = (x_heads * step_size.reshape(tok_rows, groups_here, per_group)[..., None]).astype(
        jnp.bfloat16
    )

    def blocked(value_entries):
        return value_entries.reshape((n_blocks, BLOCK) + value_entries.shape[1:])

    scaled_b = blocked(scaled)
    b_rows = blocked(b_conv.reshape(tok_rows, groups_here, N))
    c_rows = blocked(c_conv.reshape(tok_rows, groups_here, N))
    cum_log = jnp.cumsum(blocked(log_decay.reshape(tok_rows, groups_here, per_group)), axis=1)
    blk_states = jax.vmap(block_state)(scaled_b, b_rows, cum_log)
    blk_decay = jnp.exp(cum_log[:, -1])

    def fold_local(state_carry, block_in):
        decay_b, state_b = block_in
        return (decay_b[..., None, None] * state_carry + state_b, None)

    dev_state, _ = lax.scan(
        fold_local, jnp.zeros(blk_states.shape[1:], jnp.float32), (blk_decay, blk_states)
    )
    dev_decay = jnp.prod(blk_decay, axis=0)
    incoming = prefix_states(dev_decay, dev_state, ctx_axes, ctx_count)

    def advance(state_carry, block_in):
        scaled_k, b_k, c_k, cum_k, decay_k, state_k = block_in
        block_y = intra_block(scaled_k, b_k, c_k, cum_k) + inter_block(c_k, cum_k, state_carry)
        return (decay_k[..., None, None] * state_carry + state_k, block_y)

    _, ssm_y = lax.scan(
        advance, incoming, (scaled_b, b_rows, c_rows, cum_log, blk_decay, blk_states)
    )
    mixed_y = ssm_y.reshape(tok_rows, groups_here, per_group, head_dim)
    mixed_y = mixed_y + skip_gain.reshape(groups_here, per_group)[..., None] * x_heads
    gated_y = mixed_y.reshape(tok_rows, width_x) * jax.nn.silu(gate_in.astype(jnp.float32))
    grouped = gated_y.reshape(tok_rows, groups_here, width_x // groups_here)
    inv_root = lax.rsqrt(jnp.mean(grouped * grouped, axis=-1, keepdims=True) + 1e-05)
    hidden = ((grouped * inv_root).reshape(tok_rows, width_x) * norm_gain).astype(jnp.bfloat16)
    if outer_axis is None:
        partial_out = jnp.dot(
            hidden,
            lax.all_gather(out_weight, ctx_axes, axis=1, tiled=True),
            preferred_element_type=jnp.float32,
        )
        return lax.psum_scatter(partial_out, "tp", scatter_dimension=1, tiled=True).astype(
            jnp.bfloat16
        )
    outer_at = lax.axis_index(outer_axis)
    tp_at = lax.axis_index("tp")
    inner_count = ctx_count // tp_count
    weight_pieces = [out_weight] + [
        lax.ppermute(
            out_weight, inner_axis, [(s, (s + d) % inner_count) for s in range(inner_count)]
        )
        for d in range(1, inner_count)
    ]
    weight_pieces, hidden = lax.optimization_barrier((weight_pieces, hidden))
    weight_cat = jnp.concatenate(weight_pieces, axis=1)

    def times_weight(rows):
        return jnp.dot(rows, weight_cat, preferred_element_type=jnp.float32)

    from_left, from_right = {}, {}
    going_right = going_left = hidden
    for step in range(1, tp_count - 1):
        going_right = lax.ppermute(
            going_right, outer_axis, [(s, s + 1) for s in range(step - 1, tp_count - 1)]
        )
        going_left = lax.ppermute(
            going_left, outer_axis, [(s, s - 1) for s in range(1, tp_count - step + 1)]
        )
        from_left[step], from_right[step] = going_right, going_left
    far = lax.ppermute(
        jnp.where(outer_at == tp_count - 2, going_right, going_left),
        outer_axis,
        [(tp_count - 2, tp_count - 1), (1, 0)],
    )
    far_part = times_weight(far)
    by_source = jnp.stack(
        [times_weight(hidden)]
        + [
            jnp.where(
                outer_at >= d,
                times_weight(from_left[d]) if d < tp_count - 1 else far_part,
                times_weight(from_right[tp_count - d]) if d > 1 else far_part,
            )
            if d != tp_count // 2
            else times_weight(jnp.where(outer_at >= d, from_left[d], from_right[d]))
            for d in range(1, tp_count)
        ]
    )

    def for_target(target):
        return lax.dynamic_index_in_dim(
            by_source, (outer_at - target + tp_count) % tp_count, 0, keepdims=False
        )

    held = {m: for_target(tp_at ^ m) for m in range(tp_count)}
    bit = 1
    while bit < tp_count:
        going = sorted(m for m in held if m & bit)
        sent = jnp.stack([held[m] for m in going])
        got = lax.ppermute(
            sent.astype(jnp.bfloat16),
            "tp",
            [(s, s ^ bit) for s in range(tp_count)],
        )
        held = {m: held[m] for m in held if not m & bit}
        for index, m in enumerate(going):
            held[m ^ bit] = held[m ^ bit] + got[index].astype(jnp.float32)
        bit *= 2
    swap = [(o * tp_count + t, t * tp_count + o) for o in range(tp_count) for t in range(tp_count)]
    rotated = lax.ppermute(held[0].astype(jnp.bfloat16), (outer_axis, "tp"), swap)
    width = out_weight.shape[1]
    pieces = jnp.stack([rotated[:, d * width : (d + 1) * width] for d in range(inner_count)])
    inner_at = lax.axis_index(inner_axis)
    return jnp.concatenate(
        [
            lax.dynamic_index_in_dim(
                pieces, (inner_at - place + inner_count) % inner_count, 0, keepdims=False
            )
            for place in range(inner_count)
        ],
        axis=1,
    )


def solution(mesh):
    ctx_count = mesh.shape["ctx"]
    tp_count = mesh.shape["tp"]
    if ctx_count % tp_count == 0 and tp_count == 4:
        inner = ctx_count // tp_count
        grid = mesh.devices.reshape(tp_count, inner, tp_count)
        mesh = jax.sharding.Mesh(grid, ("outer", "inner", "tp"))
        ctx_axes = ("outer", "inner")
        layout = (ctx_axes, ctx_count, "outer", "inner", tp_count)
    else:
        ctx_axes = "ctx"
        layout = (ctx_axes, ctx_count, None, None, tp_count)
    placed = (
        P(ctx_axes, "tp"),
        P(ctx_axes, "tp"),
        P(ctx_axes, "tp"),
        P(ctx_axes, "tp"),
        P(None, "tp"),
        P(None, "tp"),
        P(None, "tp"),
        P(ctx_axes, "tp"),
        P(ctx_axes, "tp"),
        P("tp"),
        P("tp"),
        P("tp", ctx_axes),
    )
    return jax.shard_map(
        functools.partial(on_device, layout),
        mesh=mesh,
        in_specs=placed,
        out_specs=P(ctx_axes, "tp"),
        check_vma=False,
    )
```

```python
import functools

import jax
import jax.numpy as jnp
from jax import lax
from jax.sharding import PartitionSpec as P

N = 128
BLOCK = 256


def shifted(value, axis, steps, count):
    first, last = (max(0, -steps), min(count, count - steps))
    return lax.ppermute(value, axis, [(source, source + steps) for source in range(first, last)])


def local_conv(packed, kernel, tok_rows):
    tail_len = kernel.shape[0] - 1
    padded = jnp.pad(packed.astype(jnp.float32), ((tail_len, 0), (0, 0)))
    pre_act = jnp.zeros((tok_rows, kernel.shape[1]), jnp.float32)
    for tap_index in range(kernel.shape[0]):
        pre_act = pre_act + kernel[tap_index] * padded[tap_index : tap_index + tok_rows]
    return pre_act


def edge_partial(tail_rows, kernel):
    tail_len = kernel.shape[0] - 1
    tail_vals = tail_rows.astype(jnp.float32)
    outputs = []
    for row_index in range(tail_len):
        accum = jnp.zeros((kernel.shape[1],), jnp.float32)
        for tap_index in range(tail_len - row_index):
            accum = accum + kernel[tap_index] * tail_vals[row_index + tap_index]
        outputs.append(accum)
    return jnp.stack(outputs, axis=0)


def intra_block(scaled, b_rows, c_rows, cum_log):
    scores = jnp.einsum("tgn,sgn->gts", c_rows, b_rows, preferred_element_type=jnp.float32)
    cum_cols = jnp.moveaxis(cum_log, 0, -1)
    log_gap = cum_cols[..., :, None] - cum_cols[..., None, :]
    block_len = cum_log.shape[0]
    causal = jnp.arange(block_len)[:, None] >= jnp.arange(block_len)[None, :]
    decays = jnp.exp(jnp.where(causal, log_gap, -jnp.inf))
    weights = (scores[:, None] * decays).astype(jnp.bfloat16)
    return jnp.einsum("gjts,sgjp->tgjp", weights, scaled, preferred_element_type=jnp.float32)


def block_state(scaled, b_rows, cum_log):
    end_decay = jnp.exp(cum_log[-1][None] - cum_log)
    b_weighted = (b_rows.astype(jnp.float32)[:, :, None, :] * end_decay[..., None]).astype(
        jnp.bfloat16
    )
    return jnp.einsum("sgjp,sgjn->gjpn", scaled, b_weighted, preferred_element_type=jnp.float32)


def inter_block(c_rows, cum_log, state_carry):
    rounded = state_carry.astype(jnp.bfloat16)
    inner = jnp.einsum("tgn,gjpn->tgjp", c_rows, rounded, preferred_element_type=jnp.float32)
    return inner * jnp.exp(cum_log)[..., None]


def combine(first_part, second_part):
    decay_first, state_first = first_part
    decay_second, state_second = second_part
    return (
        decay_first * decay_second,
        decay_second[..., None, None] * state_first.astype(jnp.float32) + state_second,
    )


def on_link(part):
    decay, state = part
    return (decay, state.astype(jnp.bfloat16))


def prefix_states(dev_decay, dev_state, axis, count):
    own = (dev_decay, dev_state)
    if count == 1:
        return jnp.zeros_like(dev_state)
    got = shifted(on_link(own), axis, 1, count)
    before = got
    upto = combine(got, own)
    step = 2
    while step < count:
        got = shifted(on_link(upto), axis, step, count)
        before = combine(got, before)
        if step * 2 < count:
            upto = combine(got, upto)
        step *= 2
    return before[1].astype(jnp.float32)


def on_device(
    layout,
    features,
    input_map,
    output_map,
    gate_in,
    conv_feat,
    conv_input,
    conv_output,
    step_size,
    log_decay,
    skip_gain,
    norm_gain,
    out_weight,
):
    tok_rows, width_x = features.shape
    width_b = input_map.shape[1]
    head_count = step_size.shape[1]
    head_dim = width_x // head_count
    groups_here = width_b // N
    per_group = head_count // groups_here
    tail_len = conv_feat.shape[0] - 1
    n_blocks = tok_rows // BLOCK
    packed = jnp.concatenate([features, input_map, output_map], axis=1)
    kernel = jnp.concatenate([conv_feat, conv_input, conv_output], axis=1)
    pre_act = local_conv(packed, kernel, tok_rows)
    ctx_axes, ctx_count, outer_axis, inner_axis, tp_count = layout
    tail_rows = shifted(packed[tok_rows - tail_len :], ctx_axes, 1, ctx_count)
    edge_sums = edge_partial(tail_rows, kernel)
    pre_act = pre_act + jnp.pad(edge_sums, ((0, tok_rows - tail_len), (0, 0)))
    conv_out = jax.nn.silu(pre_act).astype(jnp.bfloat16)
    x_conv = conv_out[:, :width_x]
    b_conv = conv_out[:, width_x : width_x + width_b]
    c_conv = conv_out[:, width_x + width_b :]
    x_heads = x_conv.astype(jnp.float32).reshape(tok_rows, groups_here, per_group, head_dim)
    scaled = (x_heads * step_size.reshape(tok_rows, groups_here, per_group)[..., None]).astype(
        jnp.bfloat16
    )

    def blocked(value_entries):
        return value_entries.reshape((n_blocks, BLOCK) + value_entries.shape[1:])

    scaled_b = blocked(scaled)
    b_rows = blocked(b_conv.reshape(tok_rows, groups_here, N))
    c_rows = blocked(c_conv.reshape(tok_rows, groups_here, N))
    cum_log = jnp.cumsum(blocked(log_decay.reshape(tok_rows, groups_here, per_group)), axis=1)
    blk_states = jax.vmap(block_state)(scaled_b, b_rows, cum_log)
    blk_decay = jnp.exp(cum_log[:, -1])

    def fold_local(state_carry, block_in):
        decay_b, state_b = block_in
        return (decay_b[..., None, None] * state_carry + state_b, None)

    dev_state, _ = lax.scan(
        fold_local, jnp.zeros(blk_states.shape[1:], jnp.float32), (blk_decay, blk_states)
    )
    dev_decay = jnp.prod(blk_decay, axis=0)
    incoming = prefix_states(dev_decay, dev_state, ctx_axes, ctx_count)

    def advance(state_carry, block_in):
        scaled_k, b_k, c_k, cum_k, decay_k, state_k = block_in
        block_y = intra_block(scaled_k, b_k, c_k, cum_k) + inter_block(c_k, cum_k, state_carry)
        return (decay_k[..., None, None] * state_carry + state_k, block_y)

    _, ssm_y = lax.scan(
        advance, incoming, (scaled_b, b_rows, c_rows, cum_log, blk_decay, blk_states)
    )
    mixed_y = ssm_y.reshape(tok_rows, groups_here, per_group, head_dim)
    mixed_y = mixed_y + skip_gain.reshape(groups_here, per_group)[..., None] * x_heads
    gated_y = mixed_y.reshape(tok_rows, width_x) * jax.nn.silu(gate_in.astype(jnp.float32))
    grouped = gated_y.reshape(tok_rows, groups_here, width_x // groups_here)
    inv_root = lax.rsqrt(jnp.mean(grouped * grouped, axis=-1, keepdims=True) + 1e-05)
    hidden = ((grouped * inv_root).reshape(tok_rows, width_x) * norm_gain).astype(jnp.bfloat16)
    if outer_axis is None:
        partial_out = jnp.dot(
            hidden,
            lax.all_gather(out_weight, ctx_axes, axis=1, tiled=True),
            preferred_element_type=jnp.float32,
        )
        return lax.psum_scatter(partial_out, "tp", scatter_dimension=1, tiled=True).astype(
            jnp.bfloat16
        )
    outer_at = lax.axis_index(outer_axis)
    tp_at = lax.axis_index("tp")
    inner_count = ctx_count // tp_count
    weight_pieces = [out_weight] + [
        lax.ppermute(
            out_weight, inner_axis, [(s, (s + d) % inner_count) for s in range(inner_count)]
        )
        for d in range(1, inner_count)
    ]
    weight_pieces, hidden = lax.optimization_barrier((weight_pieces, hidden))
    def times_weight(rows):
        return jnp.concatenate(
            [jnp.dot(rows, piece, preferred_element_type=jnp.float32) for piece in weight_pieces],
            axis=1,
        )

    from_left, from_right = {}, {}
    going_right = going_left = hidden
    for step in range(1, tp_count - 1):
        going_right = lax.ppermute(
            going_right, outer_axis, [(s, s + 1) for s in range(step - 1, tp_count - 1)]
        )
        going_left = lax.ppermute(
            going_left, outer_axis, [(s, s - 1) for s in range(1, tp_count - step + 1)]
        )
        from_left[step], from_right[step] = going_right, going_left
    far = lax.ppermute(
        jnp.where(outer_at == tp_count - 2, going_right, going_left),
        outer_axis,
        [(tp_count - 2, tp_count - 1), (1, 0)],
    )
    far_part = times_weight(far)
    by_source = jnp.stack(
        [times_weight(hidden)]
        + [
            jnp.where(
                outer_at >= d,
                times_weight(from_left[d]) if d < tp_count - 1 else far_part,
                times_weight(from_right[tp_count - d]) if d > 1 else far_part,
            )
            if d != tp_count // 2
            else times_weight(jnp.where(outer_at >= d, from_left[d], from_right[d]))
            for d in range(1, tp_count)
        ]
    )

    def for_target(target):
        return lax.dynamic_index_in_dim(
            by_source, (outer_at - target + tp_count) % tp_count, 0, keepdims=False
        )

    held = {m: for_target(tp_at ^ m) for m in range(tp_count)}
    bit = 1
    while bit < tp_count:
        going = sorted(m for m in held if m & bit)
        sent = jnp.stack([held[m] for m in going])
        got = lax.ppermute(
            sent.astype(jnp.bfloat16),
            "tp",
            [(s, s ^ bit) for s in range(tp_count)],
        )
        held = {m: held[m] for m in held if not m & bit}
        for index, m in enumerate(going):
            held[m ^ bit] = held[m ^ bit] + got[index].astype(jnp.float32)
        bit *= 2
    swap = [(o * tp_count + t, t * tp_count + o) for o in range(tp_count) for t in range(tp_count)]
    final = held[0].astype(jnp.bfloat16)
    width = out_weight.shape[1]
    pieces = jnp.stack([final[:, d * width : (d + 1) * width] for d in range(inner_count)])
    inner_at = lax.axis_index(inner_axis)
    ordered = jnp.concatenate(
        [
            lax.dynamic_index_in_dim(
                pieces, (inner_at - place + inner_count) % inner_count, 0, keepdims=False
            )
            for place in range(inner_count)
        ],
        axis=1,
    )
    return lax.ppermute(ordered, (outer_axis, "tp"), swap)


def solution(mesh):
    ctx_count = mesh.shape["ctx"]
    tp_count = mesh.shape["tp"]
    if ctx_count % tp_count == 0 and tp_count == 4:
        inner = ctx_count // tp_count
        grid = mesh.devices.reshape(tp_count, inner, tp_count)
        mesh = jax.sharding.Mesh(grid, ("outer", "inner", "tp"))
        ctx_axes = ("outer", "inner")
        layout = (ctx_axes, ctx_count, "outer", "inner", tp_count)
    else:
        ctx_axes = "ctx"
        layout = (ctx_axes, ctx_count, None, None, tp_count)
    placed = (
        P(ctx_axes, "tp"),
        P(ctx_axes, "tp"),
        P(ctx_axes, "tp"),
        P(ctx_axes, "tp"),
        P(None, "tp"),
        P(None, "tp"),
        P(None, "tp"),
        P(ctx_axes, "tp"),
        P(ctx_axes, "tp"),
        P("tp"),
        P("tp"),
        P("tp", ctx_axes),
    )
    return jax.shard_map(
        functools.partial(on_device, layout),
        mesh=mesh,
        in_specs=placed,
        out_specs=P(ctx_axes, "tp"),
        check_vma=False,
    )
```

```python
import functools

import jax
import jax.numpy as jnp
from jax import lax
from jax.sharding import PartitionSpec as P

N = 128
BLOCK = 256


def shifted(value, axis, steps, count):
    first, last = (max(0, -steps), min(count, count - steps))
    return lax.ppermute(value, axis, [(source, source + steps) for source in range(first, last)])


def local_conv(packed, kernel, tok_rows):
    tail_len = kernel.shape[0] - 1
    padded = jnp.pad(packed.astype(jnp.float32), ((tail_len, 0), (0, 0)))
    pre_act = jnp.zeros((tok_rows, kernel.shape[1]), jnp.float32)
    for tap_index in range(kernel.shape[0]):
        pre_act = pre_act + kernel[tap_index] * padded[tap_index : tap_index + tok_rows]
    return pre_act


def edge_partial(tail_rows, kernel):
    tail_len = kernel.shape[0] - 1
    tail_vals = tail_rows.astype(jnp.float32)
    outputs = []
    for row_index in range(tail_len):
        accum = jnp.zeros((kernel.shape[1],), jnp.float32)
        for tap_index in range(tail_len - row_index):
            accum = accum + kernel[tap_index] * tail_vals[row_index + tap_index]
        outputs.append(accum)
    return jnp.stack(outputs, axis=0)


def intra_block(scaled, b_rows, c_rows, cum_log):
    scores = jnp.einsum("tgn,sgn->gts", c_rows, b_rows, preferred_element_type=jnp.float32)
    cum_cols = jnp.moveaxis(cum_log, 0, -1)
    log_gap = cum_cols[..., :, None] - cum_cols[..., None, :]
    block_len = cum_log.shape[0]
    causal = jnp.arange(block_len)[:, None] >= jnp.arange(block_len)[None, :]
    decays = jnp.exp(jnp.where(causal, log_gap, -jnp.inf))
    weights = (scores[:, None] * decays).astype(jnp.bfloat16)
    return jnp.einsum("gjts,sgjp->tgjp", weights, scaled, preferred_element_type=jnp.float32)


def block_state(scaled, b_rows, cum_log):
    end_decay = jnp.exp(cum_log[-1][None] - cum_log)
    b_weighted = (b_rows.astype(jnp.float32)[:, :, None, :] * end_decay[..., None]).astype(
        jnp.bfloat16
    )
    return jnp.einsum("sgjp,sgjn->gjpn", scaled, b_weighted, preferred_element_type=jnp.float32)


def inter_block(c_rows, cum_log, state_carry):
    rounded = state_carry.astype(jnp.bfloat16)
    inner = jnp.einsum("tgn,gjpn->tgjp", c_rows, rounded, preferred_element_type=jnp.float32)
    return inner * jnp.exp(cum_log)[..., None]


def combine(first_part, second_part):
    decay_first, state_first = first_part
    decay_second, state_second = second_part
    return (
        decay_first * decay_second,
        decay_second[..., None, None] * state_first.astype(jnp.float32) + state_second,
    )


def on_link(part):
    decay, state = part
    return (decay, state.astype(jnp.bfloat16))


def prefix_states(dev_decay, dev_state, axis, count):
    own = (dev_decay, dev_state)
    if count == 1:
        return jnp.zeros_like(dev_state)
    got = shifted(on_link(own), axis, 1, count)
    before = got
    upto = combine(got, own)
    step = 2
    while step < count:
        got = shifted(on_link(upto), axis, step, count)
        before = combine(got, before)
        if step * 2 < count:
            upto = combine(got, upto)
        step *= 2
    return before[1].astype(jnp.float32)


def on_device(
    layout,
    features,
    input_map,
    output_map,
    gate_in,
    conv_feat,
    conv_input,
    conv_output,
    step_size,
    log_decay,
    skip_gain,
    norm_gain,
    out_weight,
):
    tok_rows, width_x = features.shape
    width_b = input_map.shape[1]
    head_count = step_size.shape[1]
    head_dim = width_x // head_count
    groups_here = width_b // N
    per_group = head_count // groups_here
    tail_len = conv_feat.shape[0] - 1
    n_blocks = tok_rows // BLOCK
    packed = jnp.concatenate([features, input_map, output_map], axis=1)
    kernel = jnp.concatenate([conv_feat, conv_input, conv_output], axis=1)
    pre_act = local_conv(packed, kernel, tok_rows)
    ctx_axes, ctx_count, outer_axis, inner_axis, tp_count = layout
    tail_rows = shifted(packed[tok_rows - tail_len :], ctx_axes, 1, ctx_count)
    edge_sums = edge_partial(tail_rows, kernel)
    pre_act = pre_act + jnp.pad(edge_sums, ((0, tok_rows - tail_len), (0, 0)))
    conv_out = jax.nn.silu(pre_act).astype(jnp.bfloat16)
    x_conv = conv_out[:, :width_x]
    b_conv = conv_out[:, width_x : width_x + width_b]
    c_conv = conv_out[:, width_x + width_b :]
    x_heads = x_conv.astype(jnp.float32).reshape(tok_rows, groups_here, per_group, head_dim)
    scaled = (x_heads * step_size.reshape(tok_rows, groups_here, per_group)[..., None]).astype(
        jnp.bfloat16
    )

    def blocked(value_entries):
        return value_entries.reshape((n_blocks, BLOCK) + value_entries.shape[1:])

    scaled_b = blocked(scaled)
    b_rows = blocked(b_conv.reshape(tok_rows, groups_here, N))
    c_rows = blocked(c_conv.reshape(tok_rows, groups_here, N))
    cum_log = jnp.cumsum(blocked(log_decay.reshape(tok_rows, groups_here, per_group)), axis=1)
    blk_states = jax.vmap(block_state)(scaled_b, b_rows, cum_log)
    blk_decay = jnp.exp(cum_log[:, -1])

    def fold_local(state_carry, block_in):
        decay_b, state_b = block_in
        return (decay_b[..., None, None] * state_carry + state_b, None)

    dev_state, _ = lax.scan(
        fold_local, jnp.zeros(blk_states.shape[1:], jnp.float32), (blk_decay, blk_states)
    )
    dev_decay = jnp.prod(blk_decay, axis=0)
    incoming = prefix_states(dev_decay, dev_state, ctx_axes, ctx_count)

    def advance(state_carry, block_in):
        scaled_k, b_k, c_k, cum_k, decay_k, state_k = block_in
        block_y = intra_block(scaled_k, b_k, c_k, cum_k) + inter_block(c_k, cum_k, state_carry)
        return (decay_k[..., None, None] * state_carry + state_k, block_y)

    _, ssm_y = lax.scan(
        advance, incoming, (scaled_b, b_rows, c_rows, cum_log, blk_decay, blk_states)
    )
    mixed_y = ssm_y.reshape(tok_rows, groups_here, per_group, head_dim)
    mixed_y = mixed_y + skip_gain.reshape(groups_here, per_group)[..., None] * x_heads
    gated_y = mixed_y.reshape(tok_rows, width_x) * jax.nn.silu(gate_in.astype(jnp.float32))
    grouped = gated_y.reshape(tok_rows, groups_here, width_x // groups_here)
    inv_root = lax.rsqrt(jnp.mean(grouped * grouped, axis=-1, keepdims=True) + 1e-05)
    hidden = ((grouped * inv_root).reshape(tok_rows, width_x) * norm_gain).astype(jnp.bfloat16)
    if outer_axis is None:
        partial_out = jnp.dot(
            hidden,
            lax.all_gather(out_weight, ctx_axes, axis=1, tiled=True),
            preferred_element_type=jnp.float32,
        )
        return lax.psum_scatter(partial_out, "tp", scatter_dimension=1, tiled=True).astype(
            jnp.bfloat16
        )
    outer_at = lax.axis_index(outer_axis)
    tp_at = lax.axis_index("tp")
    inner_count = ctx_count // tp_count
    weight_pieces = [out_weight] + [
        lax.ppermute(
            out_weight, inner_axis, [(s, (s + d) % inner_count) for s in range(inner_count)]
        )
        for d in range(1, inner_count)
    ]
    weight_pieces, hidden = lax.optimization_barrier((weight_pieces, hidden))
    def times_weight(rows):
        return jnp.concatenate(
            [jnp.dot(rows, piece, preferred_element_type=jnp.float32) for piece in weight_pieces],
            axis=1,
        )

    from_left, from_right = {}, {}
    going_right = going_left = hidden
    for step in range(1, tp_count - 1):
        going_right = lax.ppermute(
            going_right, outer_axis, [(s, s + 1) for s in range(step - 1, tp_count - 1)]
        )
        going_left = lax.ppermute(
            going_left, outer_axis, [(s, s - 1) for s in range(1, tp_count - step + 1)]
        )
        from_left[step], from_right[step] = going_right, going_left
    far = lax.ppermute(
        jnp.where(outer_at == tp_count - 2, going_right, going_left),
        outer_axis,
        [(tp_count - 2, tp_count - 1), (1, 0)],
    )
    far_part = times_weight(far)
    by_source = jnp.stack(
        [times_weight(hidden)]
        + [
            jnp.where(
                outer_at >= d,
                times_weight(from_left[d]) if d < tp_count - 1 else far_part,
                times_weight(from_right[tp_count - d]) if d > 1 else far_part,
            )
            if d != tp_count // 2
            else times_weight(jnp.where(outer_at >= d, from_left[d], from_right[d]))
            for d in range(1, tp_count)
        ]
    )

    def for_target(target):
        return lax.dynamic_index_in_dim(
            by_source, (outer_at - target + tp_count) % tp_count, 0, keepdims=False
        )

    by_source_low = by_source.astype(jnp.bfloat16)
    held = {m: for_target(tp_at ^ m) for m in range(tp_count)}
    bit = 1
    while bit < tp_count:
        going = sorted(m for m in held if m & bit)
        if bit == 1:
            sent = jnp.stack(
                [
                    lax.dynamic_index_in_dim(
                        by_source_low,
                        (outer_at - (tp_at ^ m) + tp_count) % tp_count,
                        0,
                        keepdims=False,
                    )
                    for m in going
                ]
            )
        else:
            sent = jnp.stack([held[m] for m in going])
        got = lax.ppermute(
            sent.astype(jnp.bfloat16),
            "tp",
            [(s, s ^ bit) for s in range(tp_count)],
        )
        held = {m: held[m] for m in held if not m & bit}
        for index, m in enumerate(going):
            held[m ^ bit] = held[m ^ bit] + got[index].astype(jnp.float32)
        bit *= 2
    swap = [(o * tp_count + t, t * tp_count + o) for o in range(tp_count) for t in range(tp_count)]
    rotated = lax.ppermute(held[0].astype(jnp.bfloat16), (outer_axis, "tp"), swap)
    width = out_weight.shape[1]
    pieces = jnp.stack([rotated[:, d * width : (d + 1) * width] for d in range(inner_count)])
    inner_at = lax.axis_index(inner_axis)
    return jnp.concatenate(
        [
            lax.dynamic_index_in_dim(
                pieces, (inner_at - place + inner_count) % inner_count, 0, keepdims=False
            )
            for place in range(inner_count)
        ],
        axis=1,
    )


def solution(mesh):
    ctx_count = mesh.shape["ctx"]
    tp_count = mesh.shape["tp"]
    if ctx_count % tp_count == 0 and tp_count == 4:
        inner = ctx_count // tp_count
        grid = mesh.devices.reshape(tp_count, inner, tp_count)
        mesh = jax.sharding.Mesh(grid, ("outer", "inner", "tp"))
        ctx_axes = ("outer", "inner")
        layout = (ctx_axes, ctx_count, "outer", "inner", tp_count)
    else:
        ctx_axes = "ctx"
        layout = (ctx_axes, ctx_count, None, None, tp_count)
    placed = (
        P(ctx_axes, "tp"),
        P(ctx_axes, "tp"),
        P(ctx_axes, "tp"),
        P(ctx_axes, "tp"),
        P(None, "tp"),
        P(None, "tp"),
        P(None, "tp"),
        P(ctx_axes, "tp"),
        P(ctx_axes, "tp"),
        P("tp"),
        P("tp"),
        P("tp", ctx_axes),
    )
    return jax.shard_map(
        functools.partial(on_device, layout),
        mesh=mesh,
        in_specs=placed,
        out_specs=P(ctx_axes, "tp"),
        check_vma=False,
    )
```
